32 devices in a mesh: cap: 4 (over z), lat: 4 (over x, core), rad: 2 (over y).
Axes of the slice: x: 2, y: 2, z: 4, core: 2. Of those that a mesh axis runs over, the one named last changes fastest.
Arguments:
- adjoint_temp: float32 [64, 128, 1024], P('rad', 'cap', 'lat'), may hold values from -6 to 6
- velocity: bfloat16 [2, 64, 128, 1024], P(None, 'rad', 'cap', 'lat'), may hold values from -6 to 6
- visc_flow: bfloat16 [64, 128, 1024], P('rad', 'cap', 'lat'), may hold values from 0.099609375 to 1
- visc_yield: bfloat16 [64, 128, 1024], P('rad', 'cap', 'lat'), may hold values from 0.049804688 to 1
- yield_mask: int32 [64, 128, 1024], P('rad', 'cap', 'lat'), may hold values 0 or 1
- radial_inverse: float32 [64, 64], replicated
- marker_rows: bfloat16 [64, 32768], P('rad', ('cap', 'lat')), may hold values from -6 to 6
- recv_cells: int32 [32768], P(('cap', 'lat')), may hold values from 0 to 8191
- recv_counts: int32 [64], P(('cap', 'lat')), may hold values from 64 to 512, as said below
Outputs:
- adjoint_prev: float32 [64, 128, 1024], P(None, ('cap', 'rad'), 'lat')
The draws below stay inside these ranges and needn't reach their ends.
Inputs may be any that keep to these rules, and one draw needn't show every extreme that they name: `recv_counts`: some bucket holds exactly 512 live slots and some exactly 64 in every draw.
All inputs are finite; a program needn't handle non-finite values. No bound on the sum of `yield_mask` on one device may be relied on, other than what follows from the above.
Results may differ from the reference program's by a relative error of at most 0.0003.
Values may be sent and summed in bfloat16 or wider, within the bound.
No kernel may reach another device: no remote copies, remote signals or barrier semaphores. Data moves between devices by JAX's collectives and lax.ppermute only.
A program may use at most 64 MiB of HBM per device.

```python
import math
import jax
import jax.numpy as jnp
from jax import lax

A_DEV = 32
B_DEV = 256
SLOTS = 512
PICARD = 3
NR = 64
NA = 128
NB = 1024
MSLOTS = 32768
N_CAP = 4
N_LAT = 4


def draw_radial_inverse(key, part):
    first = jax.random.fold_in(key, 11)
    second = jax.random.fold_in(key, 12)
    rows = jnp.arange(NR, dtype=jnp.int32)[:, None]
    cols = jnp.arange(NR, dtype=jnp.int32)[None, :]
    eye = (rows == cols).astype(jnp.float32)
    diag = jax.random.uniform(first, (NR, 1), jnp.float32, 1.0, 2.0)
    off = jax.random.normal(second, (NR, NR), jnp.float32)
    scale = 0.5 / NR ** 0.5
    return eye * diag + (1.0 - eye) * off * scale


def draw_recv_cells(key, part):
    cells = jax.random.randint(jax.random.fold_in(key, 21), (MSLOTS,), 0, A_DEV * B_DEV, jnp.int32)
    return cells.at[0].set(A_DEV * B_DEV - 1).at[1].set(0)


def draw_recv_counts(key, part):
    heavy = jax.random.randint(jax.random.fold_in(key, 31), (N_CAP, 1), 0, 4, jnp.int32) == 0
    base = jax.random.randint(jax.random.fold_in(key, 32), (N_CAP, N_LAT * N_LAT), SLOTS // 8, SLOTS // 2 + 1, jnp.int32)
    counts = jnp.where(heavy, SLOTS, base).reshape(-1)
    return counts.at[0].set(SLOTS).at[1].set(SLOTS // 8)


def touch_ends(drawn, rng, smallest, high):
    longest = drawn.shape.index(max(drawn.shape))
    spots = []
    for shift in (0, 1):
        where = [jax.random.randint(jax.random.fold_in(rng, axis), (), 0, length) for axis, length in enumerate(drawn.shape)]
        where[longest] = (where[longest] + shift) % drawn.shape[longest]
        spots.append(tuple(where))
    return drawn.at[spots[0]].set(smallest).at[spots[1]].set(high)


def level_of(stream_key, shape, pieces, smallest, largest):
    def one(dim, parts):
        heights = jax.random.uniform(jax.random.fold_in(jax.random.fold_in(stream_key, 6), dim), (parts,), jnp.float32, smallest / len(pieces), largest / len(pieces))
        return jnp.repeat(jnp.exp(heights), shape[dim] // parts).reshape((-1,) + (1,) * (len(shape) - dim - 1))

    level = one(*pieces[0])
    for cut in pieces[1:]:
        level = level * one(*cut)
    return level


def bell_draw(stream_key, dims, deviation, bound, shards=(), kind=jnp.bfloat16):
    entries = deviation * jax.random.normal(stream_key, dims, jnp.float32)
    if shards:
        entries = entries * level_of(stream_key, dims, shards, -0.22, 0.18)
    return jnp.clip(entries, -bound, bound).astype(kind)


def setup_inputs(seed: int = 0) -> dict:
    streams_of = jax.random.split(jax.random.key(seed), 10)
    return {
        "adjoint_temp": bell_draw(streams_of[0], (NR, NA, NB), 1.0, 6.0, ((0, 2), (1, 4), (2, 4)), jnp.float32),
        "velocity": bell_draw(streams_of[1], (2, NR, NA, NB), 1.0, 6.0, ((1, 2), (2, 4), (3, 4))),
        "visc_flow": jnp.clip(jnp.exp(math.log(1.0) - 2.306499 * jax.random.uniform(streams_of[2], (NR, NA, NB), jnp.float32) ** level_of(streams_of[2], (NR, NA, NB), ((0, 2), (1, 4), (2, 4)), -0.2, 0.2)), 0.099609375, 1.0).astype(jnp.bfloat16),
        "visc_yield": jnp.clip(jnp.exp(math.log(1.0) - 2.9996462 * jax.random.uniform(streams_of[3], (NR, NA, NB), jnp.float32) ** level_of(streams_of[3], (NR, NA, NB), ((0, 2), (1, 4), (2, 4)), -0.2, 0.2)), 0.049804688, 1.0).astype(jnp.bfloat16),
        "yield_mask": touch_ends((jax.random.randint(streams_of[4], (NR, NA, NB), 0, 2) < 1).astype(jnp.int32), jax.random.fold_in(streams_of[4], 1), 0, 1),
        "radial_inverse": draw_radial_inverse(jax.random.fold_in(streams_of[9], 71), 0),
        "marker_rows": bell_draw(streams_of[6], (NR, MSLOTS), 1.0, 6.0, ((0, 2), (1, 16))),
        "recv_cells": draw_recv_cells(jax.random.fold_in(streams_of[9], 71), 0),
        "recv_counts": draw_recv_counts(jax.random.fold_in(streams_of[9], 71), 0),
    }


relax_coef = 0.25
advect_coef = 0.1


def lateral_pad(field):
    return jnp.pad(field, ((0, 0), (1, 1), (1, 1)))


def viscous(w_pad, eta_pad, w_mid, eta_mid):
    total = jnp.zeros_like(w_mid)
    for neigh_w, neigh_e in ((w_pad[:, 2:, 1:-1], eta_pad[:, 2:, 1:-1]), (w_pad[:, :-2, 1:-1], eta_pad[:, :-2, 1:-1]), (w_pad[:, 1:-1, 2:], eta_pad[:, 1:-1, 2:]), (w_pad[:, 1:-1, :-2], eta_pad[:, 1:-1, :-2])):
        total = total + 0.5 * (eta_mid + neigh_e) * (neigh_w - w_mid)
    return total


def reference(adjoint_temp, velocity, visc_flow, visc_yield, yield_mask, radial_inverse, marker_rows, recv_cells, recv_counts):
    flow = visc_flow.astype(jnp.float32)
    plast = visc_yield.astype(jnp.float32)
    eta = jnp.where(yield_mask == 1, flow * plast / (flow + plast), flow)
    eta_pad = lateral_pad(eta)
    lam = adjoint_temp
    lam_pad = lateral_pad(lam)
    iterate = lam
    for sweep in range(PICARD):
        iterate = lam + relax_coef * viscous(lateral_pad(iterate), eta_pad, iterate, eta)
    advect = velocity[0] * (lam_pad[:, 2:, 1:-1] - lam_pad[:, :-2, 1:-1]) + velocity[1] * (lam_pad[:, 1:-1, 2:] - lam_pad[:, 1:-1, :-2])
    rows = marker_rows.reshape(NR, N_CAP, N_LAT, N_LAT, SLOTS).transpose(0, 1, 3, 2, 4)
    cells = recv_cells.reshape(N_CAP, N_LAT, N_LAT, SLOTS)
    counts = recv_counts.reshape(N_CAP, N_LAT, N_LAT)
    live = jnp.arange(SLOTS, dtype=jnp.int32)[None, None, None, :] < counts[..., None]
    cap_idx = jnp.arange(N_CAP, dtype=jnp.int32)[:, None, None, None]
    own_idx = jnp.arange(N_LAT, dtype=jnp.int32)[None, :, None, None]
    first = cap_idx * A_DEV + cells // B_DEV
    second = own_idx * B_DEV + cells % B_DEV
    flat = (first * NB + second).astype(jnp.int32).reshape(-1)
    values = (rows.astype(jnp.float32) * live[None].astype(jnp.float32)).reshape(NR, -1)
    deposit = jnp.zeros((NR, NA * NB), jnp.float32).at[:, flat].add(values).reshape(NR, NA, NB)
    rhs = iterate + advect_coef * advect + deposit
    out = jnp.dot(radial_inverse, rhs.reshape(NR, -1), precision=lax.Precision.HIGHEST)
    return out.reshape(NR, NA, NB)
```

```python
import functools

import jax
import jax.numpy as jnp
from jax import lax
from jax.experimental import pallas as pl
from jax.experimental.pallas import tpu as pltpu
from jax.sharding import PartitionSpec as P

PICARD = 3
GHOST = 3

relax_coef = 0.25
advect_coef = 0.1


def _shift_pairs(n_rows, n_cols, dr, dc):
    pairs = []
    for r in range(n_rows):
        for c in range(n_cols):
            rr, cc = r + dr, c + dc
            if 0 <= rr < n_rows and 0 <= cc < n_cols:
                pairs.append((r * n_cols + c, rr * n_cols + cc))
    return pairs


def _halo(x, n_cap, n_lat):
    g = GHOST
    rows, cols = x.shape[2], x.shape[3]
    top_src = x[:, :, rows - g:, :]
    bot_src = x[:, :, :g, :]
    left_src = x[:, :, :, cols - g:]
    right_src = x[:, :, :, :g]
    both = ("cap", "lat")
    top = lax.ppermute(top_src, "cap", _shift_pairs(n_cap, 1, 1, 0))
    bot = lax.ppermute(bot_src, "cap", _shift_pairs(n_cap, 1, -1, 0))
    left = lax.ppermute(left_src, "lat", _shift_pairs(1, n_lat, 0, 1))
    right = lax.ppermute(right_src, "lat", _shift_pairs(1, n_lat, 0, -1))
    tl = lax.ppermute(x[:, :, rows - g:, cols - g:], both, _shift_pairs(n_cap, n_lat, 1, 1))
    tr = lax.ppermute(x[:, :, rows - g:, :g], both, _shift_pairs(n_cap, n_lat, 1, -1))
    bl = lax.ppermute(x[:, :, :g, cols - g:], both, _shift_pairs(n_cap, n_lat, -1, 1))
    br = lax.ppermute(x[:, :, :g, :g], both, _shift_pairs(n_cap, n_lat, -1, -1))
    return top, bot, left, right, tl, tr, bl, br


def _extend(main, top, bot, left, right, tl, tr, bl, br, ext_rows, ext_cols):
    g = GHOST
    layers, rows, cols = main.shape
    zc = ext_cols - cols - 2 * g
    zr = ext_rows - rows - 2 * g

    def row_band(mid, rgt, lft, n):
        z = jnp.zeros((layers, n, zc), main.dtype)
        return jnp.concatenate([mid, rgt, z, lft], axis=2)

    band_main = row_band(main, right, left, rows)
    band_bot = row_band(bot, br, bl, g)
    band_top = row_band(top, tr, tl, g)
    zero_rows = jnp.zeros((layers, zr, ext_cols), main.dtype)
    return jnp.concatenate([band_main, band_bot, zero_rows, band_top], axis=1)


def _inside_mask(rows, cols, ext_rows, ext_cols, c, d, n_cap, n_lat):
    g = GHOST
    i = jnp.arange(ext_rows, dtype=jnp.int32)
    j = jnp.arange(ext_cols, dtype=jnp.int32)
    local_r = jnp.where(i < rows + g, i, jnp.where(i >= ext_rows - g, i - ext_rows, -10**6))
    local_c = jnp.where(j < cols + g, j, jnp.where(j >= ext_cols - g, j - ext_cols, -10**6))
    glob_r = c * rows + local_r
    glob_c = d * cols + local_c
    ok_r = (local_r > -10**5) & (glob_r >= 0) & (glob_r < n_cap * rows)
    ok_c = (local_c > -10**5) & (glob_c >= 0) & (glob_c < n_lat * cols)
    return (ok_r[:, None] & ok_c[None, :]).astype(jnp.float32)


def _sweep_kernel(rad_ref, lam_ref, eta_ref, mask_ref, vel_ref, dep_ref, send_ref, keep_ref):
    lam = lam_ref[...]
    eta = eta_ref[...]
    m = mask_ref[...][None] > 0.5
    n_r, n_c = lam.shape[1], lam.shape[2]
    rows, cols = dep_ref.shape[1], dep_ref.shape[2]

    def up(x):
        return pltpu.roll(x, n_r - 1, 1)

    def dn(x):
        return pltpu.roll(x, 1, 1)

    def rt(x):
        return pltpu.roll(x, n_c - 1, 2)

    def lf(x):
        return pltpu.roll(x, 1, 2)

    ca = 0.5 * (eta + up(eta))
    cd = dn(ca)
    cb = 0.5 * (eta + rt(eta))
    cl = lf(cb)
    w = lam
    for _ in range(PICARD):
        total = ca * (up(w) - w)
        total = total + cd * (dn(w) - w)
        total = total + cb * (rt(w) - w)
        total = total + cl * (lf(w) - w)
        w = jnp.where(m, lam + relax_coef * total, 0.0)
    v0 = vel_ref[0].astype(jnp.float32)
    v1 = vel_ref[1].astype(jnp.float32)
    da = (up(lam) - dn(lam))[:, :rows, :cols]
    db = (rt(lam) - lf(lam))[:, :rows, :cols]
    adv = v0 * da + v1 * db
    rhs = w[:, :rows, :cols] + advect_coef * adv + dep_ref[...]
    half = rows // 2
    lo = rhs[:, :half, :]
    hi = rhs[:, half:, :]
    is_zero = rad_ref[0] == 0
    send_ref[...] = jnp.where(is_zero, hi, lo)
    keep_ref[...] = jnp.where(is_zero, lo, hi)


def _sweeps(rad_idx, lam_ext, eta_ext, mask, vel, dep, block_layers):
    layers, ext_r, ext_c = lam_ext.shape
    rows, cols = dep.shape[1], dep.shape[2]
    half = rows // 2
    grid = (layers // block_layers,)
    out_shape = [jax.ShapeDtypeStruct((layers, half, cols), jnp.float32)] * 2
    return pl.pallas_call(
        _sweep_kernel,
        out_shape=out_shape,
        grid=grid,
        in_specs=[
            pl.BlockSpec(memory_space=pltpu.SMEM),
            pl.BlockSpec((block_layers, ext_r, ext_c), lambda i: (i, 0, 0)),
            pl.BlockSpec((block_layers, ext_r, ext_c), lambda i: (i, 0, 0)),
            pl.BlockSpec((ext_r, ext_c), lambda i: (0, 0)),
            pl.BlockSpec((2, block_layers, rows, cols), lambda i: (0, i, 0, 0)),
            pl.BlockSpec((block_layers, rows, cols), lambda i: (i, 0, 0)),
        ],
        out_specs=[
            pl.BlockSpec((block_layers, half, cols), lambda i: (i, 0, 0)),
            pl.BlockSpec((block_layers, half, cols), lambda i: (i, 0, 0)),
        ],
    )(rad_idx, lam_ext, eta_ext, mask, vel, dep)


def per_device(
    adjoint_temp,
    velocity,
    visc_flow,
    visc_yield,
    yield_mask,
    radial_inverse,
    marker_rows,
    recv_cells,
    recv_counts,
):
    layers, rows, cols = adjoint_temp.shape
    n_cap = lax.axis_size("cap")
    n_lat = lax.axis_size("lat")
    n_rad = lax.axis_size("rad")
    c = lax.axis_index("cap")
    d = lax.axis_index("lat")
    r = lax.axis_index("rad")

    received = lax.all_to_all(marker_rows, "lat", split_axis=1, concat_axis=1, tiled=True)

    flow = visc_flow.astype(jnp.float32)
    plast = visc_yield.astype(jnp.float32)
    eta = jnp.where(yield_mask == 1, flow * plast / (flow + plast), flow)

    stacked = jnp.stack([adjoint_temp, eta])
    pieces = _halo(stacked, n_cap, n_lat)
    ext_rows = ((rows + 2 * GHOST + 7) // 8) * 8
    ext_cols = ((cols + 2 * GHOST + 127) // 128) * 128
    lam_ext = _extend(adjoint_temp, *[p[0] for p in pieces], ext_rows, ext_cols)
    eta_ext = _extend(eta, *[p[1] for p in pieces], ext_rows, ext_cols)
    mask = _inside_mask(rows, cols, ext_rows, ext_cols, c, d, n_cap, n_lat)

    senders = n_lat
    slot_total = received.shape[1]
    per_sender = slot_total // senders
    live = (jnp.arange(per_sender, dtype=jnp.int32)[None, :] < recv_counts[:, None]).reshape(-1)
    cell_a = recv_cells // cols
    cell_b = recv_cells % cols
    hit_a = (cell_a[None, :] == jnp.arange(rows, dtype=jnp.int32)[:, None]) & live[None, :]
    xa = jnp.where(hit_a[None], received[:, None, :], jnp.zeros((), received.dtype))
    onehot_b = (cell_b[:, None] == jnp.arange(cols, dtype=jnp.int32)[None, :]).astype(received.dtype)
    deposit = jnp.einsum("las,sb->lab", xa, onehot_b, preferred_element_type=jnp.float32)

    rad_idx = r.astype(jnp.int32).reshape(1)
    n_chunks = 2
    chunk = layers // n_chunks
    block_layers = 4
    keeps = []
    recvs = []
    for k in range(n_chunks):
        sl = slice(k * chunk, (k + 1) * chunk)
        send, keep = _sweeps(
            rad_idx, lam_ext[sl], eta_ext[sl], mask, velocity[:, sl], deposit[sl], block_layers
        )
        recvs.append(lax.ppermute(send, "rad", _shift_pairs(1, n_rad, 0, 1) + _shift_pairs(1, n_rad, 0, -1)))
        keeps.append(keep)

    full_layers = radial_inverse.shape[0]
    mine = jnp.concatenate(keeps, axis=0)
    theirs = jnp.concatenate(recvs, axis=0)
    columns = jnp.concatenate([mine, theirs], axis=0)
    my_cols = lax.dynamic_slice_in_dim(radial_inverse, r * layers, layers, axis=1)
    peer_cols = lax.dynamic_slice_in_dim(radial_inverse, (1 - r) * layers, layers, axis=1)
    r_perm = jnp.concatenate([my_cols, peer_cols], axis=1)
    result = jnp.dot(
        r_perm, columns.reshape(full_layers, -1), precision=lax.Precision.HIGHEST
    )
    return result.reshape(columns.shape)


def solution(mesh):
    in_specs = (
        P("rad", "cap", "lat"),
        P(None, "rad", "cap", "lat"),
        P("rad", "cap", "lat"),
        P("rad", "cap", "lat"),
        P("rad", "cap", "lat"),
        P(),
        P("rad", ("cap", "lat")),
        P(("cap", "lat")),
        P(("cap", "lat")),
    )
    out_specs = P(None, ("cap", "rad"), "lat")
    return jax.shard_map(
        per_device, mesh=mesh, in_specs=in_specs, out_specs=out_specs, check_vma=False
    )
```

```python
import jax
import jax.numpy as jnp
from jax import lax
from jax.experimental import pallas as pl
from jax.experimental.pallas import tpu as pltpu
from jax.sharding import PartitionSpec as P

PICARD = 3
GHOST = 3

relax_coef = 0.25
advect_coef = 0.1


def _inside_mask(rows, cols, ext_rows, ext_cols, c, d, n_cap, n_lat):
    g = GHOST
    far = -(1 << 20)
    i = jnp.arange(ext_rows, dtype=jnp.int32)
    j = jnp.arange(ext_cols, dtype=jnp.int32)
    local_r = jnp.where(i < rows + g, i, jnp.where(i >= ext_rows - g, i - ext_rows, far))
    local_c = jnp.where(j < cols + g, j, jnp.where(j >= ext_cols - g, j - ext_cols, far))
    glob_r = c * rows + local_r
    glob_c = d * cols + local_c
    ok_r = (local_r > far) & (glob_r >= 0) & (glob_r < n_cap * rows)
    ok_c = (local_c > far) & (glob_c >= 0) & (glob_c < n_lat * cols)
    return (ok_r[:, None] & ok_c[None, :]).astype(jnp.float32)


def _pairs(n, step):
    return [(i, i + step) for i in range(n) if 0 <= i + step < n]


def _sweep_kernel(rad_ref, lam_ref, eta_ref, rowh_ref, colh_ref, mask_ref, vel_ref, dep_ref,
                  send_ref, keep_ref, lam_x, eta_x):
    layers, rows, cols = lam_ref.shape
    n_r, n_c = lam_x.shape[1], lam_x.shape[2]
    for ref, src, k in ((lam_x, lam_ref, 0), (eta_x, eta_ref, 1)):
        ref[:, :rows, :cols] = src[...]
        ref[:, rows:, :cols] = rowh_ref[k]
        ref[:, :, cols:] = colh_ref[k]
    lam = lam_x[...]
    eta = eta_x[...]
    m = mask_ref[...][None]

    def up(x):
        return pltpu.roll(x, n_r - 1, 1)

    def dn(x):
        return pltpu.roll(x, 1, 1)

    def rt(x):
        return pltpu.roll(x, n_c - 1, 2)

    def lf(x):
        return pltpu.roll(x, 1, 2)

    ca_raw = 0.5 * (eta + up(eta))
    cb_raw = 0.5 * (eta + rt(eta))
    mq = relax_coef * m
    ca = ca_raw * mq
    cd = dn(ca_raw) * mq
    cb = cb_raw * mq
    cl = lf(cb_raw) * mq
    w = lam
    for _ in range(PICARD - 1):
        total = ca * (up(w) - w)
        total = total + cd * (dn(w) - w)
        total = total + cb * (rt(w) - w)
        total = total + cl * (lf(w) - w)
        w = lam + total

    def main(x):
        return x[:, :rows, :cols]

    wm = main(w)
    total = main(ca) * (main(up(w)) - wm)
    total = total + main(cd) * (main(dn(w)) - wm)
    total = total + main(cb) * (main(rt(w)) - wm)
    total = total + main(cl) * (main(lf(w)) - wm)
    w3 = main(lam) + total
    v0 = vel_ref[0].astype(jnp.float32)
    v1 = vel_ref[1].astype(jnp.float32)
    adv = v0 * main(up(lam) - dn(lam)) + v1 * main(rt(lam) - lf(lam))
    rhs = w3 + advect_coef * adv + dep_ref[...]
    half = rows // 2
    lo = rhs[:, :half, :]
    hi = rhs[:, half:, :]
    is_zero = rad_ref[0] == 0
    send_ref[...] = jnp.where(is_zero, hi, lo)
    keep_ref[...] = jnp.where(is_zero, lo, hi)


def _sweeps(rad_idx, lam, eta, rowh, colh, mask, vel, dep, first_layer, n_layers, block_layers):
    _, rows, cols = lam.shape
    ext_r, ext_c = mask.shape
    half = rows // 2
    off = first_layer // block_layers
    bl = block_layers
    grid = (n_layers // bl,)
    out_shape = [jax.ShapeDtypeStruct((n_layers, half, cols), jnp.float32)] * 2
    return pl.pallas_call(
        _sweep_kernel,
        out_shape=out_shape,
        grid=grid,
        in_specs=[
            pl.BlockSpec(memory_space=pltpu.SMEM),
            pl.BlockSpec((bl, rows, cols), lambda i: (i + off, 0, 0)),
            pl.BlockSpec((bl, rows, cols), lambda i: (i + off, 0, 0)),
            pl.BlockSpec((2, bl, ext_r - rows, cols), lambda i: (0, i + off, 0, 0)),
            pl.BlockSpec((2, bl, ext_r, ext_c - cols), lambda i: (0, i + off, 0, 0)),
            pl.BlockSpec((ext_r, ext_c), lambda i: (0, 0)),
            pl.BlockSpec((2, bl, rows, cols), lambda i: (0, i + off, 0, 0)),
            pl.BlockSpec((bl, rows, cols), lambda i: (i + off, 0, 0)),
        ],
        out_specs=[
            pl.BlockSpec((bl, half, cols), lambda i: (i, 0, 0)),
            pl.BlockSpec((bl, half, cols), lambda i: (i, 0, 0)),
        ],
        scratch_shapes=[
            pltpu.VMEM((bl, ext_r, ext_c), jnp.float32),
            pltpu.VMEM((bl, ext_r, ext_c), jnp.float32),
        ],
    )(rad_idx, lam, eta, rowh, colh, mask, vel, dep)


def per_device(
    adjoint_temp,
    velocity,
    visc_flow,
    visc_yield,
    yield_mask,
    radial_inverse,
    marker_rows,
    recv_cells,
    recv_counts,
):
    layers, rows, cols = adjoint_temp.shape
    n_cap = lax.axis_size("cap")
    n_lat = lax.axis_size("lat")
    n_rad = lax.axis_size("rad")
    c = lax.axis_index("cap")
    d = lax.axis_index("lat")
    r = lax.axis_index("rad")

    received = lax.all_to_all(marker_rows, "lat", split_axis=1, concat_axis=1, tiled=True)

    flow = visc_flow.astype(jnp.float32)
    plast = visc_yield.astype(jnp.float32)
    eta = jnp.where(yield_mask == 1, flow * plast / (flow + plast), flow)

    g = GHOST
    ext_rows = ((rows + 2 * g + 7) // 8) * 8
    ext_cols = ((cols + 2 * g + 127) // 128) * 128
    top_send = jnp.concatenate([adjoint_temp[:, rows - g:], eta[:, rows - g:]], axis=1)
    bot_send = jnp.concatenate([adjoint_temp[:, :g], eta[:, :g]], axis=1)
    top = lax.ppermute(top_send, "cap", _pairs(n_cap, 1))
    bot = lax.ppermute(bot_send, "cap", _pairs(n_cap, -1))
    zr = jnp.zeros((layers, ext_rows - rows - 2 * g, cols), jnp.float32)
    rowh = jnp.stack([
        jnp.concatenate([bot[:, :g], zr, top[:, :g]], axis=1),
        jnp.concatenate([bot[:, g:], zr, top[:, g:]], axis=1),
    ])

    def col_piece(sl):
        parts = []
        for k, src in enumerate((adjoint_temp, eta)):
            parts.append(jnp.concatenate([src[:, :, sl], rowh[k][:, :, sl]], axis=1))
        return jnp.stack(parts)

    left_send = col_piece(slice(0, g)).reshape(-1)
    right_send = col_piece(slice(cols - g, cols)).reshape(-1)
    from_right = lax.ppermute(left_send, "lat", _pairs(n_lat, -1)).reshape(2, layers, ext_rows, g)
    from_left = lax.ppermute(right_send, "lat", _pairs(n_lat, 1)).reshape(2, layers, ext_rows, g)
    zc = jnp.zeros((2, layers, ext_rows, ext_cols - cols - 2 * g), jnp.float32)
    colh = jnp.concatenate([from_right, zc, from_left], axis=3)
    mask = _inside_mask(rows, cols, ext_rows, ext_cols, c, d, n_cap, n_lat)

    senders = n_lat
    slot_total = received.shape[1]
    per_sender = slot_total // senders
    live = (jnp.arange(per_sender, dtype=jnp.int32)[None, :] < recv_counts[:, None]).reshape(-1)
    cell_a = recv_cells // cols
    cell_b = recv_cells % cols
    hit_a = (cell_a[None, :] == jnp.arange(rows, dtype=jnp.int32)[:, None]) & live[None, :]
    xa = jnp.where(hit_a[None], received[:, None, :], jnp.zeros((), received.dtype))
    onehot_b = (cell_b[:, None] == jnp.arange(cols, dtype=jnp.int32)[None, :]).astype(received.dtype)
    deposit = jnp.einsum("las,sb->lab", xa, onehot_b, preferred_element_type=jnp.float32)

    rad_idx = r.astype(jnp.int32).reshape(1)
    n_chunks = 4
    chunk = layers // n_chunks
    block_layers = 4
    keeps = []
    recvs = []
    for k in range(n_chunks):
        send, keep = _sweeps(
            rad_idx, adjoint_temp, eta, rowh, colh, mask, velocity, deposit,
            k * chunk, chunk, block_layers,
        )
        recvs.append(lax.ppermute(send, "rad", _pairs(n_rad, 1) + _pairs(n_rad, -1)))
        keeps.append(keep)

    full_layers = radial_inverse.shape[0]
    mine = jnp.concatenate(keeps, axis=0)
    theirs = jnp.concatenate(recvs, axis=0)
    columns = jnp.concatenate([mine, theirs], axis=0)
    my_cols = lax.dynamic_slice_in_dim(radial_inverse, r * layers, layers, axis=1)
    peer_cols = lax.dynamic_slice_in_dim(radial_inverse, (1 - r) * layers, layers, axis=1)
    r_perm = jnp.concatenate([my_cols, peer_cols], axis=1)
    result = jnp.dot(
        r_perm, columns.reshape(full_layers, -1), precision=lax.Precision.HIGHEST
    )
    return result.reshape(columns.shape)


def solution(mesh):
    in_specs = (
        P("rad", "cap", "lat"),
        P(None, "rad", "cap", "lat"),
        P("rad", "cap", "lat"),
        P("rad", "cap", "lat"),
        P("rad", "cap", "lat"),
        P(),
        P("rad", ("cap", "lat")),
        P(("cap", "lat")),
        P(("cap", "lat")),
    )
    out_specs = P(None, ("cap", "rad"), "lat")
    return jax.shard_map(
        per_device, mesh=mesh, in_specs=in_specs, out_specs=out_specs, check_vma=False
    )
```

```python
import jax
import jax.numpy as jnp
from jax import lax
from jax.experimental import pallas as pl
from jax.experimental.pallas import tpu as pltpu
from jax.sharding import PartitionSpec as P

PICARD = 3
GHOST = 3

relax_coef = 0.25
advect_coef = 0.1


def _inside_mask(rows, cols, ext_rows, ext_cols, c, d, n_cap, n_lat):
    g = GHOST
    far = -(1 << 20)
    i = jnp.arange(ext_rows, dtype=jnp.int32)
    j = jnp.arange(ext_cols, dtype=jnp.int32)
    local_r = jnp.where(i < rows + g, i, jnp.where(i >= ext_rows - g, i - ext_rows, far))
    local_c = jnp.where(j < cols + g, j, jnp.where(j >= ext_cols - g, j - ext_cols, far))
    glob_r = c * rows + local_r
    glob_c = d * cols + local_c
    ok_r = (local_r > far) & (glob_r >= 0) & (glob_r < n_cap * rows)
    ok_c = (local_c > far) & (glob_c >= 0) & (glob_c < n_lat * cols)
    return (ok_r[:, None] & ok_c[None, :]).astype(jnp.float32)


def _pairs(n, step):
    return [(i, i + step) for i in range(n) if 0 <= i + step < n]


def _sweep_kernel(rad_ref, lam_ref, eta_ref, rowh_ref, colh_ref, mask_ref, vel_ref, dep_ref,
                  after_ref, recv_ref, send_ref, keep_ref, lam_x, eta_x):
    layers, rows, cols = lam_ref.shape
    n_r, n_c = lam_x.shape[1], lam_x.shape[2]
    for ref, src, k in ((lam_x, lam_ref, 0), (eta_x, eta_ref, 1)):
        ref[:, :rows, :cols] = src[...]
        ref[:, rows:, :cols] = rowh_ref[k]
        ref[:, :, cols:] = colh_ref[k]
    lam = lam_x[...]
    eta = eta_x[...]
    m = mask_ref[...][None]

    def up(x):
        return pltpu.roll(x, n_r - 1, 1)

    def dn(x):
        return pltpu.roll(x, 1, 1)

    def rt(x):
        return pltpu.roll(x, n_c - 1, 2)

    def lf(x):
        return pltpu.roll(x, 1, 2)

    ca_raw = 0.5 * (eta + up(eta))
    cb_raw = 0.5 * (eta + rt(eta))
    mq = relax_coef * m
    ca = ca_raw * mq
    cd = dn(ca_raw) * mq
    cb = cb_raw * mq
    cl = lf(cb_raw) * mq
    w = lam
    for _ in range(PICARD - 1):
        total = ca * (up(w) - w)
        total = total + cd * (dn(w) - w)
        total = total + cb * (rt(w) - w)
        total = total + cl * (lf(w) - w)
        w = lam + total

    def main(x):
        return x[:, :rows, :cols]

    wm = main(w)
    total = main(ca) * (main(up(w)) - wm)
    total = total + main(cd) * (main(dn(w)) - wm)
    total = total + main(cb) * (main(rt(w)) - wm)
    total = total + main(cl) * (main(lf(w)) - wm)
    w3 = main(lam) + total
    v0 = vel_ref[0].astype(jnp.float32)
    v1 = vel_ref[1].astype(jnp.float32)
    adv = v0 * main(up(lam) - dn(lam)) + v1 * main(rt(lam) - lf(lam))
    rhs = w3 + advect_coef * adv + dep_ref[...]
    half = rows // 2
    lo = rhs[:, :half, :]
    hi = rhs[:, half:, :]
    is_zero = rad_ref[0] == 0
    send_ref[...] = jnp.where(is_zero, hi, lo)
    keep_ref[...] = jnp.where(is_zero, lo, hi)


def _sweeps(rad_idx, lam, eta, rowh, colh, mask, vel, dep, after, recv, first_layer, n_layers,
            block_layers):
    _, rows, cols = lam.shape
    ext_r, ext_c = mask.shape
    half = rows // 2
    off = first_layer // block_layers
    bl = block_layers
    grid = (n_layers // bl,)
    out_shape = [jax.ShapeDtypeStruct((n_layers, half, cols), jnp.float32)] * 2
    return pl.pallas_call(
        _sweep_kernel,
        out_shape=out_shape,
        grid=grid,
        in_specs=[
            pl.BlockSpec(memory_space=pltpu.SMEM),
            pl.BlockSpec((bl, rows, cols), lambda i: (i + off, 0, 0)),
            pl.BlockSpec((bl, rows, cols), lambda i: (i + off, 0, 0)),
            pl.BlockSpec((2, bl, ext_r - rows, cols), lambda i: (0, i + off, 0, 0)),
            pl.BlockSpec((2, bl, ext_r, ext_c - cols), lambda i: (0, i + off, 0, 0)),
            pl.BlockSpec((ext_r, ext_c), lambda i: (0, 0)),
            pl.BlockSpec((2, bl, rows, cols), lambda i: (0, i + off, 0, 0)),
            pl.BlockSpec((bl, rows, cols), lambda i: (i + off, 0, 0)),
            pl.BlockSpec(memory_space=pl.ANY),
            pl.BlockSpec(memory_space=pl.ANY),
        ],
        out_specs=[
            pl.BlockSpec((bl, half, cols), lambda i: (i, 0, 0)),
            pl.BlockSpec((bl, half, cols), lambda i: (i, 0, 0)),
        ],
        scratch_shapes=[
            pltpu.VMEM((bl, ext_r, ext_c), jnp.float32),
            pltpu.VMEM((bl, ext_r, ext_c), jnp.float32),
        ],
        cost_estimate=pl.CostEstimate(
            flops=n_layers * ext_r * ext_c * 60,
            transcendentals=0,
            bytes_accessed=n_layers * (2 * ext_r * ext_c * 4 + rows * cols * 12),
        ),
    )(rad_idx, lam, eta, rowh, colh, mask, vel, dep, after, recv)


def per_device(
    adjoint_temp,
    velocity,
    visc_flow,
    visc_yield,
    yield_mask,
    radial_inverse,
    marker_rows,
    recv_cells,
    recv_counts,
):
    layers, rows, cols = adjoint_temp.shape
    n_cap = lax.axis_size("cap")
    n_lat = lax.axis_size("lat")
    n_rad = lax.axis_size("rad")
    c = lax.axis_index("cap")
    d = lax.axis_index("lat")
    r = lax.axis_index("rad")

    received = lax.all_to_all(marker_rows, "lat", split_axis=1, concat_axis=1, tiled=True)

    flow = visc_flow.astype(jnp.float32)
    plast = visc_yield.astype(jnp.float32)
    eta = jnp.where(yield_mask == 1, flow * plast / (flow + plast), flow)

    g = GHOST
    ext_rows = ((rows + 2 * g + 7) // 8) * 8
    ext_cols = ((cols + 2 * g + 127) // 128) * 128
    top_send = jnp.concatenate([adjoint_temp[:, rows - g:], eta[:, rows - g:]], axis=1)
    bot_send = jnp.concatenate([adjoint_temp[:, :g], eta[:, :g]], axis=1)
    top = lax.ppermute(top_send, "cap", _pairs(n_cap, 1))
    bot = lax.ppermute(bot_send, "cap", _pairs(n_cap, -1))
    zr = jnp.zeros((layers, ext_rows - rows - 2 * g, cols), jnp.float32)
    rowh = jnp.stack([
        jnp.concatenate([bot[:, :g], zr, top[:, :g]], axis=1),
        jnp.concatenate([bot[:, g:], zr, top[:, g:]], axis=1),
    ])

    def col_piece(sl):
        parts = []
        for k, src in enumerate((adjoint_temp, eta)):
            parts.append(jnp.concatenate([src[:, :, sl], rowh[k][:, :, sl]], axis=1))
        return jnp.stack(parts)

    flat = jnp.stack([col_piece(slice(0, g)), col_piece(slice(cols - g, cols))]).reshape(-1)
    piece = flat.shape[0] // 2
    from_right = lax.ppermute(flat[:piece], "lat", _pairs(n_lat, -1))
    from_left = lax.ppermute(flat[piece:], "lat", _pairs(n_lat, 1))
    got = jnp.concatenate([from_right, from_left]).reshape(2, 2, layers, ext_rows, g)
    zc = jnp.zeros((2, layers, ext_rows, ext_cols - cols - 2 * g), jnp.float32)
    colh = jnp.concatenate([got[0], zc, got[1]], axis=3)
    mask = _inside_mask(rows, cols, ext_rows, ext_cols, c, d, n_cap, n_lat)

    senders = n_lat
    slot_total = received.shape[1]
    per_sender = slot_total // senders
    live = (jnp.arange(per_sender, dtype=jnp.int32)[None, :] < recv_counts[:, None]).reshape(-1)
    cell_a = recv_cells // cols
    cell_b = recv_cells % cols
    hit_a = (cell_a[None, :] == jnp.arange(rows, dtype=jnp.int32)[:, None]) & live[None, :]
    xa = jnp.where(hit_a[None], received[:, None, :], jnp.zeros((), received.dtype))
    onehot_b = (cell_b[:, None] == jnp.arange(cols, dtype=jnp.int32)[None, :]).astype(received.dtype)
    deposit = jnp.einsum("las,sb->lab", xa, onehot_b, preferred_element_type=jnp.float32)

    rad_idx = r.astype(jnp.int32).reshape(1)
    n_chunks = 4
    chunk = layers // n_chunks
    block_layers = 4
    keeps = []
    recvs = []
    after = rad_idx
    for k in range(n_chunks):
        landed = recvs[k - 2] if k >= 2 else rad_idx
        send, keep = _sweeps(
            rad_idx, adjoint_temp, eta, rowh, colh, mask, velocity, deposit, after, landed,
            k * chunk, chunk, block_layers,
        )
        after = keep
        recvs.append(lax.ppermute(send, "rad", _pairs(n_rad, 1) + _pairs(n_rad, -1)))
        keeps.append(keep)

    full_layers = radial_inverse.shape[0]
    mine = jnp.concatenate(keeps, axis=0)
    theirs = jnp.concatenate(recvs, axis=0)
    columns = jnp.concatenate([mine, theirs], axis=0)
    my_cols = lax.dynamic_slice_in_dim(radial_inverse, r * layers, layers, axis=1)
    peer_cols = lax.dynamic_slice_in_dim(radial_inverse, (1 - r) * layers, layers, axis=1)
    r_perm = jnp.concatenate([my_cols, peer_cols], axis=1)
    result = jnp.dot(
        r_perm, columns.reshape(full_layers, -1), precision=lax.Precision.HIGHEST
    )
    return result.reshape(columns.shape)


def solution(mesh):
    in_specs = (
        P("rad", "cap", "lat"),
        P(None, "rad", "cap", "lat"),
        P("rad", "cap", "lat"),
        P("rad", "cap", "lat"),
        P("rad", "cap", "lat"),
        P(),
        P("rad", ("cap", "lat")),
        P(("cap", "lat")),
        P(("cap", "lat")),
    )
    out_specs = P(None, ("cap", "rad"), "lat")
    return jax.shard_map(
        per_device, mesh=mesh, in_specs=in_specs, out_specs=out_specs, check_vma=False
    )
```

```python
import jax
import jax.numpy as jnp
from jax import lax
from jax.experimental import pallas as pl
from jax.experimental.pallas import tpu as pltpu
from jax.sharding import PartitionSpec as P

PICARD = 3
GHOST = 3

relax_coef = 0.25
advect_coef = 0.1


def _inside_mask(rows, cols, ext_rows, ext_cols, c, d, n_cap, n_lat):
    g = GHOST
    far = -(1 << 20)
    i = jnp.arange(ext_rows, dtype=jnp.int32)
    j = jnp.arange(ext_cols, dtype=jnp.int32)
    local_r = jnp.where(i < rows + g, i, jnp.where(i >= ext_rows - g, i - ext_rows, far))
    local_c = jnp.where(j < cols + g, j, jnp.where(j >= ext_cols - g, j - ext_cols, far))
    glob_r = c * rows + local_r
    glob_c = d * cols + local_c
    ok_r = (local_r > far) & (glob_r >= 0) & (glob_r < n_cap * rows)
    ok_c = (local_c > far) & (glob_c >= 0) & (glob_c < n_lat * cols)
    return (ok_r[:, None] & ok_c[None, :]).astype(jnp.float32)


def _pairs(n, step):
    return [(i, i + step) for i in range(n) if 0 <= i + step < n]


def _sweep_kernel(rad_ref, lam_ref, eta_ref, rowh_ref, colh_ref, mask_ref, vel_ref, dep_ref,
                  after_ref, recv_ref, send_ref, keep_ref, lam_x, eta_x):
    layers, rows, cols = lam_ref.shape
    n_r, n_c = lam_x.shape[1], lam_x.shape[2]
    for ref, src, k in ((lam_x, lam_ref, 0), (eta_x, eta_ref, 1)):
        ref[:, :rows, :cols] = src[...]
        ref[:, rows:, :cols] = rowh_ref[k]
        ref[:, :, cols:] = colh_ref[k]
    lam = lam_x[...]
    eta = eta_x[...]
    m = mask_ref[...][None]

    def up(x):
        return pltpu.roll(x, n_r - 1, 1)

    def dn(x):
        return pltpu.roll(x, 1, 1)

    def rt(x):
        return pltpu.roll(x, n_c - 1, 2)

    def lf(x):
        return pltpu.roll(x, 1, 2)

    ca_raw = 0.5 * (eta + up(eta))
    cb_raw = 0.5 * (eta + rt(eta))
    mq = relax_coef * m
    ca = ca_raw * mq
    cd = dn(ca_raw) * mq
    cb = cb_raw * mq
    cl = lf(cb_raw) * mq
    w = lam
    for _ in range(PICARD - 1):
        total = ca * (up(w) - w)
        total = total + cd * (dn(w) - w)
        total = total + cb * (rt(w) - w)
        total = total + cl * (lf(w) - w)
        w = lam + total

    def main(x):
        return x[:, :rows, :cols]

    wm = main(w)
    total = main(ca) * (main(up(w)) - wm)
    total = total + main(cd) * (main(dn(w)) - wm)
    total = total + main(cb) * (main(rt(w)) - wm)
    total = total + main(cl) * (main(lf(w)) - wm)
    w3 = main(lam) + total
    v0 = vel_ref[0].astype(jnp.float32)
    v1 = vel_ref[1].astype(jnp.float32)
    adv = v0 * main(up(lam) - dn(lam)) + v1 * main(rt(lam) - lf(lam))
    rhs = w3 + advect_coef * adv + dep_ref[...]
    half = rows // 2
    lo = rhs[:, :half, :]
    hi = rhs[:, half:, :]
    is_zero = rad_ref[0] == 0
    send_ref[...] = jnp.where(is_zero, hi, lo)
    keep_ref[...] = jnp.where(is_zero, lo, hi)


def _sweeps(rad_idx, lam, eta, rowh, colh, mask, vel, dep, after, recv, first_layer, n_layers,
            block_layers):
    _, rows, cols = lam.shape
    ext_r, ext_c = mask.shape
    half = rows // 2
    off = first_layer // block_layers
    bl = block_layers
    grid = (n_layers // bl,)
    out_shape = [jax.ShapeDtypeStruct((n_layers, half, cols), jnp.float32)] * 2
    return pl.pallas_call(
        _sweep_kernel,
        out_shape=out_shape,
        grid=grid,
        in_specs=[
            pl.BlockSpec(memory_space=pltpu.SMEM),
            pl.BlockSpec((bl, rows, cols), lambda i: (i + off, 0, 0)),
            pl.BlockSpec((bl, rows, cols), lambda i: (i + off, 0, 0)),
            pl.BlockSpec((2, bl, ext_r - rows, cols), lambda i: (0, i + off, 0, 0)),
            pl.BlockSpec((2, bl, ext_r, ext_c - cols), lambda i: (0, i + off, 0, 0)),
            pl.BlockSpec((ext_r, ext_c), lambda i: (0, 0)),
            pl.BlockSpec((2, bl, rows, cols), lambda i: (0, i + off, 0, 0)),
            pl.BlockSpec((bl, rows, cols), lambda i: (i + off, 0, 0)),
            pl.BlockSpec(memory_space=pl.ANY),
            pl.BlockSpec(memory_space=pl.ANY),
        ],
        out_specs=[
            pl.BlockSpec((bl, half, cols), lambda i: (i, 0, 0)),
            pl.BlockSpec((bl, half, cols), lambda i: (i, 0, 0)),
        ],
        scratch_shapes=[
            pltpu.VMEM((bl, ext_r, ext_c), jnp.float32),
            pltpu.VMEM((bl, ext_r, ext_c), jnp.float32),
        ],
        cost_estimate=pl.CostEstimate(
            flops=n_layers * ext_r * ext_c * 6000,
            transcendentals=0,
            bytes_accessed=n_layers * 1_600_000,
        ),
    )(rad_idx, lam, eta, rowh, colh, mask, vel, dep, after, recv)


def per_device(
    adjoint_temp,
    velocity,
    visc_flow,
    visc_yield,
    yield_mask,
    radial_inverse,
    marker_rows,
    recv_cells,
    recv_counts,
):
    layers, rows, cols = adjoint_temp.shape
    n_cap = lax.axis_size("cap")
    n_lat = lax.axis_size("lat")
    n_rad = lax.axis_size("rad")
    c = lax.axis_index("cap")
    d = lax.axis_index("lat")
    r = lax.axis_index("rad")

    received = lax.all_to_all(marker_rows, "lat", split_axis=1, concat_axis=1, tiled=True)

    flow = visc_flow.astype(jnp.float32)
    plast = visc_yield.astype(jnp.float32)
    eta = jnp.where(yield_mask == 1, flow * plast / (flow + plast), flow)

    g = GHOST
    ext_rows = ((rows + 2 * g + 7) // 8) * 8
    ext_cols = ((cols + 2 * g + 127) // 128) * 128
    top_send = jnp.concatenate([adjoint_temp[:, rows - g:], eta[:, rows - g:]], axis=1)
    bot_send = jnp.concatenate([adjoint_temp[:, :g], eta[:, :g]], axis=1)
    top = lax.ppermute(top_send, "cap", _pairs(n_cap, 1))
    bot = lax.ppermute(bot_send, "cap", _pairs(n_cap, -1))
    zr = jnp.zeros((layers, ext_rows - rows - 2 * g, cols), jnp.float32)
    rowh = jnp.stack([
        jnp.concatenate([bot[:, :g], zr, top[:, :g]], axis=1),
        jnp.concatenate([bot[:, g:], zr, top[:, g:]], axis=1),
    ])

    def col_piece(sl):
        parts = []
        for k, src in enumerate((adjoint_temp, eta)):
            parts.append(jnp.concatenate([src[:, :, sl], rowh[k][:, :, sl]], axis=1))
        return jnp.stack(parts)

    flat = jnp.stack([col_piece(slice(0, g)), col_piece(slice(cols - g, cols))]).reshape(-1)
    piece = flat.shape[0] // 2
    from_right = lax.ppermute(flat[:piece], "lat", _pairs(n_lat, -1))
    from_left = lax.ppermute(flat[piece:], "lat", _pairs(n_lat, 1))
    got = jnp.concatenate([from_right, from_left]).reshape(2, 2, layers, ext_rows, g)
    zc = jnp.zeros((2, layers, ext_rows, ext_cols - cols - 2 * g), jnp.float32)
    colh = jnp.concatenate([got[0], zc, got[1]], axis=3)
    mask = _inside_mask(rows, cols, ext_rows, ext_cols, c, d, n_cap, n_lat)

    senders = n_lat
    slot_total = received.shape[1]
    per_sender = slot_total // senders
    live = (jnp.arange(per_sender, dtype=jnp.int32)[None, :] < recv_counts[:, None]).reshape(-1)
    cell_a = recv_cells // cols
    cell_b = recv_cells % cols
    hit_a = (cell_a[None, :] == jnp.arange(rows, dtype=jnp.int32)[:, None]) & live[None, :]
    xa = jnp.where(hit_a[None], received[:, None, :], jnp.zeros((), received.dtype))
    onehot_b = (cell_b[:, None] == jnp.arange(cols, dtype=jnp.int32)[None, :]).astype(received.dtype)
    deposit = jnp.einsum("las,sb->lab", xa, onehot_b, preferred_element_type=jnp.float32)

    rad_idx = r.astype(jnp.int32).reshape(1)
    n_chunks = 4
    chunk = layers // n_chunks
    block_layers = 4
    keeps = []
    recvs = []
    after = rad_idx
    for k in range(n_chunks):
        landed = recvs[k - 2] if k >= 2 else rad_idx
        send, keep = _sweeps(
            rad_idx, adjoint_temp, eta, rowh, colh, mask, velocity, deposit, after, landed,
            k * chunk, chunk, block_layers,
        )
        after = keep
        recvs.append(lax.ppermute(send, "rad", _pairs(n_rad, 1) + _pairs(n_rad, -1)))
        keeps.append(keep)

    my_cols = lax.dynamic_slice_in_dim(radial_inverse, r * layers, layers, axis=1)
    peer_cols = lax.dynamic_slice_in_dim(radial_inverse, (1 - r) * layers, layers, axis=1)
    r_perm = jnp.concatenate([my_cols, peer_cols], axis=1)
    return _radial(r_perm, keeps + recvs)


def _radial_kernel(kr_ref, *refs):
    pieces, out_ref = refs[:-1], refs[-1]
    x = jnp.concatenate([p[...] for p in pieces], axis=0)
    n_l, n_a, n_b = x.shape
    tile = kr_ref.shape[0] // n_l
    for t in range(n_a // tile):
        xt = x[:, t * tile:(t + 1) * tile, :].reshape(n_l * tile, n_b)
        yt = jnp.dot(kr_ref[...], xt, precision=lax.Precision.HIGHEST,
                     preferred_element_type=jnp.float32)
        out_ref[:, t * tile:(t + 1) * tile, :] = yt.reshape(n_l, tile, n_b)


def _radial(r_perm, pieces):
    tile = 8
    n_l = r_perm.shape[0]
    _, n_a, n_b = pieces[0].shape
    kr = jnp.kron(r_perm, jnp.eye(tile, dtype=jnp.float32))
    return pl.pallas_call(
        _radial_kernel,
        out_shape=jax.ShapeDtypeStruct((n_l, n_a, n_b), jnp.float32),
        in_specs=[pl.BlockSpec(memory_space=pltpu.VMEM)] * (1 + len(pieces)),
        out_specs=pl.BlockSpec(memory_space=pltpu.VMEM),
    )(kr, *pieces)


def solution(mesh):
    in_specs = (
        P("rad", "cap", "lat"),
        P(None, "rad", "cap", "lat"),
        P("rad", "cap", "lat"),
        P("rad", "cap", "lat"),
        P("rad", "cap", "lat"),
        P(),
        P("rad", ("cap", "lat")),
        P(("cap", "lat")),
        P(("cap", "lat")),
    )
    out_specs = P(None, ("cap", "rad"), "lat")
    return jax.shard_map(
        per_device, mesh=mesh, in_specs=in_specs, out_specs=out_specs, check_vma=False
    )
```

```python
import functools

import jax
import jax.numpy as jnp
from jax import lax
from jax.experimental import pallas as pl
from jax.experimental.pallas import tpu as pltpu
from jax.sharding import PartitionSpec as P

PICARD = 3
GHOST = 3

relax_coef = 0.25
advect_coef = 0.1


def _inside_mask(rows, cols, ext_rows, ext_cols, c, d, n_cap, n_lat):
    g = GHOST
    far = -(1 << 20)
    i = jnp.arange(ext_rows, dtype=jnp.int32)
    j = jnp.arange(ext_cols, dtype=jnp.int32)
    local_r = jnp.where(i < rows + g, i, jnp.where(i >= ext_rows - g, i - ext_rows, far))
    local_c = jnp.where(j < cols + g, j, jnp.where(j >= ext_cols - g, j - ext_cols, far))
    glob_r = c * rows + local_r
    glob_c = d * cols + local_c
    ok_r = (local_r > far) & (glob_r >= 0) & (glob_r < n_cap * rows)
    ok_c = (local_c > far) & (glob_c >= 0) & (glob_c < n_lat * cols)
    return (ok_r[:, None] & ok_c[None, :]).astype(jnp.float32)


def _pairs(n, step):
    return [(i, i + step) for i in range(n) if 0 <= i + step < n]


def _sweep_kernel(rad_ref, lam_ref, eta_ref, rowh_ref, colh_ref, mask_ref, vel_ref, dep_ref,
                  after_ref, recv_ref, send_ref, keep_ref, lam_x, eta_x):
    layers, rows, cols = lam_ref.shape
    n_r, n_c = lam_x.shape[1], lam_x.shape[2]
    for ref, src, k in ((lam_x, lam_ref, 0), (eta_x, eta_ref, 1)):
        ref[:, :rows, :cols] = src[...]
        ref[:, rows:, :cols] = rowh_ref[k]
        ref[:, :, cols:] = colh_ref[k]
    lam = lam_x[...]
    eta = eta_x[...]
    m = mask_ref[...][None]

    def up(x):
        return pltpu.roll(x, n_r - 1, 1)

    def dn(x):
        return pltpu.roll(x, 1, 1)

    def rt(x):
        return pltpu.roll(x, n_c - 1, 2)

    def lf(x):
        return pltpu.roll(x, 1, 2)

    ca_raw = 0.5 * (eta + up(eta))
    cb_raw = 0.5 * (eta + rt(eta))
    mq = relax_coef * m
    ca = ca_raw * mq
    cd = dn(ca_raw) * mq
    cb = cb_raw * mq
    cl = lf(cb_raw) * mq
    w = lam
    for _ in range(PICARD - 1):
        total = ca * (up(w) - w)
        total = total + cd * (dn(w) - w)
        total = total + cb * (rt(w) - w)
        total = total + cl * (lf(w) - w)
        w = lam + total

    def main(x):
        return x[:, :rows, :cols]

    wm = main(w)
    total = main(ca) * (main(up(w)) - wm)
    total = total + main(cd) * (main(dn(w)) - wm)
    total = total + main(cb) * (main(rt(w)) - wm)
    total = total + main(cl) * (main(lf(w)) - wm)
    w3 = main(lam) + total
    v0 = vel_ref[0].astype(jnp.float32)
    v1 = vel_ref[1].astype(jnp.float32)
    adv = v0 * main(up(lam) - dn(lam)) + v1 * main(rt(lam) - lf(lam))
    rhs = w3 + advect_coef * adv + dep_ref[...]
    half = rows // 2
    lo = rhs[:, :half, :]
    hi = rhs[:, half:, :]
    is_zero = rad_ref[0] == 0
    send_ref[...] = jnp.where(is_zero, hi, lo)
    keep_ref[...] = jnp.where(is_zero, lo, hi)


def _sweeps(rad_idx, lam, eta, rowh, colh, mask, vel, dep, after, recv, first_layer, n_layers,
            block_layers):
    _, rows, cols = lam.shape
    ext_r, ext_c = mask.shape
    half = rows // 2
    off = first_layer // block_layers
    bl = block_layers
    grid = (n_layers // bl,)
    out_shape = [jax.ShapeDtypeStruct((n_layers, half, cols), jnp.float32)] * 2
    return pl.pallas_call(
        _sweep_kernel,
        out_shape=out_shape,
        grid=grid,
        in_specs=[
            pl.BlockSpec(memory_space=pltpu.SMEM),
            pl.BlockSpec((bl, rows, cols), lambda i: (i + off, 0, 0)),
            pl.BlockSpec((bl, rows, cols), lambda i: (i + off, 0, 0)),
            pl.BlockSpec((2, bl, ext_r - rows, cols), lambda i: (0, i + off, 0, 0)),
            pl.BlockSpec((2, bl, ext_r, ext_c - cols), lambda i: (0, i + off, 0, 0)),
            pl.BlockSpec((ext_r, ext_c), lambda i: (0, 0)),
            pl.BlockSpec((2, bl, rows, cols), lambda i: (0, i + off, 0, 0)),
            pl.BlockSpec((bl, rows, cols), lambda i: (i + off, 0, 0)),
            pl.BlockSpec(memory_space=pl.ANY),
            pl.BlockSpec(memory_space=pl.ANY),
        ],
        out_specs=[
            pl.BlockSpec((bl, half, cols), lambda i: (i, 0, 0)),
            pl.BlockSpec((bl, half, cols), lambda i: (i, 0, 0)),
        ],
        scratch_shapes=[
            pltpu.VMEM((bl, ext_r, ext_c), jnp.float32),
            pltpu.VMEM((bl, ext_r, ext_c), jnp.float32),
        ],
        cost_estimate=pl.CostEstimate(
            flops=n_layers * ext_r * ext_c * 6000,
            transcendentals=0,
            bytes_accessed=n_layers * 1_600_000,
        ),
    )(rad_idx, lam, eta, rowh, colh, mask, vel, dep, after, recv)


def per_device(
    adjoint_temp,
    velocity,
    visc_flow,
    visc_yield,
    yield_mask,
    radial_inverse,
    marker_rows,
    recv_cells,
    recv_counts,
):
    layers, rows, cols = adjoint_temp.shape
    n_cap = lax.axis_size("cap")
    n_lat = lax.axis_size("lat")
    n_rad = lax.axis_size("rad")
    c = lax.axis_index("cap")
    d = lax.axis_index("lat")
    r = lax.axis_index("rad")

    received = lax.all_to_all(marker_rows, "lat", split_axis=1, concat_axis=1, tiled=True)

    flow = visc_flow.astype(jnp.float32)
    plast = visc_yield.astype(jnp.float32)
    eta = jnp.where(yield_mask == 1, flow * plast / (flow + plast), flow)

    g = GHOST
    ext_rows = ((rows + 2 * g + 7) // 8) * 8
    ext_cols = ((cols + 2 * g + 127) // 128) * 128
    top_send = jnp.concatenate([adjoint_temp[:, rows - g:], eta[:, rows - g:]], axis=1)
    bot_send = jnp.concatenate([adjoint_temp[:, :g], eta[:, :g]], axis=1)
    top = lax.ppermute(top_send, "cap", _pairs(n_cap, 1))
    bot = lax.ppermute(bot_send, "cap", _pairs(n_cap, -1))
    zr = jnp.zeros((layers, ext_rows - rows - 2 * g, cols), jnp.float32)
    rowh = jnp.stack([
        jnp.concatenate([bot[:, :g], zr, top[:, :g]], axis=1),
        jnp.concatenate([bot[:, g:], zr, top[:, g:]], axis=1),
    ])

    def col_piece(sl):
        parts = []
        for k, src in enumerate((adjoint_temp, eta)):
            parts.append(jnp.concatenate([src[:, :, sl], rowh[k][:, :, sl]], axis=1))
        return jnp.stack(parts)

    flat = jnp.stack([col_piece(slice(0, g)), col_piece(slice(cols - g, cols))]).reshape(-1)
    piece = flat.shape[0] // 2
    from_right = lax.ppermute(flat[:piece], "lat", _pairs(n_lat, -1))
    from_left = lax.ppermute(flat[piece:], "lat", _pairs(n_lat, 1))
    got = jnp.concatenate([from_right, from_left]).reshape(2, 2, layers, ext_rows, g)
    zc = jnp.zeros((2, layers, ext_rows, ext_cols - cols - 2 * g), jnp.float32)
    colh = jnp.concatenate([got[0], zc, got[1]], axis=3)
    mask = _inside_mask(rows, cols, ext_rows, ext_cols, c, d, n_cap, n_lat)

    senders = n_lat
    slot_total = received.shape[1]
    per_sender = slot_total // senders
    live = (jnp.arange(per_sender, dtype=jnp.int32)[None, :] < recv_counts[:, None]).reshape(-1)
    cell_a = recv_cells // cols
    cell_b = recv_cells % cols
    hit_a = (cell_a[None, :] == jnp.arange(rows, dtype=jnp.int32)[:, None]) & live[None, :]
    xa = jnp.where(hit_a[None], received[:, None, :], jnp.zeros((), received.dtype))
    onehot_b = (cell_b[:, None] == jnp.arange(cols, dtype=jnp.int32)[None, :]).astype(received.dtype)
    deposit = jnp.einsum("las,sb->lab", xa, onehot_b, preferred_element_type=jnp.float32)

    rad_idx = r.astype(jnp.int32).reshape(1)
    n_chunks = 4
    chunk = layers // n_chunks
    block_layers = 4
    keeps = []
    recvs = []
    after = rad_idx
    for k in range(n_chunks):
        landed = recvs[k - 2] if k >= 2 else rad_idx
        send, keep = _sweeps(
            rad_idx, adjoint_temp, eta, rowh, colh, mask, velocity, deposit, after, landed,
            k * chunk, chunk, block_layers,
        )
        after = keep
        recvs.append(lax.ppermute(send, "rad", _pairs(n_rad, 1) + _pairs(n_rad, -1)))
        keeps.append(keep)

    my_cols = lax.dynamic_slice_in_dim(radial_inverse, r * layers, layers, axis=1)
    peer_cols = lax.dynamic_slice_in_dim(radial_inverse, (1 - r) * layers, layers, axis=1)
    r_perm = jnp.concatenate([my_cols, peer_cols], axis=1)
    pieces = keeps + recvs
    split = len(pieces) - 2
    step = pieces[0].shape[0]
    partial = _radial(r_perm[:, :split * step], pieces[:split], after=recvs[-2])
    return _radial(r_perm[:, split * step:], pieces[split:], partial=partial)


def _radial_kernel(n_pieces, has_partial, r_ref, *refs):
    pieces = refs[:n_pieces]
    rest = refs[n_pieces:]
    partial_ref = rest[0] if has_partial else None
    out_ref, xs = rest[-2], rest[-1]
    step = pieces[0].shape[0]
    for i, p in enumerate(pieces):
        xs[i * step:(i + 1) * step] = p[...]
    rmat = r_ref[...]
    for a in range(xs.shape[1]):
        y = jnp.dot(rmat, xs[:, a, :], precision=lax.Precision.HIGHEST,
                    preferred_element_type=jnp.float32)
        if has_partial:
            y = partial_ref[:, a, :] + y
        out_ref[:, a, :] = y


def _radial(r_cols, pieces, partial=None, after=None):
    n_k, n_l = r_cols.shape
    _, n_a, n_b = pieces[0].shape
    extra = [] if partial is None else [partial]
    fake = [] if after is None else [after]
    in_specs = [pl.BlockSpec(memory_space=pltpu.VMEM)] * (1 + len(pieces) + len(extra))
    in_specs += [pl.BlockSpec(memory_space=pl.ANY)] * len(fake)
    return pl.pallas_call(
        functools.partial(_radial_kernel, len(pieces), partial is not None),
        out_shape=jax.ShapeDtypeStruct((n_k, n_a, n_b), jnp.float32),
        in_specs=in_specs,
        out_specs=pl.BlockSpec(memory_space=pltpu.VMEM),
        scratch_shapes=[pltpu.VMEM((n_l, n_a, n_b), jnp.float32)],
    )(r_cols, *pieces, *extra, *fake)


def solution(mesh):
    in_specs = (
        P("rad", "cap", "lat"),
        P(None, "rad", "cap", "lat"),
        P("rad", "cap", "lat"),
        P("rad", "cap", "lat"),
        P("rad", "cap", "lat"),
        P(),
        P("rad", ("cap", "lat")),
        P(("cap", "lat")),
        P(("cap", "lat")),
    )
    out_specs = P(None, ("cap", "rad"), "lat")
    return jax.shard_map(
        per_device, mesh=mesh, in_specs=in_specs, out_specs=out_specs, check_vma=False
    )
```

```python
import functools

import jax
import jax.numpy as jnp
from jax import lax
from jax.experimental import pallas as pl
from jax.experimental.pallas import tpu as pltpu
from jax.sharding import PartitionSpec as P

PICARD = 3
GHOST = 3

relax_coef = 0.25
advect_coef = 0.1


def _inside_mask(rows, cols, ext_rows, ext_cols, c, d, n_cap, n_lat):
    g = GHOST
    far = -(1 << 20)
    i = jnp.arange(ext_rows, dtype=jnp.int32)
    j = jnp.arange(ext_cols, dtype=jnp.int32)
    local_r = jnp.where(i < rows + g, i, jnp.where(i >= ext_rows - g, i - ext_rows, far))
    local_c = jnp.where(j < cols + g, j, jnp.where(j >= ext_cols - g, j - ext_cols, far))
    glob_r = c * rows + local_r
    glob_c = d * cols + local_c
    ok_r = (local_r > far) & (glob_r >= 0) & (glob_r < n_cap * rows)
    ok_c = (local_c > far) & (glob_c >= 0) & (glob_c < n_lat * cols)
    return (ok_r[:, None] & ok_c[None, :]).astype(jnp.float32)


def _pairs(n, step):
    return [(i, i + step) for i in range(n) if 0 <= i + step < n]


def _sweep_kernel(rad_ref, lam_ref, eta_ref, rowh_ref, colh_ref, mask_ref, vel_ref, dep_ref,
                  after_ref, recv_ref, send_ref, keep_ref, lam_x, eta_x):
    layers, rows, cols = lam_ref.shape
    n_r, n_c = lam_x.shape[1], lam_x.shape[2]
    for ref, src, k in ((lam_x, lam_ref, 0), (eta_x, eta_ref, 1)):
        ref[:, :rows, :cols] = src[...]
        ref[:, rows:, :cols] = rowh_ref[k]
        ref[:, :, cols:] = colh_ref[k]
    lam = lam_x[...]
    eta = eta_x[...]
    m = mask_ref[...][None]

    def up(x):
        return pltpu.roll(x, n_r - 1, 1)

    def dn(x):
        return pltpu.roll(x, 1, 1)

    def rt(x):
        return pltpu.roll(x, n_c - 1, 2)

    def lf(x):
        return pltpu.roll(x, 1, 2)

    ca_raw = 0.5 * (eta + up(eta))
    cb_raw = 0.5 * (eta + rt(eta))
    mq = relax_coef * m
    ca = ca_raw * mq
    cd = dn(ca_raw) * mq
    cb = cb_raw * mq
    cl = lf(cb_raw) * mq
    w = lam
    for _ in range(PICARD - 1):
        total = ca * (up(w) - w)
        total = total + cd * (dn(w) - w)
        total = total + cb * (rt(w) - w)
        total = total + cl * (lf(w) - w)
        w = lam + total

    def main(x):
        return x[:, :rows, :cols]

    wm = main(w)
    total = main(ca) * (main(up(w)) - wm)
    total = total + main(cd) * (main(dn(w)) - wm)
    total = total + main(cb) * (main(rt(w)) - wm)
    total = total + main(cl) * (main(lf(w)) - wm)
    w3 = main(lam) + total
    v0 = vel_ref[0].astype(jnp.float32)
    v1 = vel_ref[1].astype(jnp.float32)
    adv = v0 * main(up(lam) - dn(lam)) + v1 * main(rt(lam) - lf(lam))
    rhs = w3 + advect_coef * adv + dep_ref[...]
    half = rows // 2
    lo = rhs[:, :half, :]
    hi = rhs[:, half:, :]
    is_zero = rad_ref[0] == 0
    send_ref[...] = jnp.where(is_zero, hi, lo)
    keep_ref[...] = jnp.where(is_zero, lo, hi)


def _sweeps(rad_idx, lam, eta, rowh, colh, mask, vel, dep, after, recv, first_layer, n_layers,
            block_layers):
    _, rows, cols = lam.shape
    ext_r, ext_c = mask.shape
    half = rows // 2
    off = first_layer // block_layers
    bl = block_layers
    grid = (n_layers // bl,)
    out_shape = [jax.ShapeDtypeStruct((n_layers, half, cols), jnp.float32)] * 2
    return pl.pallas_call(
        _sweep_kernel,
        out_shape=out_shape,
        grid=grid,
        in_specs=[
            pl.BlockSpec(memory_space=pltpu.SMEM),
            pl.BlockSpec((bl, rows, cols), lambda i: (i + off, 0, 0)),
            pl.BlockSpec((bl, rows, cols), lambda i: (i + off, 0, 0)),
            pl.BlockSpec((2, bl, ext_r - rows, cols), lambda i: (0, i + off, 0, 0)),
            pl.BlockSpec((2, bl, ext_r, ext_c - cols), lambda i: (0, i + off, 0, 0)),
            pl.BlockSpec((ext_r, ext_c), lambda i: (0, 0)),
            pl.BlockSpec((2, bl, rows, cols), lambda i: (0, i + off, 0, 0)),
            pl.BlockSpec((bl, rows, cols), lambda i: (i + off, 0, 0)),
            pl.BlockSpec(memory_space=pl.ANY),
            pl.BlockSpec(memory_space=pl.ANY),
        ],
        out_specs=[
            pl.BlockSpec((bl, half, cols), lambda i: (i, 0, 0)),
            pl.BlockSpec((bl, half, cols), lambda i: (i, 0, 0)),
        ],
        scratch_shapes=[
            pltpu.VMEM((bl, ext_r, ext_c), jnp.float32),
            pltpu.VMEM((bl, ext_r, ext_c), jnp.float32),
        ],
        cost_estimate=pl.CostEstimate(
            flops=n_layers * ext_r * ext_c * 6000,
            transcendentals=0,
            bytes_accessed=n_layers * 1_600_000,
        ),
    )(rad_idx, lam, eta, rowh, colh, mask, vel, dep, after, recv)


def per_device(
    adjoint_temp,
    velocity,
    visc_flow,
    visc_yield,
    yield_mask,
    radial_inverse,
    marker_rows,
    recv_cells,
    recv_counts,
):
    layers, rows, cols = adjoint_temp.shape
    n_cap = lax.axis_size("cap")
    n_lat = lax.axis_size("lat")
    n_rad = lax.axis_size("rad")
    c = lax.axis_index("cap")
    d = lax.axis_index("lat")
    r = lax.axis_index("rad")

    received = lax.all_to_all(marker_rows, "lat", split_axis=1, concat_axis=1, tiled=True)

    flow = visc_flow.astype(jnp.float32)
    plast = visc_yield.astype(jnp.float32)
    eta = jnp.where(yield_mask == 1, flow * plast / (flow + plast), flow)

    g = GHOST
    ext_rows = ((rows + 2 * g + 7) // 8) * 8
    ext_cols = ((cols + 2 * g + 127) // 128) * 128
    top_send = jnp.concatenate([adjoint_temp[:, rows - g:], eta[:, rows - g:]], axis=1)
    bot_send = jnp.concatenate([adjoint_temp[:, :g], eta[:, :g]], axis=1)
    top = lax.ppermute(top_send, "cap", _pairs(n_cap, 1))
    bot = lax.ppermute(bot_send, "cap", _pairs(n_cap, -1))
    zr = jnp.zeros((layers, ext_rows - rows - 2 * g, cols), jnp.float32)
    rowh = jnp.stack([
        jnp.concatenate([bot[:, :g], zr, top[:, :g]], axis=1),
        jnp.concatenate([bot[:, g:], zr, top[:, g:]], axis=1),
    ])

    def col_piece(sl):
        parts = []
        for k, src in enumerate((adjoint_temp, eta)):
            parts.append(jnp.concatenate([src[:, :, sl], rowh[k][:, :, sl]], axis=1))
        return jnp.stack(parts)

    flat = jnp.stack([col_piece(slice(0, g)), col_piece(slice(cols - g, cols))]).reshape(-1)
    piece = flat.shape[0] // 2
    from_right = lax.ppermute(flat[:piece], "lat", _pairs(n_lat, -1))
    from_left = lax.ppermute(flat[piece:], "lat", _pairs(n_lat, 1))
    got = jnp.concatenate([from_right, from_left]).reshape(2, 2, layers, ext_rows, g)
    zc = jnp.zeros((2, layers, ext_rows, ext_cols - cols - 2 * g), jnp.float32)
    colh = jnp.concatenate([got[0], zc, got[1]], axis=3)
    mask = _inside_mask(rows, cols, ext_rows, ext_cols, c, d, n_cap, n_lat)

    senders = n_lat
    slot_total = received.shape[1]
    per_sender = slot_total // senders
    live = (jnp.arange(per_sender, dtype=jnp.int32)[None, :] < recv_counts[:, None]).reshape(-1)
    cell_a = recv_cells // cols
    cell_b = recv_cells % cols
    hit_a = (cell_a[None, :] == jnp.arange(rows, dtype=jnp.int32)[:, None]) & live[None, :]
    xa = jnp.where(hit_a[None], received[:, None, :], jnp.zeros((), received.dtype))
    onehot_b = (cell_b[:, None] == jnp.arange(cols, dtype=jnp.int32)[None, :]).astype(received.dtype)
    deposit = jnp.einsum("las,sb->lab", xa, onehot_b, preferred_element_type=jnp.float32)

    rad_idx = r.astype(jnp.int32).reshape(1)
    n_chunks = 4
    chunk = layers // n_chunks
    block_layers = 4
    keeps = []
    recvs = []
    after = rad_idx
    for k in range(n_chunks):
        landed = recvs[k - 2] if k >= 2 else rad_idx
        send, keep = _sweeps(
            rad_idx, adjoint_temp, eta, rowh, colh, mask, velocity, deposit, after, landed,
            k * chunk, chunk, block_layers,
        )
        after = keep
        recvs.append(lax.ppermute(send, "rad", _pairs(n_rad, 1) + _pairs(n_rad, -1)))
        keeps.append(keep)

    my_cols = lax.dynamic_slice_in_dim(radial_inverse, r * layers, layers, axis=1)
    peer_cols = lax.dynamic_slice_in_dim(radial_inverse, (1 - r) * layers, layers, axis=1)
    r_perm = jnp.concatenate([my_cols, peer_cols], axis=1)
    pieces = keeps + recvs
    split = len(pieces) - 2
    step = pieces[0].shape[0]
    partial = _radial(r_perm[:, :split * step], pieces[:split], after=recvs[-2])
    return _radial(r_perm[:, split * step:], pieces[split:], partial=partial)


def _radial_kernel(n_pieces, has_partial, r_ref, *refs):
    pieces = refs[:n_pieces]
    rest = refs[n_pieces:]
    partial_ref = rest[0] if has_partial else None
    out_ref, xs = rest[-2], rest[-1]
    step = pieces[0].shape[0]
    for i, p in enumerate(pieces):
        xs[i * step:(i + 1) * step] = p[...]
    rmat = r_ref[...]
    for a in range(xs.shape[1]):
        y = jnp.dot(rmat, xs[:, a, :], precision=lax.Precision.HIGH,
                    preferred_element_type=jnp.float32)
        if has_partial:
            y = partial_ref[:, a, :] + y
        out_ref[:, a, :] = y


def _radial(r_cols, pieces, partial=None, after=None):
    n_k, n_l = r_cols.shape
    _, n_a, n_b = pieces[0].shape
    extra = [] if partial is None else [partial]
    fake = [] if after is None else [after]
    in_specs = [pl.BlockSpec(memory_space=pltpu.VMEM)] * (1 + len(pieces) + len(extra))
    in_specs += [pl.BlockSpec(memory_space=pl.ANY)] * len(fake)
    return pl.pallas_call(
        functools.partial(_radial_kernel, len(pieces), partial is not None),
        out_shape=jax.ShapeDtypeStruct((n_k, n_a, n_b), jnp.float32),
        in_specs=in_specs,
        out_specs=pl.BlockSpec(memory_space=pltpu.VMEM),
        scratch_shapes=[pltpu.VMEM((n_l, n_a, n_b), jnp.float32)],
    )(r_cols, *pieces, *extra, *fake)


def solution(mesh):
    in_specs = (
        P("rad", "cap", "lat"),
        P(None, "rad", "cap", "lat"),
        P("rad", "cap", "lat"),
        P("rad", "cap", "lat"),
        P("rad", "cap", "lat"),
        P(),
        P("rad", ("cap", "lat")),
        P(("cap", "lat")),
        P(("cap", "lat")),
    )
    out_specs = P(None, ("cap", "rad"), "lat")
    return jax.shard_map(
        per_device, mesh=mesh, in_specs=in_specs, out_specs=out_specs, check_vma=False
    )
```

```python
import functools

import jax
import jax.numpy as jnp
from jax import lax
from jax.experimental import pallas as pl
from jax.experimental.pallas import tpu as pltpu
from jax.sharding import PartitionSpec as P

PICARD = 3
GHOST = 3

relax_coef = 0.25
advect_coef = 0.1


def _inside_mask(rows, cols, ext_rows, ext_cols, c, d, n_cap, n_lat):
    g = GHOST
    far = -(1 << 20)
    i = jnp.arange(ext_rows, dtype=jnp.int32)
    j = jnp.arange(ext_cols, dtype=jnp.int32)
    local_r = jnp.where(i < rows + g, i, jnp.where(i >= ext_rows - g, i - ext_rows, far))
    local_c = jnp.where(j < cols + g, j, jnp.where(j >= ext_cols - g, j - ext_cols, far))
    glob_r = c * rows + local_r
    glob_c = d * cols + local_c
    ok_r = (local_r > far) & (glob_r >= 0) & (glob_r < n_cap * rows)
    ok_c = (local_c > far) & (glob_c >= 0) & (glob_c < n_lat * cols)
    return (ok_r[:, None] & ok_c[None, :]).astype(jnp.float32)


def _pairs(n, step):
    return [(i, i + step) for i in range(n) if 0 <= i + step < n]


def _sweep_kernel(rad_ref, lam_ref, eta_ref, rowh_ref, colh_ref, mask_ref, vel_ref, dep_ref,
                  after_ref, recv_ref, send_ref, keep_ref, lam_x, eta_x):
    layers, rows, cols = lam_ref.shape
    n_r, n_c = lam_x.shape[1], lam_x.shape[2]
    for ref, src, k in ((lam_x, lam_ref, 0), (eta_x, eta_ref, 1)):
        ref[:, :rows, :cols] = src[...]
        ref[:, rows:, :cols] = rowh_ref[k]
        ref[:, :, cols:] = colh_ref[k]
    lam = lam_x[...]
    eta = eta_x[...]
    m = mask_ref[...][None]

    def up(x):
        return pltpu.roll(x, n_r - 1, 1)

    def dn(x):
        return pltpu.roll(x, 1, 1)

    def rt(x):
        return pltpu.roll(x, n_c - 1, 2)

    def lf(x):
        return pltpu.roll(x, 1, 2)

    ca_raw = 0.5 * (eta + up(eta))
    cb_raw = 0.5 * (eta + rt(eta))
    mq = relax_coef * m
    ca = ca_raw * mq
    cd = dn(ca_raw) * mq
    cb = cb_raw * mq
    cl = lf(cb_raw) * mq
    w = lam
    for _ in range(PICARD - 1):
        total = ca * (up(w) - w)
        total = total + cd * (dn(w) - w)
        total = total + cb * (rt(w) - w)
        total = total + cl * (lf(w) - w)
        w = lam + total

    def main(x):
        return x[:, :rows, :cols]

    wm = main(w)
    total = main(ca) * (main(up(w)) - wm)
    total = total + main(cd) * (main(dn(w)) - wm)
    total = total + main(cb) * (main(rt(w)) - wm)
    total = total + main(cl) * (main(lf(w)) - wm)
    w3 = main(lam) + total
    v0 = vel_ref[0].astype(jnp.float32)
    v1 = vel_ref[1].astype(jnp.float32)
    adv = v0 * main(up(lam) - dn(lam)) + v1 * main(rt(lam) - lf(lam))
    rhs = w3 + advect_coef * adv + dep_ref[...]
    half = rows // 2
    lo = rhs[:, :half, :]
    hi = rhs[:, half:, :]
    is_zero = rad_ref[0] == 0
    send_ref[...] = jnp.where(is_zero, hi, lo)
    keep_ref[...] = jnp.where(is_zero, lo, hi)


def _sweeps(rad_idx, lam, eta, rowh, colh, mask, vel, dep, after, recv, first_layer, n_layers,
            block_layers):
    _, rows, cols = lam.shape
    ext_r, ext_c = mask.shape
    half = rows // 2
    off = first_layer // block_layers
    bl = block_layers
    grid = (n_layers // bl,)
    out_shape = [jax.ShapeDtypeStruct((n_layers, half, cols), jnp.float32)] * 2
    return pl.pallas_call(
        _sweep_kernel,
        out_shape=out_shape,
        grid=grid,
        in_specs=[
            pl.BlockSpec(memory_space=pltpu.SMEM),
            pl.BlockSpec((bl, rows, cols), lambda i: (i + off, 0, 0)),
            pl.BlockSpec((bl, rows, cols), lambda i: (i + off, 0, 0)),
            pl.BlockSpec((2, bl, ext_r - rows, cols), lambda i: (0, i + off, 0, 0)),
            pl.BlockSpec((2, bl, ext_r, ext_c - cols), lambda i: (0, i + off, 0, 0)),
            pl.BlockSpec((ext_r, ext_c), lambda i: (0, 0)),
            pl.BlockSpec((2, bl, rows, cols), lambda i: (0, i + off, 0, 0)),
            pl.BlockSpec((bl, rows, cols), lambda i: (i + off, 0, 0)),
            pl.BlockSpec(memory_space=pl.ANY),
            pl.BlockSpec(memory_space=pl.ANY),
        ],
        out_specs=[
            pl.BlockSpec((bl, half, cols), lambda i: (i, 0, 0)),
            pl.BlockSpec((bl, half, cols), lambda i: (i, 0, 0)),
        ],
        scratch_shapes=[
            pltpu.VMEM((bl, ext_r, ext_c), jnp.float32),
            pltpu.VMEM((bl, ext_r, ext_c), jnp.float32),
        ],
        cost_estimate=pl.CostEstimate(
            flops=n_layers * ext_r * ext_c * 6000,
            transcendentals=0,
            bytes_accessed=n_layers * 1_600_000,
        ),
    )(rad_idx, lam, eta, rowh, colh, mask, vel, dep, after, recv)


def per_device(
    adjoint_temp,
    velocity,
    visc_flow,
    visc_yield,
    yield_mask,
    radial_inverse,
    marker_rows,
    recv_cells,
    recv_counts,
):
    layers, rows, cols = adjoint_temp.shape
    n_cap = lax.axis_size("cap")
    n_lat = lax.axis_size("lat")
    n_rad = lax.axis_size("rad")
    c = lax.axis_index("cap")
    d = lax.axis_index("lat")
    r = lax.axis_index("rad")

    flow = visc_flow.astype(jnp.float32)
    plast = visc_yield.astype(jnp.float32)
    eta = jnp.where(yield_mask == 1, flow * plast / (flow + plast), flow)

    g = GHOST
    ext_rows = ((rows + 2 * g + 7) // 8) * 8
    ext_cols = ((cols + 2 * g + 127) // 128) * 128
    top_send = jnp.concatenate([adjoint_temp[:, rows - g:], eta[:, rows - g:]], axis=1)
    bot_send = jnp.concatenate([adjoint_temp[:, :g], eta[:, :g]], axis=1)
    top = lax.ppermute(top_send, "cap", _pairs(n_cap, 1))
    bot = lax.ppermute(bot_send, "cap", _pairs(n_cap, -1))
    zr = jnp.zeros((layers, ext_rows - rows - 2 * g, cols), jnp.float32)
    rowh = jnp.stack([
        jnp.concatenate([bot[:, :g], zr, top[:, :g]], axis=1),
        jnp.concatenate([bot[:, g:], zr, top[:, g:]], axis=1),
    ])

    def col_piece(sl):
        parts = []
        for k, src in enumerate((adjoint_temp, eta)):
            parts.append(jnp.concatenate([src[:, :, sl], rowh[k][:, :, sl]], axis=1))
        return jnp.stack(parts)

    flat = jnp.stack([col_piece(slice(0, g)), col_piece(slice(cols - g, cols))]).reshape(-1)
    piece = flat.shape[0] // 2
    flat, markers = lax.optimization_barrier((flat, marker_rows))
    received = lax.all_to_all(markers, "lat", split_axis=1, concat_axis=1, tiled=True)
    from_right = lax.ppermute(flat[:piece], "lat", _pairs(n_lat, -1))
    from_left = lax.ppermute(flat[piece:], "lat", _pairs(n_lat, 1))
    got = jnp.concatenate([from_right, from_left]).reshape(2, 2, layers, ext_rows, g)
    zc = jnp.zeros((2, layers, ext_rows, ext_cols - cols - 2 * g), jnp.float32)
    colh = jnp.concatenate([got[0], zc, got[1]], axis=3)
    mask = _inside_mask(rows, cols, ext_rows, ext_cols, c, d, n_cap, n_lat)

    senders = n_lat
    slot_total = received.shape[1]
    per_sender = slot_total // senders
    live = (jnp.arange(per_sender, dtype=jnp.int32)[None, :] < recv_counts[:, None]).reshape(-1)
    cell_a = recv_cells // cols
    cell_b = recv_cells % cols
    hit_a = (cell_a[None, :] == jnp.arange(rows, dtype=jnp.int32)[:, None]) & live[None, :]
    xa = jnp.where(hit_a[None], received[:, None, :], jnp.zeros((), received.dtype))
    onehot_b = (cell_b[:, None] == jnp.arange(cols, dtype=jnp.int32)[None, :]).astype(received.dtype)
    deposit = jnp.einsum("las,sb->lab", xa, onehot_b, preferred_element_type=jnp.float32)

    rad_idx = r.astype(jnp.int32).reshape(1)
    n_chunks = 4
    chunk = layers // n_chunks
    block_layers = 4
    keeps = []
    recvs = []
    after = rad_idx
    for k in range(n_chunks):
        landed = recvs[k - 2] if k >= 2 else rad_idx
        send, keep = _sweeps(
            rad_idx, adjoint_temp, eta, rowh, colh, mask, velocity, deposit, after, landed,
            k * chunk, chunk, block_layers,
        )
        after = keep
        recvs.append(lax.ppermute(send, "rad", _pairs(n_rad, 1) + _pairs(n_rad, -1)))
        keeps.append(keep)

    my_cols = lax.dynamic_slice_in_dim(radial_inverse, r * layers, layers, axis=1)
    peer_cols = lax.dynamic_slice_in_dim(radial_inverse, (1 - r) * layers, layers, axis=1)
    r_perm = jnp.concatenate([my_cols, peer_cols], axis=1)
    pieces = keeps + recvs
    split = len(pieces) - 2
    step = pieces[0].shape[0]
    partial = _radial(r_perm[:, :split * step], pieces[:split], after=recvs[-2])
    return _radial(r_perm[:, split * step:], pieces[split:], partial=partial)


def _radial_kernel(n_pieces, has_partial, r_ref, *refs):
    pieces = refs[:n_pieces]
    rest = refs[n_pieces:]
    partial_ref = rest[0] if has_partial else None
    out_ref, xs = rest[-2], rest[-1]
    step = pieces[0].shape[0]
    for i, p in enumerate(pieces):
        xs[i * step:(i + 1) * step] = p[...]
    rmat = r_ref[...]
    for a in range(xs.shape[1]):
        y = jnp.dot(rmat, xs[:, a, :], precision=lax.Precision.HIGHEST,
                    preferred_element_type=jnp.float32)
        if has_partial:
            y = partial_ref[:, a, :] + y
        out_ref[:, a, :] = y


def _radial(r_cols, pieces, partial=None, after=None):
    n_k, n_l = r_cols.shape
    _, n_a, n_b = pieces[0].shape
    extra = [] if partial is None else [partial]
    fake = [] if after is None else [after]
    in_specs = [pl.BlockSpec(memory_space=pltpu.VMEM)] * (1 + len(pieces) + len(extra))
    in_specs += [pl.BlockSpec(memory_space=pl.ANY)] * len(fake)
    return pl.pallas_call(
        functools.partial(_radial_kernel, len(pieces), partial is not None),
        out_shape=jax.ShapeDtypeStruct((n_k, n_a, n_b), jnp.float32),
        in_specs=in_specs,
        out_specs=pl.BlockSpec(memory_space=pltpu.VMEM),
        scratch_shapes=[pltpu.VMEM((n_l, n_a, n_b), jnp.float32)],
    )(r_cols, *pieces, *extra, *fake)


def solution(mesh):
    in_specs = (
        P("rad", "cap", "lat"),
        P(None, "rad", "cap", "lat"),
        P("rad", "cap", "lat"),
        P("rad", "cap", "lat"),
        P("rad", "cap", "lat"),
        P(),
        P("rad", ("cap", "lat")),
        P(("cap", "lat")),
        P(("cap", "lat")),
    )
    out_specs = P(None, ("cap", "rad"), "lat")
    return jax.shard_map(
        per_device, mesh=mesh, in_specs=in_specs, out_specs=out_specs, check_vma=False
    )
```

```python
import functools

import jax
import jax.numpy as jnp
from jax import lax
from jax.experimental import pallas as pl
from jax.experimental.pallas import tpu as pltpu
from jax.sharding import PartitionSpec as P

PICARD = 3
GHOST = 3

relax_coef = 0.25
advect_coef = 0.1


def _inside_mask(rows, cols, ext_rows, ext_cols, c, d, n_cap, n_lat):
    g = GHOST
    far = -(1 << 20)
    i = jnp.arange(ext_rows, dtype=jnp.int32)
    j = jnp.arange(ext_cols, dtype=jnp.int32)
    local_r = jnp.where(i < rows + g, i, jnp.where(i >= ext_rows - g, i - ext_rows, far))
    local_c = jnp.where(j < cols + g, j, jnp.where(j >= ext_cols - g, j - ext_cols, far))
    glob_r = c * rows + local_r
    glob_c = d * cols + local_c
    ok_r = (local_r > far) & (glob_r >= 0) & (glob_r < n_cap * rows)
    ok_c = (local_c > far) & (glob_c >= 0) & (glob_c < n_lat * cols)
    return (ok_r[:, None] & ok_c[None, :]).astype(jnp.float32)


def _pairs(n, step):
    return [(i, i + step) for i in range(n) if 0 <= i + step < n]


def _sweep_kernel(rad_ref, lam_ref, eta_ref, rowh_ref, colh_ref, mask_ref, vel_ref, dep_ref,
                  after_ref, recv_ref, send_ref, keep_ref, lam_x, eta_x):
    layers, rows, cols = lam_ref.shape
    n_r, n_c = lam_x.shape[1], lam_x.shape[2]
    for ref, src, k in ((lam_x, lam_ref, 0), (eta_x, eta_ref, 1)):
        ref[:, :rows, :cols] = src[...]
        ref[:, rows:, :cols] = rowh_ref[k]
        ref[:, :, cols:] = colh_ref[k]
    lam = lam_x[...]
    eta = eta_x[...]
    m = mask_ref[...][None]

    def up(x):
        return pltpu.roll(x, n_r - 1, 1)

    def dn(x):
        return pltpu.roll(x, 1, 1)

    def rt(x):
        return pltpu.roll(x, n_c - 1, 2)

    def lf(x):
        return pltpu.roll(x, 1, 2)

    ca_raw = 0.5 * (eta + up(eta))
    cb_raw = 0.5 * (eta + rt(eta))
    mq = relax_coef * m
    ca = ca_raw * mq
    cd = dn(ca_raw) * mq
    cb = cb_raw * mq
    cl = lf(cb_raw) * mq
    w = lam
    for _ in range(PICARD - 1):
        total = ca * (up(w) - w)
        total = total + cd * (dn(w) - w)
        total = total + cb * (rt(w) - w)
        total = total + cl * (lf(w) - w)
        w = lam + total

    def main(x):
        return x[:, :rows, :cols]

    wm = main(w)
    total = main(ca) * (main(up(w)) - wm)
    total = total + main(cd) * (main(dn(w)) - wm)
    total = total + main(cb) * (main(rt(w)) - wm)
    total = total + main(cl) * (main(lf(w)) - wm)
    w3 = main(lam) + total
    v0 = vel_ref[0].astype(jnp.float32)
    v1 = vel_ref[1].astype(jnp.float32)
    adv = v0 * main(up(lam) - dn(lam)) + v1 * main(rt(lam) - lf(lam))
    rhs = w3 + advect_coef * adv + dep_ref[...]
    half = rows // 2
    lo = rhs[:, :half, :]
    hi = rhs[:, half:, :]
    is_zero = rad_ref[0] == 0
    send_ref[...] = jnp.where(is_zero, hi, lo)
    keep_ref[...] = jnp.where(is_zero, lo, hi)


def _sweeps(rad_idx, lam, eta, rowh, colh, mask, vel, dep, after, recv, first_layer, n_layers,
            block_layers):
    _, rows, cols = lam.shape
    ext_r, ext_c = mask.shape
    half = rows // 2
    off = first_layer // block_layers
    bl = block_layers
    grid = (n_layers // bl,)
    out_shape = [jax.ShapeDtypeStruct((n_layers, half, cols), jnp.float32)] * 2
    return pl.pallas_call(
        _sweep_kernel,
        out_shape=out_shape,
        grid=grid,
        in_specs=[
            pl.BlockSpec(memory_space=pltpu.SMEM),
            pl.BlockSpec((bl, rows, cols), lambda i: (i + off, 0, 0)),
            pl.BlockSpec((bl, rows, cols), lambda i: (i + off, 0, 0)),
            pl.BlockSpec((2, bl, ext_r - rows, cols), lambda i: (0, i + off, 0, 0)),
            pl.BlockSpec((2, bl, ext_r, ext_c - cols), lambda i: (0, i + off, 0, 0)),
            pl.BlockSpec((ext_r, ext_c), lambda i: (0, 0)),
            pl.BlockSpec((2, bl, rows, cols), lambda i: (0, i + off, 0, 0)),
            pl.BlockSpec((bl, rows, cols), lambda i: (i + off, 0, 0)),
            pl.BlockSpec(memory_space=pl.ANY),
            pl.BlockSpec(memory_space=pl.ANY),
        ],
        out_specs=[
            pl.BlockSpec((bl, half, cols), lambda i: (i, 0, 0)),
            pl.BlockSpec((bl, half, cols), lambda i: (i, 0, 0)),
        ],
        scratch_shapes=[
            pltpu.VMEM((bl, ext_r, ext_c), jnp.float32),
            pltpu.VMEM((bl, ext_r, ext_c), jnp.float32),
        ],
        cost_estimate=pl.CostEstimate(
            flops=n_layers * ext_r * ext_c * 6000,
            transcendentals=0,
            bytes_accessed=n_layers * 1_600_000,
        ),
    )(rad_idx, lam, eta, rowh, colh, mask, vel, dep, after, recv)


def per_device(
    adjoint_temp,
    velocity,
    visc_flow,
    visc_yield,
    yield_mask,
    radial_inverse,
    marker_rows,
    recv_cells,
    recv_counts,
):
    layers, rows, cols = adjoint_temp.shape
    n_cap = lax.axis_size("cap")
    n_lat = lax.axis_size("lat")
    n_rad = lax.axis_size("rad")
    c = lax.axis_index("cap")
    d = lax.axis_index("lat")
    r = lax.axis_index("rad")

    def eta_of(sl):
        flow = visc_flow[:, sl].astype(jnp.float32)
        plast = visc_yield[:, sl].astype(jnp.float32)
        return jnp.where(yield_mask[:, sl] == 1, flow * plast / (flow + plast), flow)

    eta = eta_of(slice(None))

    g = GHOST
    ext_rows = ((rows + 2 * g + 7) // 8) * 8
    ext_cols = ((cols + 2 * g + 127) // 128) * 128
    top_send = jnp.concatenate([adjoint_temp[:, rows - g:], eta_of(slice(rows - g, rows))], axis=1)
    bot_send = jnp.concatenate([adjoint_temp[:, :g], eta_of(slice(0, g))], axis=1)
    top = lax.ppermute(top_send, "cap", _pairs(n_cap, 1))
    bot = lax.ppermute(bot_send, "cap", _pairs(n_cap, -1))
    zr = jnp.zeros((layers, ext_rows - rows - 2 * g, cols), jnp.float32)
    rowh = jnp.stack([
        jnp.concatenate([bot[:, :g], zr, top[:, :g]], axis=1),
        jnp.concatenate([bot[:, g:], zr, top[:, g:]], axis=1),
    ])

    def col_piece(sl):
        parts = []
        for k, src in enumerate((adjoint_temp, eta)):
            parts.append(jnp.concatenate([src[:, :, sl], rowh[k][:, :, sl]], axis=1))
        return jnp.stack(parts)

    flat = jnp.stack([col_piece(slice(0, g)), col_piece(slice(cols - g, cols))]).reshape(-1)
    piece = flat.shape[0] // 2
    flat, markers = lax.optimization_barrier((flat, marker_rows))
    received = lax.all_to_all(markers, "lat", split_axis=1, concat_axis=1, tiled=True)
    from_right = lax.ppermute(flat[:piece], "lat", _pairs(n_lat, -1))
    from_left = lax.ppermute(flat[piece:], "lat", _pairs(n_lat, 1))
    got = jnp.concatenate([from_right, from_left]).reshape(2, 2, layers, ext_rows, g)
    zc = jnp.zeros((2, layers, ext_rows, ext_cols - cols - 2 * g), jnp.float32)
    colh = jnp.concatenate([got[0], zc, got[1]], axis=3)
    mask = _inside_mask(rows, cols, ext_rows, ext_cols, c, d, n_cap, n_lat)

    senders = n_lat
    slot_total = received.shape[1]
    per_sender = slot_total // senders
    live = (jnp.arange(per_sender, dtype=jnp.int32)[None, :] < recv_counts[:, None]).reshape(-1)
    cell_a = recv_cells // cols
    cell_b = recv_cells % cols
    hit_a = (cell_a[None, :] == jnp.arange(rows, dtype=jnp.int32)[:, None]) & live[None, :]
    xa = jnp.where(hit_a[None], received[:, None, :], jnp.zeros((), received.dtype))
    onehot_b = (cell_b[:, None] == jnp.arange(cols, dtype=jnp.int32)[None, :]).astype(received.dtype)
    deposit = jnp.einsum("las,sb->lab", xa, onehot_b, preferred_element_type=jnp.float32)

    rad_idx = r.astype(jnp.int32).reshape(1)
    n_chunks = 4
    chunk = layers // n_chunks
    block_layers = 4
    keeps = []
    recvs = []
    after = rad_idx
    for k in range(n_chunks):
        landed = recvs[k - 2] if k >= 2 else rad_idx
        send, keep = _sweeps(
            rad_idx, adjoint_temp, eta, rowh, colh, mask, velocity, deposit, after, landed,
            k * chunk, chunk, block_layers,
        )
        after = keep
        recvs.append(lax.ppermute(send, "rad", _pairs(n_rad, 1) + _pairs(n_rad, -1)))
        keeps.append(keep)

    my_cols = lax.dynamic_slice_in_dim(radial_inverse, r * layers, layers, axis=1)
    peer_cols = lax.dynamic_slice_in_dim(radial_inverse, (1 - r) * layers, layers, axis=1)
    r_perm = jnp.concatenate([my_cols, peer_cols], axis=1)
    pieces = keeps + recvs
    split = len(pieces) - 2
    step = pieces[0].shape[0]
    partial = _radial(r_perm[:, :split * step], pieces[:split], after=recvs[-2])
    return _radial(r_perm[:, split * step:], pieces[split:], partial=partial)


def _radial_kernel(n_pieces, has_partial, r_ref, *refs):
    pieces = refs[:n_pieces]
    rest = refs[n_pieces:]
    partial_ref = rest[0] if has_partial else None
    out_ref, xs = rest[-2], rest[-1]
    step = pieces[0].shape[0]
    for i, p in enumerate(pieces):
        xs[i * step:(i + 1) * step] = p[...]
    rmat = r_ref[...]
    for a in range(xs.shape[1]):
        y = jnp.dot(rmat, xs[:, a, :], precision=lax.Precision.HIGHEST,
                    preferred_element_type=jnp.float32)
        if has_partial:
            y = partial_ref[:, a, :] + y
        out_ref[:, a, :] = y


def _radial(r_cols, pieces, partial=None, after=None):
    n_k, n_l = r_cols.shape
    _, n_a, n_b = pieces[0].shape
    extra = [] if partial is None else [partial]
    fake = [] if after is None else [after]
    in_specs = [pl.BlockSpec(memory_space=pltpu.VMEM)] * (1 + len(pieces) + len(extra))
    in_specs += [pl.BlockSpec(memory_space=pl.ANY)] * len(fake)
    return pl.pallas_call(
        functools.partial(_radial_kernel, len(pieces), partial is not None),
        out_shape=jax.ShapeDtypeStruct((n_k, n_a, n_b), jnp.float32),
        in_specs=in_specs,
        out_specs=pl.BlockSpec(memory_space=pltpu.VMEM),
        scratch_shapes=[pltpu.VMEM((n_l, n_a, n_b), jnp.float32)],
    )(r_cols, *pieces, *extra, *fake)


def solution(mesh):
    in_specs = (
        P("rad", "cap", "lat"),
        P(None, "rad", "cap", "lat"),
        P("rad", "cap", "lat"),
        P("rad", "cap", "lat"),
        P("rad", "cap", "lat"),
        P(),
        P("rad", ("cap", "lat")),
        P(("cap", "lat")),
        P(("cap", "lat")),
    )
    out_specs = P(None, ("cap", "rad"), "lat")
    return jax.shard_map(
        per_device, mesh=mesh, in_specs=in_specs, out_specs=out_specs, check_vma=False
    )
```

```python
import functools

import jax
import jax.numpy as jnp
from jax import lax
from jax.experimental import pallas as pl
from jax.experimental.pallas import tpu as pltpu
from jax.sharding import PartitionSpec as P

PICARD = 3
GHOST = 3

relax_coef = 0.25
advect_coef = 0.1


def _inside_mask(rows, cols, ext_rows, ext_cols, c, d, n_cap, n_lat):
    g = GHOST
    far = -(1 << 20)
    i = jnp.arange(ext_rows, dtype=jnp.int32)
    j = jnp.arange(ext_cols, dtype=jnp.int32)
    local_r = jnp.where(i < rows + g, i, jnp.where(i >= ext_rows - g, i - ext_rows, far))
    local_c = jnp.where(j < cols + g, j, jnp.where(j >= ext_cols - g, j - ext_cols, far))
    glob_r = c * rows + local_r
    glob_c = d * cols + local_c
    ok_r = (local_r > far) & (glob_r >= 0) & (glob_r < n_cap * rows)
    ok_c = (local_c > far) & (glob_c >= 0) & (glob_c < n_lat * cols)
    return (ok_r[:, None] & ok_c[None, :]).astype(jnp.float32)


def _pairs(n, step):
    return [(i, i + step) for i in range(n) if 0 <= i + step < n]


def _sweep_kernel(rad_ref, lam_ref, eta_ref, rowh_ref, colh_ref, mask_ref, vel_ref, dep_ref,
                  after_ref, recv_ref, send_ref, keep_ref, lam_x, eta_x):
    layers, rows, cols = lam_ref.shape
    n_r, n_c = lam_x.shape[1], lam_x.shape[2]
    for ref, src, k in ((lam_x, lam_ref, 0), (eta_x, eta_ref, 1)):
        ref[:, :rows, :cols] = src[...]
        ref[:, rows:, :cols] = rowh_ref[k]
        ref[:, :, cols:] = colh_ref[k]
    lam = lam_x[...]
    eta = eta_x[...]
    m = mask_ref[...][None]

    def up(x):
        return pltpu.roll(x, n_r - 1, 1)

    def dn(x):
        return pltpu.roll(x, 1, 1)

    def rt(x):
        return pltpu.roll(x, n_c - 1, 2)

    def lf(x):
        return pltpu.roll(x, 1, 2)

    ca_raw = 0.5 * (eta + up(eta))
    cb_raw = 0.5 * (eta + rt(eta))
    mq = relax_coef * m
    ca = ca_raw * mq
    cd = dn(ca_raw) * mq
    cb = cb_raw * mq
    cl = lf(cb_raw) * mq
    csum = (ca + cd) + (cb + cl)
    w = lam
    for _ in range(PICARD - 1):
        near = (ca * up(w) + cd * dn(w)) + (cb * rt(w) + cl * lf(w))
        w = lam + (near - csum * w)

    def main(x):
        return x[:, :rows, :cols]

    near = (main(ca) * main(up(w)) + main(cd) * main(dn(w))) + (
        main(cb) * main(rt(w)) + main(cl) * main(lf(w)))
    w3 = main(lam) + (near - main(csum) * main(w))
    v0 = vel_ref[0].astype(jnp.float32)
    v1 = vel_ref[1].astype(jnp.float32)
    adv = v0 * main(up(lam) - dn(lam)) + v1 * main(rt(lam) - lf(lam))
    rhs = w3 + advect_coef * adv + dep_ref[...]
    half = rows // 2
    lo = rhs[:, :half, :]
    hi = rhs[:, half:, :]
    is_zero = rad_ref[0] == 0
    send_ref[...] = jnp.where(is_zero, hi, lo)
    keep_ref[...] = jnp.where(is_zero, lo, hi)


def _sweeps(rad_idx, lam, eta, rowh, colh, mask, vel, dep, after, recv, first_layer, n_layers,
            block_layers):
    _, rows, cols = lam.shape
    ext_r, ext_c = mask.shape
    half = rows // 2
    off = first_layer // block_layers
    bl = block_layers
    grid = (n_layers // bl,)
    out_shape = [jax.ShapeDtypeStruct((n_layers, half, cols), jnp.float32)] * 2
    return pl.pallas_call(
        _sweep_kernel,
        out_shape=out_shape,
        grid=grid,
        in_specs=[
            pl.BlockSpec(memory_space=pltpu.SMEM),
            pl.BlockSpec((bl, rows, cols), lambda i: (i + off, 0, 0)),
            pl.BlockSpec((bl, rows, cols), lambda i: (i + off, 0, 0)),
            pl.BlockSpec((2, bl, ext_r - rows, cols), lambda i: (0, i + off, 0, 0)),
            pl.BlockSpec((2, bl, ext_r, ext_c - cols), lambda i: (0, i + off, 0, 0)),
            pl.BlockSpec((ext_r, ext_c), lambda i: (0, 0)),
            pl.BlockSpec((2, bl, rows, cols), lambda i: (0, i + off, 0, 0)),
            pl.BlockSpec((bl, rows, cols), lambda i: (i + off, 0, 0)),
            pl.BlockSpec(memory_space=pl.ANY),
            pl.BlockSpec(memory_space=pl.ANY),
        ],
        out_specs=[
            pl.BlockSpec((bl, half, cols), lambda i: (i, 0, 0)),
            pl.BlockSpec((bl, half, cols), lambda i: (i, 0, 0)),
        ],
        scratch_shapes=[
            pltpu.VMEM((bl, ext_r, ext_c), jnp.float32),
            pltpu.VMEM((bl, ext_r, ext_c), jnp.float32),
        ],
        cost_estimate=pl.CostEstimate(
            flops=n_layers * ext_r * ext_c * 6000,
            transcendentals=0,
            bytes_accessed=n_layers * 1_600_000,
        ),
    )(rad_idx, lam, eta, rowh, colh, mask, vel, dep, after, recv)


def per_device(
    adjoint_temp,
    velocity,
    visc_flow,
    visc_yield,
    yield_mask,
    radial_inverse,
    marker_rows,
    recv_cells,
    recv_counts,
):
    layers, rows, cols = adjoint_temp.shape
    n_cap = lax.axis_size("cap")
    n_lat = lax.axis_size("lat")
    n_rad = lax.axis_size("rad")
    c = lax.axis_index("cap")
    d = lax.axis_index("lat")
    r = lax.axis_index("rad")

    flow = visc_flow.astype(jnp.float32)
    plast = visc_yield.astype(jnp.float32)
    eta = jnp.where(yield_mask == 1, flow * plast / (flow + plast), flow)

    g = GHOST
    ext_rows = ((rows + 2 * g + 7) // 8) * 8
    ext_cols = ((cols + 2 * g + 127) // 128) * 128
    top_send = jnp.concatenate([adjoint_temp[:, rows - g:], eta[:, rows - g:]], axis=1)
    bot_send = jnp.concatenate([adjoint_temp[:, :g], eta[:, :g]], axis=1)
    top = lax.ppermute(top_send, "cap", _pairs(n_cap, 1))
    bot = lax.ppermute(bot_send, "cap", _pairs(n_cap, -1))
    zr = jnp.zeros((layers, ext_rows - rows - 2 * g, cols), jnp.float32)
    rowh = jnp.stack([
        jnp.concatenate([bot[:, :g], zr, top[:, :g]], axis=1),
        jnp.concatenate([bot[:, g:], zr, top[:, g:]], axis=1),
    ])

    def col_piece(sl):
        parts = []
        for k, src in enumerate((adjoint_temp, eta)):
            parts.append(jnp.concatenate([src[:, :, sl], rowh[k][:, :, sl]], axis=1))
        return jnp.stack(parts)

    flat = jnp.stack([col_piece(slice(0, g)), col_piece(slice(cols - g, cols))]).reshape(-1)
    piece = flat.shape[0] // 2
    flat, markers = lax.optimization_barrier((flat, marker_rows))
    received = lax.all_to_all(markers, "lat", split_axis=1, concat_axis=1, tiled=True)
    from_right = lax.ppermute(flat[:piece], "lat", _pairs(n_lat, -1))
    from_left = lax.ppermute(flat[piece:], "lat", _pairs(n_lat, 1))
    got = jnp.concatenate([from_right, from_left]).reshape(2, 2, layers, ext_rows, g)
    zc = jnp.zeros((2, layers, ext_rows, ext_cols - cols - 2 * g), jnp.float32)
    colh = jnp.concatenate([got[0], zc, got[1]], axis=3)
    mask = _inside_mask(rows, cols, ext_rows, ext_cols, c, d, n_cap, n_lat)

    senders = n_lat
    slot_total = received.shape[1]
    per_sender = slot_total // senders
    live = (jnp.arange(per_sender, dtype=jnp.int32)[None, :] < recv_counts[:, None]).reshape(-1)
    cell_a = recv_cells // cols
    cell_b = recv_cells % cols
    hit_a = (cell_a[None, :] == jnp.arange(rows, dtype=jnp.int32)[:, None]) & live[None, :]
    xa = jnp.where(hit_a[None], received[:, None, :], jnp.zeros((), received.dtype))
    onehot_b = (cell_b[:, None] == jnp.arange(cols, dtype=jnp.int32)[None, :]).astype(received.dtype)
    deposit = jnp.einsum("las,sb->lab", xa, onehot_b, preferred_element_type=jnp.float32)

    rad_idx = r.astype(jnp.int32).reshape(1)
    n_chunks = 4
    chunk = layers // n_chunks
    block_layers = 4
    keeps = []
    recvs = []
    after = rad_idx
    for k in range(n_chunks):
        landed = recvs[k - 2] if k >= 2 else rad_idx
        send, keep = _sweeps(
            rad_idx, adjoint_temp, eta, rowh, colh, mask, velocity, deposit, after, landed,
            k * chunk, chunk, block_layers,
        )
        after = keep
        recvs.append(lax.ppermute(send, "rad", _pairs(n_rad, 1) + _pairs(n_rad, -1)))
        keeps.append(keep)

    my_cols = lax.dynamic_slice_in_dim(radial_inverse, r * layers, layers, axis=1)
    peer_cols = lax.dynamic_slice_in_dim(radial_inverse, (1 - r) * layers, layers, axis=1)
    r_perm = jnp.concatenate([my_cols, peer_cols], axis=1)
    pieces = keeps + recvs
    split = len(pieces) - 2
    step = pieces[0].shape[0]
    partial = _radial(r_perm[:, :split * step], pieces[:split], after=recvs[-2])
    return _radial(r_perm[:, split * step:], pieces[split:], partial=partial)


def _radial_kernel(n_pieces, has_partial, r_ref, *refs):
    pieces = refs[:n_pieces]
    rest = refs[n_pieces:]
    partial_ref = rest[0] if has_partial else None
    out_ref, xs = rest[-2], rest[-1]
    step = pieces[0].shape[0]
    for i, p in enumerate(pieces):
        xs[i * step:(i + 1) * step] = p[...]
    rmat = r_ref[...]
    for a in range(xs.shape[1]):
        y = jnp.dot(rmat, xs[:, a, :], precision=lax.Precision.HIGHEST,
                    preferred_element_type=jnp.float32)
        if has_partial:
            y = partial_ref[:, a, :] + y
        out_ref[:, a, :] = y


def _radial(r_cols, pieces, partial=None, after=None):
    n_k, n_l = r_cols.shape
    _, n_a, n_b = pieces[0].shape
    extra = [] if partial is None else [partial]
    fake = [] if after is None else [after]
    in_specs = [pl.BlockSpec(memory_space=pltpu.VMEM)] * (1 + len(pieces) + len(extra))
    in_specs += [pl.BlockSpec(memory_space=pl.ANY)] * len(fake)
    return pl.pallas_call(
        functools.partial(_radial_kernel, len(pieces), partial is not None),
        out_shape=jax.ShapeDtypeStruct((n_k, n_a, n_b), jnp.float32),
        in_specs=in_specs,
        out_specs=pl.BlockSpec(memory_space=pltpu.VMEM),
        scratch_shapes=[pltpu.VMEM((n_l, n_a, n_b), jnp.float32)],
    )(r_cols, *pieces, *extra, *fake)


def solution(mesh):
    in_specs = (
        P("rad", "cap", "lat"),
        P(None, "rad", "cap", "lat"),
        P("rad", "cap", "lat"),
        P("rad", "cap", "lat"),
        P("rad", "cap", "lat"),
        P(),
        P("rad", ("cap", "lat")),
        P(("cap", "lat")),
        P(("cap", "lat")),
    )
    out_specs = P(None, ("cap", "rad"), "lat")
    return jax.shard_map(
        per_device, mesh=mesh, in_specs=in_specs, out_specs=out_specs, check_vma=False
    )
```

```python
import functools

import jax
import jax.numpy as jnp
from jax import lax
from jax.experimental import pallas as pl
from jax.experimental.pallas import tpu as pltpu
from jax.sharding import PartitionSpec as P

PICARD = 3
GHOST = 3

relax_coef = 0.25
advect_coef = 0.1


def _inside_mask(rows, cols, ext_rows, ext_cols, c, d, n_cap, n_lat):
    g = GHOST
    far = -(1 << 20)
    i = jnp.arange(ext_rows, dtype=jnp.int32)
    j = jnp.arange(ext_cols, dtype=jnp.int32)
    local_r = jnp.where(i < rows + g, i, jnp.where(i >= ext_rows - g, i - ext_rows, far))
    local_c = jnp.where(j < cols + g, j, jnp.where(j >= ext_cols - g, j - ext_cols, far))
    glob_r = c * rows + local_r
    glob_c = d * cols + local_c
    ok_r = (local_r > far) & (glob_r >= 0) & (glob_r < n_cap * rows)
    ok_c = (local_c > far) & (glob_c >= 0) & (glob_c < n_lat * cols)
    return (ok_r[:, None] & ok_c[None, :]).astype(jnp.float32)


def _pairs(n, step):
    return [(i, i + step) for i in range(n) if 0 <= i + step < n]


def _sweep_kernel(rad_ref, lam_ref, eta_ref, rowh_ref, colh_ref, mask_ref, vel_ref, dep_ref,
                  after_ref, recv_ref, send_ref, keep_ref, lam_x, eta_x):
    layers, rows, cols = lam_ref.shape
    n_r, n_c = lam_x.shape[1], lam_x.shape[2]
    for ref, src, k in ((lam_x, lam_ref, 0), (eta_x, eta_ref, 1)):
        ref[:, :rows, :cols] = src[...]
        ref[:, rows:, :cols] = rowh_ref[k]
        ref[:, :, cols:] = colh_ref[k]
    lam = lam_x[...]
    eta = eta_x[...]
    m = mask_ref[...][None]

    def up(x):
        return pltpu.roll(x, n_r - 1, 1)

    def dn(x):
        return pltpu.roll(x, 1, 1)

    def rt(x):
        return pltpu.roll(x, n_c - 1, 2)

    def lf(x):
        return pltpu.roll(x, 1, 2)

    ca_raw = 0.5 * (eta + up(eta))
    cb_raw = 0.5 * (eta + rt(eta))
    mq = relax_coef * m
    ca = ca_raw * mq
    cd = dn(ca_raw) * mq
    cb = cb_raw * mq
    cl = lf(cb_raw) * mq
    w = lam
    for _ in range(PICARD - 1):
        total = ca * (up(w) - w)
        total = total + cd * (dn(w) - w)
        total = total + cb * (rt(w) - w)
        total = total + cl * (lf(w) - w)
        w = lam + total

    def main(x):
        return x[:, :rows, :cols]

    wm = main(w)
    total = main(ca) * (main(up(w)) - wm)
    total = total + main(cd) * (main(dn(w)) - wm)
    total = total + main(cb) * (main(rt(w)) - wm)
    total = total + main(cl) * (main(lf(w)) - wm)
    w3 = main(lam) + total
    v0 = vel_ref[0].astype(jnp.float32)
    v1 = vel_ref[1].astype(jnp.float32)
    adv = v0 * main(up(lam) - dn(lam)) + v1 * main(rt(lam) - lf(lam))
    rhs = w3 + advect_coef * adv + dep_ref[...]
    half = rows // 2
    lo = rhs[:, :half, :]
    hi = rhs[:, half:, :]
    is_zero = rad_ref[0] == 0
    send_ref[...] = jnp.where(is_zero, hi, lo)
    keep_ref[...] = jnp.where(is_zero, lo, hi)


def _sweeps(rad_idx, lam, eta, rowh, colh, mask, vel, dep, after, recv, first_layer, n_layers,
            block_layers):
    _, rows, cols = lam.shape
    ext_r, ext_c = mask.shape
    half = rows // 2
    off = first_layer // block_layers
    bl = block_layers
    grid = (n_layers // bl,)
    out_shape = [jax.ShapeDtypeStruct((n_layers, half, cols), jnp.float32)] * 2
    return pl.pallas_call(
        _sweep_kernel,
        out_shape=out_shape,
        grid=grid,
        in_specs=[
            pl.BlockSpec(memory_space=pltpu.SMEM),
            pl.BlockSpec((bl, rows, cols), lambda i: (i + off, 0, 0)),
            pl.BlockSpec((bl, rows, cols), lambda i: (i + off, 0, 0)),
            pl.BlockSpec((2, bl, ext_r - rows, cols), lambda i: (0, i + off, 0, 0)),
            pl.BlockSpec((2, bl, ext_r, ext_c - cols), lambda i: (0, i + off, 0, 0)),
            pl.BlockSpec((ext_r, ext_c), lambda i: (0, 0)),
            pl.BlockSpec((2, bl, rows, cols), lambda i: (0, i + off, 0, 0)),
            pl.BlockSpec((bl, rows, cols), lambda i: (i + off, 0, 0)),
            pl.BlockSpec(memory_space=pl.ANY),
            pl.BlockSpec(memory_space=pl.ANY),
        ],
        out_specs=[
            pl.BlockSpec((bl, half, cols), lambda i: (i, 0, 0)),
            pl.BlockSpec((bl, half, cols), lambda i: (i, 0, 0)),
        ],
        scratch_shapes=[
            pltpu.VMEM((bl, ext_r, ext_c), jnp.float32),
            pltpu.VMEM((bl, ext_r, ext_c), jnp.float32),
        ],
        cost_estimate=pl.CostEstimate(
            flops=n_layers * ext_r * ext_c * 6000,
            transcendentals=0,
            bytes_accessed=n_layers * 1_600_000,
        ),
    )(rad_idx, lam, eta, rowh, colh, mask, vel, dep, after, recv)


def per_device(
    adjoint_temp,
    velocity,
    visc_flow,
    visc_yield,
    yield_mask,
    radial_inverse,
    marker_rows,
    recv_cells,
    recv_counts,
):
    layers, rows, cols = adjoint_temp.shape
    n_cap = lax.axis_size("cap")
    n_lat = lax.axis_size("lat")
    n_rad = lax.axis_size("rad")
    c = lax.axis_index("cap")
    d = lax.axis_index("lat")
    r = lax.axis_index("rad")

    flow = visc_flow.astype(jnp.float32)
    plast = visc_yield.astype(jnp.float32)
    eta = jnp.where(yield_mask == 1, flow * plast / (flow + plast), flow)

    g = GHOST
    ext_rows = ((rows + 2 * g + 7) // 8) * 8
    ext_cols = ((cols + 2 * g + 127) // 128) * 128
    top_send = jnp.concatenate([adjoint_temp[:, rows - g:], eta[:, rows - g:]], axis=1)
    bot_send = jnp.concatenate([adjoint_temp[:, :g], eta[:, :g]], axis=1)
    top = lax.ppermute(top_send, "cap", _pairs(n_cap, 1))
    bot = lax.ppermute(bot_send, "cap", _pairs(n_cap, -1))
    zr = jnp.zeros((layers, ext_rows - rows - 2 * g, cols), jnp.float32)
    rowh = jnp.stack([
        jnp.concatenate([bot[:, :g], zr, top[:, :g]], axis=1),
        jnp.concatenate([bot[:, g:], zr, top[:, g:]], axis=1),
    ])

    def col_piece(sl):
        parts = []
        for k, src in enumerate((adjoint_temp, eta)):
            parts.append(jnp.concatenate([src[:, :, sl], rowh[k][:, :, sl]], axis=1))
        return jnp.stack(parts)

    flat = jnp.stack([col_piece(slice(0, g)), col_piece(slice(cols - g, cols))]).reshape(-1)
    piece = flat.shape[0] // 2
    flat, markers = lax.optimization_barrier((flat, marker_rows))
    received = lax.all_to_all(markers, "lat", split_axis=1, concat_axis=1, tiled=True)
    from_right = lax.ppermute(flat[:piece], "lat", _pairs(n_lat, -1))
    from_left = lax.ppermute(flat[piece:], "lat", _pairs(n_lat, 1))
    got = jnp.concatenate([from_right, from_left]).reshape(2, 2, layers, ext_rows, g)
    zc = jnp.zeros((2, layers, ext_rows, ext_cols - cols - 2 * g), jnp.float32)
    colh = jnp.concatenate([got[0], zc, got[1]], axis=3)
    mask = _inside_mask(rows, cols, ext_rows, ext_cols, c, d, n_cap, n_lat)

    senders = n_lat
    slot_total = received.shape[1]
    per_sender = slot_total // senders
    live = (jnp.arange(per_sender, dtype=jnp.int32)[None, :] < recv_counts[:, None]).reshape(-1)
    cell_a = recv_cells // cols
    cell_b = recv_cells % cols
    hit_a = (cell_a[None, :] == jnp.arange(rows, dtype=jnp.int32)[:, None]) & live[None, :]
    xa = jnp.where(hit_a[None], received[:, None, :], jnp.zeros((), received.dtype))
    onehot_b = (cell_b[:, None] == jnp.arange(cols, dtype=jnp.int32)[None, :]).astype(received.dtype)
    deposit = jnp.einsum("las,sb->lab", xa, onehot_b, preferred_element_type=jnp.float32)

    rad_idx = r.astype(jnp.int32).reshape(1)
    n_chunks = 4
    chunk = layers // n_chunks
    block_layers = 2
    keeps = []
    recvs = []
    after = rad_idx
    for k in range(n_chunks):
        landed = recvs[k - 2] if k >= 2 else rad_idx
        send, keep = _sweeps(
            rad_idx, adjoint_temp, eta, rowh, colh, mask, velocity, deposit, after, landed,
            k * chunk, chunk, block_layers,
        )
        after = keep
        recvs.append(lax.ppermute(send, "rad", _pairs(n_rad, 1) + _pairs(n_rad, -1)))
        keeps.append(keep)

    my_cols = lax.dynamic_slice_in_dim(radial_inverse, r * layers, layers, axis=1)
    peer_cols = lax.dynamic_slice_in_dim(radial_inverse, (1 - r) * layers, layers, axis=1)
    r_perm = jnp.concatenate([my_cols, peer_cols], axis=1)
    pieces = keeps + recvs
    split = len(pieces) - 2
    step = pieces[0].shape[0]
    partial = _radial(r_perm[:, :split * step], pieces[:split], after=recvs[-2])
    return _radial(r_perm[:, split * step:], pieces[split:], partial=partial)


def _radial_kernel(n_pieces, has_partial, r_ref, *refs):
    pieces = refs[:n_pieces]
    rest = refs[n_pieces:]
    partial_ref = rest[0] if has_partial else None
    out_ref, xs = rest[-2], rest[-1]
    step = pieces[0].shape[0]
    for i, p in enumerate(pieces):
        xs[i * step:(i + 1) * step] = p[...]
    rmat = r_ref[...]
    for a in range(xs.shape[1]):
        y = jnp.dot(rmat, xs[:, a, :], precision=lax.Precision.HIGHEST,
                    preferred_element_type=jnp.float32)
        if has_partial:
            y = partial_ref[:, a, :] + y
        out_ref[:, a, :] = y


def _radial(r_cols, pieces, partial=None, after=None):
    n_k, n_l = r_cols.shape
    _, n_a, n_b = pieces[0].shape
    extra = [] if partial is None else [partial]
    fake = [] if after is None else [after]
    in_specs = [pl.BlockSpec(memory_space=pltpu.VMEM)] * (1 + len(pieces) + len(extra))
    in_specs += [pl.BlockSpec(memory_space=pl.ANY)] * len(fake)
    return pl.pallas_call(
        functools.partial(_radial_kernel, len(pieces), partial is not None),
        out_shape=jax.ShapeDtypeStruct((n_k, n_a, n_b), jnp.float32),
        in_specs=in_specs,
        out_specs=pl.BlockSpec(memory_space=pltpu.VMEM),
        scratch_shapes=[pltpu.VMEM((n_l, n_a, n_b), jnp.float32)],
    )(r_cols, *pieces, *extra, *fake)


def solution(mesh):
    in_specs = (
        P("rad", "cap", "lat"),
        P(None, "rad", "cap", "lat"),
        P("rad", "cap", "lat"),
        P("rad", "cap", "lat"),
        P("rad", "cap", "lat"),
        P(),
        P("rad", ("cap", "lat")),
        P(("cap", "lat")),
        P(("cap", "lat")),
    )
    out_specs = P(None, ("cap", "rad"), "lat")
    return jax.shard_map(
        per_device, mesh=mesh, in_specs=in_specs, out_specs=out_specs, check_vma=False
    )
```

```python
import functools

import jax
import jax.numpy as jnp
from jax import lax
from jax.experimental import pallas as pl
from jax.experimental.pallas import tpu as pltpu
from jax.sharding import PartitionSpec as P

PICARD = 3
GHOST = 3

relax_coef = 0.25
advect_coef = 0.1


def _inside_mask(rows, cols, ext_rows, ext_cols, c, d, n_cap, n_lat):
    g = GHOST
    far = -(1 << 20)
    i = jnp.arange(ext_rows, dtype=jnp.int32)
    j = jnp.arange(ext_cols, dtype=jnp.int32)
    local_r = jnp.where(i < rows + g, i, jnp.where(i >= ext_rows - g, i - ext_rows, far))
    local_c = jnp.where(j < cols + g, j, jnp.where(j >= ext_cols - g, j - ext_cols, far))
    glob_r = c * rows + local_r
    glob_c = d * cols + local_c
    ok_r = (local_r > far) & (glob_r >= 0) & (glob_r < n_cap * rows)
    ok_c = (local_c > far) & (glob_c >= 0) & (glob_c < n_lat * cols)
    return (ok_r[:, None] & ok_c[None, :]).astype(jnp.float32)


def _pairs(n, step):
    return [(i, i + step) for i in range(n) if 0 <= i + step < n]


def _sweep_kernel(rad_ref, lam_ref, eta_ref, rowh_ref, colh_ref, mask_ref, vel_ref, dep_ref,
                  after_ref, recv_ref, send_ref, keep_ref, lam_x, eta_x):
    layers, rows, cols = lam_ref.shape
    n_r, n_c = lam_x.shape[1], lam_x.shape[2]
    for ref, src, k in ((lam_x, lam_ref, 0), (eta_x, eta_ref, 1)):
        ref[:, :rows, :cols] = src[...]
        ref[:, rows:, :cols] = rowh_ref[k]
        ref[:, :, cols:] = colh_ref[k]
    lam = lam_x[...]
    eta = eta_x[...]
    m = mask_ref[...][None]

    def up(x):
        return pltpu.roll(x, n_r - 1, 1)

    def dn(x):
        return pltpu.roll(x, 1, 1)

    def rt(x):
        return pltpu.roll(x, n_c - 1, 2)

    def lf(x):
        return pltpu.roll(x, 1, 2)

    ca_raw = 0.5 * (eta + up(eta))
    cb_raw = 0.5 * (eta + rt(eta))
    mq = relax_coef * m
    ca = ca_raw * mq
    cd = dn(ca_raw) * mq
    cb = cb_raw * mq
    cl = lf(cb_raw) * mq
    w = lam
    for _ in range(PICARD - 1):
        total = ca * (up(w) - w)
        total = total + cd * (dn(w) - w)
        total = total + cb * (rt(w) - w)
        total = total + cl * (lf(w) - w)
        w = lam + total

    def main(x):
        return x[:, :rows, :cols]

    wm = main(w)
    total = main(ca) * (main(up(w)) - wm)
    total = total + main(cd) * (main(dn(w)) - wm)
    total = total + main(cb) * (main(rt(w)) - wm)
    total = total + main(cl) * (main(lf(w)) - wm)
    w3 = main(lam) + total
    v0 = vel_ref[0].astype(jnp.float32)
    v1 = vel_ref[1].astype(jnp.float32)
    adv = v0 * main(up(lam) - dn(lam)) + v1 * main(rt(lam) - lf(lam))
    rhs = w3 + advect_coef * adv + dep_ref[...]
    half = rows // 2
    lo = rhs[:, :half, :]
    hi = rhs[:, half:, :]
    is_zero = rad_ref[0] == 0
    send_ref[...] = jnp.where(is_zero, hi, lo)
    keep_ref[...] = jnp.where(is_zero, lo, hi)


def _sweeps(rad_idx, lam, eta, rowh, colh, mask, vel, dep, after, recv, first_layer, n_layers,
            block_layers):
    _, rows, cols = lam.shape
    ext_r, ext_c = mask.shape
    half = rows // 2
    off = first_layer // block_layers
    bl = block_layers
    grid = (n_layers // bl,)
    out_shape = [jax.ShapeDtypeStruct((n_layers, half, cols), jnp.float32)] * 2
    return pl.pallas_call(
        _sweep_kernel,
        out_shape=out_shape,
        grid=grid,
        in_specs=[
            pl.BlockSpec(memory_space=pltpu.SMEM),
            pl.BlockSpec((bl, rows, cols), lambda i: (i + off, 0, 0)),
            pl.BlockSpec((bl, rows, cols), lambda i: (i + off, 0, 0)),
            pl.BlockSpec((2, bl, ext_r - rows, cols), lambda i: (0, i + off, 0, 0)),
            pl.BlockSpec((2, bl, ext_r, ext_c - cols), lambda i: (0, i + off, 0, 0)),
            pl.BlockSpec((ext_r, ext_c), lambda i: (0, 0)),
            pl.BlockSpec((2, bl, rows, cols), lambda i: (0, i + off, 0, 0)),
            pl.BlockSpec((bl, rows, cols), lambda i: (i + off, 0, 0)),
            pl.BlockSpec(memory_space=pl.ANY),
            pl.BlockSpec(memory_space=pl.ANY),
        ],
        out_specs=[
            pl.BlockSpec((bl, half, cols), lambda i: (i, 0, 0)),
            pl.BlockSpec((bl, half, cols), lambda i: (i, 0, 0)),
        ],
        scratch_shapes=[
            pltpu.VMEM((bl, ext_r, ext_c), jnp.float32),
            pltpu.VMEM((bl, ext_r, ext_c), jnp.float32),
        ],
        cost_estimate=pl.CostEstimate(
            flops=n_layers * ext_r * ext_c * 6000,
            transcendentals=0,
            bytes_accessed=n_layers * 1_600_000,
        ),
    )(rad_idx, lam, eta, rowh, colh, mask, vel, dep, after, recv)


def per_device(
    adjoint_temp,
    velocity,
    visc_flow,
    visc_yield,
    yield_mask,
    radial_inverse,
    marker_rows,
    recv_cells,
    recv_counts,
):
    layers, rows, cols = adjoint_temp.shape
    n_cap = lax.axis_size("cap")
    n_lat = lax.axis_size("lat")
    n_rad = lax.axis_size("rad")
    c = lax.axis_index("cap")
    d = lax.axis_index("lat")
    r = lax.axis_index("rad")

    flow = visc_flow.astype(jnp.float32)
    plast = visc_yield.astype(jnp.float32)
    eta = jnp.where(yield_mask == 1, flow * plast / (flow + plast), flow)

    g = GHOST
    ext_rows = ((rows + 2 * g + 7) // 8) * 8
    ext_cols = ((cols + 2 * g + 127) // 128) * 128
    top_send = jnp.concatenate([adjoint_temp[:, rows - g:], eta[:, rows - g:]], axis=1)
    bot_send = jnp.concatenate([adjoint_temp[:, :g], eta[:, :g]], axis=1)
    top = lax.ppermute(top_send, "cap", _pairs(n_cap, 1))
    bot = lax.ppermute(bot_send, "cap", _pairs(n_cap, -1))
    zr = jnp.zeros((layers, ext_rows - rows - 2 * g, cols), jnp.float32)
    rowh = jnp.stack([
        jnp.concatenate([bot[:, :g], zr, top[:, :g]], axis=1),
        jnp.concatenate([bot[:, g:], zr, top[:, g:]], axis=1),
    ])

    def col_piece(sl):
        parts = []
        for k, src in enumerate((adjoint_temp, eta)):
            parts.append(jnp.concatenate([src[:, :, sl], rowh[k][:, :, sl]], axis=1))
        return jnp.stack(parts)

    flat = jnp.stack([col_piece(slice(0, g)), col_piece(slice(cols - g, cols))]).reshape(-1)
    piece = flat.shape[0] // 2
    flat, markers = lax.optimization_barrier((flat, marker_rows))
    received = lax.all_to_all(markers, "lat", split_axis=1, concat_axis=1, tiled=True)
    from_right = lax.ppermute(flat[:piece], "lat", _pairs(n_lat, -1))
    from_left = lax.ppermute(flat[piece:], "lat", _pairs(n_lat, 1))
    got = jnp.concatenate([from_right, from_left]).reshape(2, 2, layers, ext_rows, g)
    zc = jnp.zeros((2, layers, ext_rows, ext_cols - cols - 2 * g), jnp.float32)
    colh = jnp.concatenate([got[0], zc, got[1]], axis=3)
    mask = _inside_mask(rows, cols, ext_rows, ext_cols, c, d, n_cap, n_lat)

    senders = n_lat
    slot_total = received.shape[1]
    per_sender = slot_total // senders
    live = (jnp.arange(per_sender, dtype=jnp.int32)[None, :] < recv_counts[:, None]).reshape(-1)
    cell_a = recv_cells // cols
    cell_b = recv_cells % cols
    hit_a = (cell_a[None, :] == jnp.arange(rows, dtype=jnp.int32)[:, None]) & live[None, :]
    xa = jnp.where(hit_a[None], received[:, None, :], jnp.zeros((), received.dtype))
    onehot_b = (cell_b[:, None] == jnp.arange(cols, dtype=jnp.int32)[None, :]).astype(received.dtype)
    deposit = jnp.einsum("las,sb->lab", xa, onehot_b, preferred_element_type=jnp.float32)

    rad_idx = r.astype(jnp.int32).reshape(1)
    n_chunks = 4
    chunk = layers // n_chunks
    block_layers = 8
    keeps = []
    recvs = []
    after = rad_idx
    for k in range(n_chunks):
        landed = recvs[k - 2] if k >= 2 else rad_idx
        send, keep = _sweeps(
            rad_idx, adjoint_temp, eta, rowh, colh, mask, velocity, deposit, after, landed,
            k * chunk, chunk, block_layers,
        )
        after = keep
        recvs.append(lax.ppermute(send, "rad", _pairs(n_rad, 1) + _pairs(n_rad, -1)))
        keeps.append(keep)

    my_cols = lax.dynamic_slice_in_dim(radial_inverse, r * layers, layers, axis=1)
    peer_cols = lax.dynamic_slice_in_dim(radial_inverse, (1 - r) * layers, layers, axis=1)
    r_perm = jnp.concatenate([my_cols, peer_cols], axis=1)
    pieces = keeps + recvs
    split = len(pieces) - 2
    step = pieces[0].shape[0]
    partial = _radial(r_perm[:, :split * step], pieces[:split], after=recvs[-2])
    return _radial(r_perm[:, split * step:], pieces[split:], partial=partial)


def _radial_kernel(n_pieces, has_partial, r_ref, *refs):
    pieces = refs[:n_pieces]
    rest = refs[n_pieces:]
    partial_ref = rest[0] if has_partial else None
    out_ref, xs = rest[-2], rest[-1]
    step = pieces[0].shape[0]
    for i, p in enumerate(pieces):
        xs[i * step:(i + 1) * step] = p[...]
    rmat = r_ref[...]
    for a in range(xs.shape[1]):
        y = jnp.dot(rmat, xs[:, a, :], precision=lax.Precision.HIGHEST,
                    preferred_element_type=jnp.float32)
        if has_partial:
            y = partial_ref[:, a, :] + y
        out_ref[:, a, :] = y


def _radial(r_cols, pieces, partial=None, after=None):
    n_k, n_l = r_cols.shape
    _, n_a, n_b = pieces[0].shape
    extra = [] if partial is None else [partial]
    fake = [] if after is None else [after]
    in_specs = [pl.BlockSpec(memory_space=pltpu.VMEM)] * (1 + len(pieces) + len(extra))
    in_specs += [pl.BlockSpec(memory_space=pl.ANY)] * len(fake)
    return pl.pallas_call(
        functools.partial(_radial_kernel, len(pieces), partial is not None),
        out_shape=jax.ShapeDtypeStruct((n_k, n_a, n_b), jnp.float32),
        in_specs=in_specs,
        out_specs=pl.BlockSpec(memory_space=pltpu.VMEM),
        scratch_shapes=[pltpu.VMEM((n_l, n_a, n_b), jnp.float32)],
    )(r_cols, *pieces, *extra, *fake)


def solution(mesh):
    in_specs = (
        P("rad", "cap", "lat"),
        P(None, "rad", "cap", "lat"),
        P("rad", "cap", "lat"),
        P("rad", "cap", "lat"),
        P("rad", "cap", "lat"),
        P(),
        P("rad", ("cap", "lat")),
        P(("cap", "lat")),
        P(("cap", "lat")),
    )
    out_specs = P(None, ("cap", "rad"), "lat")
    return jax.shard_map(
        per_device, mesh=mesh, in_specs=in_specs, out_specs=out_specs, check_vma=False
    )
```

```python
import functools

import jax
import jax.numpy as jnp
from jax import lax
from jax.experimental import pallas as pl
from jax.experimental.pallas import tpu as pltpu
from jax.sharding import PartitionSpec as P

PICARD = 3
GHOST = 3

relax_coef = 0.25
advect_coef = 0.1


def _inside_mask(rows, cols, ext_rows, ext_cols, c, d, n_cap, n_lat):
    g = GHOST
    far = -(1 << 20)
    i = jnp.arange(ext_rows, dtype=jnp.int32)
    j = jnp.arange(ext_cols, dtype=jnp.int32)
    local_r = jnp.where(i < rows + g, i, jnp.where(i >= ext_rows - g, i - ext_rows, far))
    local_c = jnp.where(j < cols + g, j, jnp.where(j >= ext_cols - g, j - ext_cols, far))
    glob_r = c * rows + local_r
    glob_c = d * cols + local_c
    ok_r = (local_r > far) & (glob_r >= 0) & (glob_r < n_cap * rows)
    ok_c = (local_c > far) & (glob_c >= 0) & (glob_c < n_lat * cols)
    return (ok_r[:, None] & ok_c[None, :]).astype(jnp.float32)


def _pairs(n, step):
    return [(i, i + step) for i in range(n) if 0 <= i + step < n]


def _sweep_kernel(rad_ref, lam_ref, eta_ref, rowh_ref, colh_ref, mask_ref, vel_ref, dep_ref,
                  after_ref, recv_ref, send_ref, keep_ref, lam_x, eta_x):
    layers, rows, cols = lam_ref.shape
    n_r, n_c = lam_x.shape[1], lam_x.shape[2]
    for ref, src, k in ((lam_x, lam_ref, 0), (eta_x, eta_ref, 1)):
        ref[:, :rows, :cols] = src[...]
        ref[:, rows:, :cols] = rowh_ref[k]
        ref[:, :, cols:] = colh_ref[k]
    lam = lam_x[...]
    eta = eta_x[...]
    m = mask_ref[...][None]

    def up(x):
        return pltpu.roll(x, n_r - 1, 1)

    def dn(x):
        return pltpu.roll(x, 1, 1)

    def rt(x):
        return pltpu.roll(x, n_c - 1, 2)

    def lf(x):
        return pltpu.roll(x, 1, 2)

    ca_raw = 0.5 * (eta + up(eta))
    cb_raw = 0.5 * (eta + rt(eta))
    mq = relax_coef * m
    ca = ca_raw * mq
    cd = dn(ca_raw) * mq
    cb = cb_raw * mq
    cl = lf(cb_raw) * mq
    w = lam
    for _ in range(PICARD - 1):
        total = ca * (up(w) - w)
        total = total + cd * (dn(w) - w)
        total = total + cb * (rt(w) - w)
        total = total + cl * (lf(w) - w)
        w = lam + total

    def main(x):
        return x[:, :rows, :cols]

    wm = main(w)
    total = main(ca) * (main(up(w)) - wm)
    total = total + main(cd) * (main(dn(w)) - wm)
    total = total + main(cb) * (main(rt(w)) - wm)
    total = total + main(cl) * (main(lf(w)) - wm)
    w3 = main(lam) + total
    v0 = vel_ref[0].astype(jnp.float32)
    v1 = vel_ref[1].astype(jnp.float32)
    adv = v0 * main(up(lam) - dn(lam)) + v1 * main(rt(lam) - lf(lam))
    rhs = w3 + advect_coef * adv + dep_ref[...]
    half = rows // 2
    lo = rhs[:, :half, :]
    hi = rhs[:, half:, :]
    is_zero = rad_ref[0] == 0
    send_ref[...] = jnp.where(is_zero, hi, lo)
    keep_ref[...] = jnp.where(is_zero, lo, hi)


def _sweeps(rad_idx, lam, eta, rowh, colh, mask, vel, dep, after, recv, first_layer, n_layers,
            block_layers):
    _, rows, cols = lam.shape
    ext_r, ext_c = mask.shape
    half = rows // 2
    off = first_layer // block_layers
    bl = block_layers
    grid = (n_layers // bl,)
    out_shape = [jax.ShapeDtypeStruct((n_layers, half, cols), jnp.float32)] * 2
    return pl.pallas_call(
        _sweep_kernel,
        out_shape=out_shape,
        grid=grid,
        in_specs=[
            pl.BlockSpec(memory_space=pltpu.SMEM),
            pl.BlockSpec((bl, rows, cols), lambda i: (i + off, 0, 0)),
            pl.BlockSpec((bl, rows, cols), lambda i: (i + off, 0, 0)),
            pl.BlockSpec((2, bl, ext_r - rows, cols), lambda i: (0, i + off, 0, 0)),
            pl.BlockSpec((2, bl, ext_r, ext_c - cols), lambda i: (0, i + off, 0, 0)),
            pl.BlockSpec((ext_r, ext_c), lambda i: (0, 0)),
            pl.BlockSpec((2, bl, rows, cols), lambda i: (0, i + off, 0, 0)),
            pl.BlockSpec((bl, rows, cols), lambda i: (i + off, 0, 0)),
            pl.BlockSpec(memory_space=pl.ANY),
            pl.BlockSpec(memory_space=pl.ANY),
        ],
        out_specs=[
            pl.BlockSpec((bl, half, cols), lambda i: (i, 0, 0)),
            pl.BlockSpec((bl, half, cols), lambda i: (i, 0, 0)),
        ],
        scratch_shapes=[
            pltpu.VMEM((bl, ext_r, ext_c), jnp.float32),
            pltpu.VMEM((bl, ext_r, ext_c), jnp.float32),
        ],
        cost_estimate=pl.CostEstimate(
            flops=n_layers * ext_r * ext_c * 6000,
            transcendentals=0,
            bytes_accessed=n_layers * 1_600_000,
        ),
    )(rad_idx, lam, eta, rowh, colh, mask, vel, dep, after, recv)


def per_device(
    adjoint_temp,
    velocity,
    visc_flow,
    visc_yield,
    yield_mask,
    radial_inverse,
    marker_rows,
    recv_cells,
    recv_counts,
):
    layers, rows, cols = adjoint_temp.shape
    n_cap = lax.axis_size("cap")
    n_lat = lax.axis_size("lat")
    n_rad = lax.axis_size("rad")
    c = lax.axis_index("cap")
    d = lax.axis_index("lat")
    r = lax.axis_index("rad")

    flow = visc_flow.astype(jnp.float32)
    plast = visc_yield.astype(jnp.float32)
    eta = jnp.where(yield_mask == 1, flow * plast / (flow + plast), flow)

    g = GHOST
    ext_rows = ((rows + 2 * g + 7) // 8) * 8
    ext_cols = ((cols + 2 * g + 127) // 128) * 128
    top_send = jnp.concatenate([adjoint_temp[:, rows - g:], eta[:, rows - g:]], axis=1)
    bot_send = jnp.concatenate([adjoint_temp[:, :g], eta[:, :g]], axis=1)
    top = lax.ppermute(top_send, "cap", _pairs(n_cap, 1))
    bot = lax.ppermute(bot_send, "cap", _pairs(n_cap, -1))
    zr = jnp.zeros((layers, ext_rows - rows - 2 * g, cols), jnp.float32)
    rowh = jnp.stack([
        jnp.concatenate([bot[:, :g], zr, top[:, :g]], axis=1),
        jnp.concatenate([bot[:, g:], zr, top[:, g:]], axis=1),
    ])

    def col_piece(sl):
        parts = []
        for k, src in enumerate((adjoint_temp, eta)):
            parts.append(jnp.concatenate([src[:, :, sl], rowh[k][:, :, sl]], axis=1))
        return jnp.stack(parts)

    flat = jnp.stack([col_piece(slice(0, g)), col_piece(slice(cols - g, cols))]).reshape(-1)
    piece = flat.shape[0] // 2
    flat, markers = lax.optimization_barrier((flat, marker_rows))
    received = lax.all_to_all(markers, "lat", split_axis=1, concat_axis=1, tiled=True)
    from_right = lax.ppermute(flat[:piece], "lat", _pairs(n_lat, -1))
    from_left = lax.ppermute(flat[piece:], "lat", _pairs(n_lat, 1))
    got = jnp.concatenate([from_right, from_left]).reshape(2, 2, layers, ext_rows, g)
    zc = jnp.zeros((2, layers, ext_rows, ext_cols - cols - 2 * g), jnp.float32)
    colh = jnp.concatenate([got[0], zc, got[1]], axis=3)
    mask = _inside_mask(rows, cols, ext_rows, ext_cols, c, d, n_cap, n_lat)

    senders = n_lat
    slot_total = received.shape[1]
    per_sender = slot_total // senders
    live = (jnp.arange(per_sender, dtype=jnp.int32)[None, :] < recv_counts[:, None]).reshape(-1)
    cell_a = recv_cells // cols
    cell_b = recv_cells % cols
    hit_a = (cell_a[None, :] == jnp.arange(rows, dtype=jnp.int32)[:, None]) & live[None, :]
    xa = jnp.where(hit_a[None], received[:, None, :], jnp.zeros((), received.dtype))
    onehot_b = (cell_b[:, None] == jnp.arange(cols, dtype=jnp.int32)[None, :]).astype(received.dtype)
    deposit = jnp.einsum("las,sb->lab", xa, onehot_b, preferred_element_type=jnp.float32)

    rad_idx = r.astype(jnp.int32).reshape(1)
    n_chunks = 4
    chunk = layers // n_chunks
    block_layers = 8
    keeps = []
    recvs = []
    after = rad_idx
    for k in range(n_chunks):
        landed = recvs[k - 2] if k >= 2 else rad_idx
        send, keep = _sweeps(
            rad_idx, adjoint_temp, eta, rowh, colh, mask, velocity, deposit, after, landed,
            k * chunk, chunk, block_layers,
        )
        after = keep
        recvs.append(lax.ppermute(send, "rad", _pairs(n_rad, 1) + _pairs(n_rad, -1)))
        keeps.append(keep)

    my_cols = lax.dynamic_slice_in_dim(radial_inverse, r * layers, layers, axis=1)
    peer_cols = lax.dynamic_slice_in_dim(radial_inverse, (1 - r) * layers, layers, axis=1)
    r_perm = jnp.concatenate([my_cols, peer_cols], axis=1)
    pieces = keeps + recvs
    split = len(pieces) - 2
    step = pieces[0].shape[0]
    partial = _radial(r_perm[:, :split * step], pieces[:split], after=recvs[-2])
    return _radial(r_perm[:, split * step:], pieces[split:], partial=partial)


def _radial_kernel(n_pieces, has_partial, r_ref, *refs):
    pieces = refs[:n_pieces]
    rest = refs[n_pieces:]
    partial_ref = rest[0] if has_partial else None
    out_ref, xs = rest[-2], rest[-1]
    step = pieces[0].shape[0]
    for i, p in enumerate(pieces):
        xs[i * step:(i + 1) * step] = p[...]
    n_l, n_a, n_b = xs.shape
    y = jnp.dot(r_ref[...], xs[...].reshape(n_l, n_a * n_b), precision=lax.Precision.HIGHEST,
                preferred_element_type=jnp.float32).reshape(out_ref.shape)
    if has_partial:
        y = partial_ref[...] + y
    out_ref[...] = y


def _radial(r_cols, pieces, partial=None, after=None):
    n_k, n_l = r_cols.shape
    _, n_a, n_b = pieces[0].shape
    extra = [] if partial is None else [partial]
    fake = [] if after is None else [after]
    in_specs = [pl.BlockSpec(memory_space=pltpu.VMEM)] * (1 + len(pieces) + len(extra))
    in_specs += [pl.BlockSpec(memory_space=pl.ANY)] * len(fake)
    return pl.pallas_call(
        functools.partial(_radial_kernel, len(pieces), partial is not None),
        out_shape=jax.ShapeDtypeStruct((n_k, n_a, n_b), jnp.float32),
        in_specs=in_specs,
        out_specs=pl.BlockSpec(memory_space=pltpu.VMEM),
        scratch_shapes=[pltpu.VMEM((n_l, n_a, n_b), jnp.float32)],
    )(r_cols, *pieces, *extra, *fake)


def solution(mesh):
    in_specs = (
        P("rad", "cap", "lat"),
        P(None, "rad", "cap", "lat"),
        P("rad", "cap", "lat"),
        P("rad", "cap", "lat"),
        P("rad", "cap", "lat"),
        P(),
        P("rad", ("cap", "lat")),
        P(("cap", "lat")),
        P(("cap", "lat")),
    )
    out_specs = P(None, ("cap", "rad"), "lat")
    return jax.shard_map(
        per_device, mesh=mesh, in_specs=in_specs, out_specs=out_specs, check_vma=False
    )
```

```python
import functools

import jax
import jax.numpy as jnp
from jax import lax
from jax.experimental import pallas as pl
from jax.experimental.pallas import tpu as pltpu
from jax.sharding import PartitionSpec as P

PICARD = 3
GHOST = 3

relax_coef = 0.25
advect_coef = 0.1


def _inside_mask(rows, cols, ext_rows, ext_cols, c, d, n_cap, n_lat):
    g = GHOST
    far = -(1 << 20)
    i = jnp.arange(ext_rows, dtype=jnp.int32)
    j = jnp.arange(ext_cols, dtype=jnp.int32)
    local_r = jnp.where(i < rows + g, i, jnp.where(i >= ext_rows - g, i - ext_rows, far))
    local_c = jnp.where(j < cols + g, j, jnp.where(j >= ext_cols - g, j - ext_cols, far))
    glob_r = c * rows + local_r
    glob_c = d * cols + local_c
    ok_r = (local_r > far) & (glob_r >= 0) & (glob_r < n_cap * rows)
    ok_c = (local_c > far) & (glob_c >= 0) & (glob_c < n_lat * cols)
    return (ok_r[:, None] & ok_c[None, :]).astype(jnp.float32)


def _pairs(n, step):
    return [(i, i + step) for i in range(n) if 0 <= i + step < n]


def _sweep_kernel(rad_ref, lam_ref, eta_ref, rowh_ref, colh_ref, mask_ref, vel_ref, dep_ref,
                  after_ref, recv_ref, send_ref, keep_ref, lam_x, eta_x):
    layers, rows, cols = lam_ref.shape
    n_r, n_c = lam_x.shape[1], lam_x.shape[2]
    for ref, src, k in ((lam_x, lam_ref, 0), (eta_x, eta_ref, 1)):
        ref[:, :rows, :cols] = src[...]
        ref[:, rows:, :cols] = rowh_ref[k]
        ref[:, :, cols:] = colh_ref[k]
    lam = lam_x[...]
    eta = eta_x[...]
    m = mask_ref[...][None]

    def up(x):
        return pltpu.roll(x, n_r - 1, 1)

    def dn(x):
        return pltpu.roll(x, 1, 1)

    def rt(x):
        return pltpu.roll(x, n_c - 1, 2)

    def lf(x):
        return pltpu.roll(x, 1, 2)

    ca_raw = 0.5 * (eta + up(eta))
    cb_raw = 0.5 * (eta + rt(eta))
    mq = relax_coef * m
    ca = ca_raw * mq
    cd = dn(ca_raw) * mq
    cb = cb_raw * mq
    cl = lf(cb_raw) * mq
    w = lam
    for _ in range(PICARD - 1):
        total = ca * (up(w) - w)
        total = total + cd * (dn(w) - w)
        total = total + cb * (rt(w) - w)
        total = total + cl * (lf(w) - w)
        w = lam + total

    def main(x):
        return x[:, :rows, :cols]

    wm = main(w)
    total = main(ca) * (main(up(w)) - wm)
    total = total + main(cd) * (main(dn(w)) - wm)
    total = total + main(cb) * (main(rt(w)) - wm)
    total = total + main(cl) * (main(lf(w)) - wm)
    w3 = main(lam) + total
    v0 = vel_ref[0].astype(jnp.float32)
    v1 = vel_ref[1].astype(jnp.float32)
    adv = v0 * main(up(lam) - dn(lam)) + v1 * main(rt(lam) - lf(lam))
    rhs = w3 + advect_coef * adv + dep_ref[...]
    half = rows // 2
    lo = rhs[:, :half, :]
    hi = rhs[:, half:, :]
    is_zero = rad_ref[0] == 0
    send_ref[...] = jnp.where(is_zero, hi, lo)
    keep_ref[...] = jnp.where(is_zero, lo, hi)


def _sweeps(rad_idx, lam, eta, rowh, colh, mask, vel, dep, after, recv, first_layer, n_layers,
            block_layers):
    _, rows, cols = lam.shape
    ext_r, ext_c = mask.shape
    half = rows // 2
    off = first_layer // block_layers
    bl = block_layers
    grid = (n_layers // bl,)
    out_shape = [jax.ShapeDtypeStruct((n_layers, half, cols), jnp.float32)] * 2
    return pl.pallas_call(
        _sweep_kernel,
        out_shape=out_shape,
        grid=grid,
        in_specs=[
            pl.BlockSpec(memory_space=pltpu.SMEM),
            pl.BlockSpec((bl, rows, cols), lambda i: (i + off, 0, 0)),
            pl.BlockSpec((bl, rows, cols), lambda i: (i + off, 0, 0)),
            pl.BlockSpec((2, bl, ext_r - rows, cols), lambda i: (0, i + off, 0, 0)),
            pl.BlockSpec((2, bl, ext_r, ext_c - cols), lambda i: (0, i + off, 0, 0)),
            pl.BlockSpec((ext_r, ext_c), lambda i: (0, 0)),
            pl.BlockSpec((2, bl, rows, cols), lambda i: (0, i + off, 0, 0)),
            pl.BlockSpec((bl, rows, cols), lambda i: (i + off, 0, 0)),
            pl.BlockSpec(memory_space=pl.ANY),
            pl.BlockSpec(memory_space=pl.ANY),
        ],
        out_specs=[
            pl.BlockSpec((bl, half, cols), lambda i: (i, 0, 0)),
            pl.BlockSpec((bl, half, cols), lambda i: (i, 0, 0)),
        ],
        scratch_shapes=[
            pltpu.VMEM((bl, ext_r, ext_c), jnp.float32),
            pltpu.VMEM((bl, ext_r, ext_c), jnp.float32),
        ],
        cost_estimate=pl.CostEstimate(
            flops=n_layers * ext_r * ext_c * 6000,
            transcendentals=0,
            bytes_accessed=n_layers * 1_600_000,
        ),
    )(rad_idx, lam, eta, rowh, colh, mask, vel, dep, after, recv)


def per_device(
    adjoint_temp,
    velocity,
    visc_flow,
    visc_yield,
    yield_mask,
    radial_inverse,
    marker_rows,
    recv_cells,
    recv_counts,
):
    layers, rows, cols = adjoint_temp.shape
    n_cap = lax.axis_size("cap")
    n_lat = lax.axis_size("lat")
    n_rad = lax.axis_size("rad")
    c = lax.axis_index("cap")
    d = lax.axis_index("lat")
    r = lax.axis_index("rad")

    flow = visc_flow.astype(jnp.float32)
    plast = visc_yield.astype(jnp.float32)
    eta = jnp.where(yield_mask == 1, flow * plast / (flow + plast), flow)

    g = GHOST
    ext_rows = ((rows + 2 * g + 7) // 8) * 8
    ext_cols = ((cols + 2 * g + 127) // 128) * 128
    top_send = jnp.concatenate([adjoint_temp[:, rows - g:], eta[:, rows - g:]], axis=1)
    bot_send = jnp.concatenate([adjoint_temp[:, :g], eta[:, :g]], axis=1)
    top = lax.ppermute(top_send, "cap", _pairs(n_cap, 1))
    bot = lax.ppermute(bot_send, "cap", _pairs(n_cap, -1))
    zr = jnp.zeros((layers, ext_rows - rows - 2 * g, cols), jnp.float32)
    rowh = jnp.stack([
        jnp.concatenate([bot[:, :g], zr, top[:, :g]], axis=1),
        jnp.concatenate([bot[:, g:], zr, top[:, g:]], axis=1),
    ])

    def col_piece(sl):
        parts = []
        for k, src in enumerate((adjoint_temp, eta)):
            parts.append(jnp.concatenate([src[:, :, sl], rowh[k][:, :, sl]], axis=1))
        return jnp.stack(parts)

    flat = jnp.stack([col_piece(slice(0, g)), col_piece(slice(cols - g, cols))]).reshape(-1)
    piece = flat.shape[0] // 2
    flat, markers = lax.optimization_barrier((flat, marker_rows))
    received = lax.all_to_all(markers, "lat", split_axis=1, concat_axis=1, tiled=True)
    from_right = lax.ppermute(flat[:piece], "lat", _pairs(n_lat, -1))
    from_left = lax.ppermute(flat[piece:], "lat", _pairs(n_lat, 1))
    got = jnp.concatenate([from_right, from_left]).reshape(2, 2, layers, ext_rows, g)
    zc = jnp.zeros((2, layers, ext_rows, ext_cols - cols - 2 * g), jnp.float32)
    colh = jnp.concatenate([got[0], zc, got[1]], axis=3)
    mask = _inside_mask(rows, cols, ext_rows, ext_cols, c, d, n_cap, n_lat)

    senders = n_lat
    slot_total = received.shape[1]
    per_sender = slot_total // senders
    live = (jnp.arange(per_sender, dtype=jnp.int32)[None, :] < recv_counts[:, None]).reshape(-1)
    cell_a = recv_cells // cols
    cell_b = recv_cells % cols
    hit_a = (cell_a[None, :] == jnp.arange(rows, dtype=jnp.int32)[:, None]) & live[None, :]
    xa = jnp.where(hit_a[None], received[:, None, :], jnp.zeros((), received.dtype))
    onehot_b = (cell_b[:, None] == jnp.arange(cols, dtype=jnp.int32)[None, :]).astype(received.dtype)
    deposit = jnp.einsum("las,sb->lab", xa, onehot_b, preferred_element_type=jnp.float32)

    rad_idx = r.astype(jnp.int32).reshape(1)
    n_chunks = 4
    chunk = layers // n_chunks
    block_layers = 8
    keeps = []
    recvs = []
    after = rad_idx
    for k in range(n_chunks):
        landed = recvs[k - 2] if k >= 2 else rad_idx
        send, keep = _sweeps(
            rad_idx, adjoint_temp, eta, rowh, colh, mask, velocity, deposit, after, landed,
            k * chunk, chunk, block_layers,
        )
        after = keep
        recvs.append(lax.ppermute(send, "rad", _pairs(n_rad, 1) + _pairs(n_rad, -1)))
        keeps.append(keep)

    my_cols = lax.dynamic_slice_in_dim(radial_inverse, r * layers, layers, axis=1)
    peer_cols = lax.dynamic_slice_in_dim(radial_inverse, (1 - r) * layers, layers, axis=1)
    r_perm = jnp.concatenate([my_cols, peer_cols], axis=1)
    pieces = keeps + recvs
    split = len(pieces) - 2
    step = pieces[0].shape[0]
    partial = _radial(r_perm[:, :split * step], pieces[:split], after=recvs[-2])
    return _radial(r_perm[:, split * step:], pieces[split:], partial=partial)


def _radial_kernel(n_pieces, has_partial, r_ref, *refs):
    pieces = refs[:n_pieces]
    rest = refs[n_pieces:]
    partial_ref = rest[0] if has_partial else None
    out_ref, xs = rest[-2], rest[-1]
    step = pieces[0].shape[0]
    for i, p in enumerate(pieces):
        xs[i * step:(i + 1) * step] = p[...]
    n_l, n_a, n_b = xs.shape
    y = jnp.dot(r_ref[...], xs[...].reshape(n_l, n_a * n_b), precision=lax.Precision.HIGHEST,
                preferred_element_type=jnp.float32).reshape(out_ref.shape)
    if has_partial:
        y = partial_ref[...] + y
    out_ref[...] = y


def _radial(r_cols, pieces, partial=None, after=None):
    n_k, n_l = r_cols.shape
    step, n_a, n_b = pieces[0].shape
    tile = 8
    extra = [] if partial is None else [partial]
    fake = [] if after is None else [after]
    in_specs = [pl.BlockSpec((n_k, n_l), lambda t: (0, 0))]
    in_specs += [pl.BlockSpec((step, tile, n_b), lambda t: (0, t, 0))] * len(pieces)
    in_specs += [pl.BlockSpec((n_k, tile, n_b), lambda t: (0, t, 0))] * len(extra)
    in_specs += [pl.BlockSpec(memory_space=pl.ANY)] * len(fake)
    return pl.pallas_call(
        functools.partial(_radial_kernel, len(pieces), partial is not None),
        out_shape=jax.ShapeDtypeStruct((n_k, n_a, n_b), jnp.float32),
        grid=(n_a // tile,),
        in_specs=in_specs,
        out_specs=pl.BlockSpec((n_k, tile, n_b), lambda t: (0, t, 0)),
        scratch_shapes=[pltpu.VMEM((n_l, tile, n_b), jnp.float32)],
    )(r_cols, *pieces, *extra, *fake)


def solution(mesh):
    in_specs = (
        P("rad", "cap", "lat"),
        P(None, "rad", "cap", "lat"),
        P("rad", "cap", "lat"),
        P("rad", "cap", "lat"),
        P("rad", "cap", "lat"),
        P(),
        P("rad", ("cap", "lat")),
        P(("cap", "lat")),
        P(("cap", "lat")),
    )
    out_specs = P(None, ("cap", "rad"), "lat")
    return jax.shard_map(
        per_device, mesh=mesh, in_specs=in_specs, out_specs=out_specs, check_vma=False
    )
```

```python
import functools

import jax
import jax.numpy as jnp
from jax import lax
from jax.experimental import pallas as pl
from jax.experimental.pallas import tpu as pltpu
from jax.sharding import PartitionSpec as P

PICARD = 3
GHOST = 3

relax_coef = 0.25
advect_coef = 0.1


def _inside_mask(rows, cols, ext_rows, ext_cols, c, d, n_cap, n_lat):
    g = GHOST
    far = -(1 << 20)
    i = jnp.arange(ext_rows, dtype=jnp.int32)
    j = jnp.arange(ext_cols, dtype=jnp.int32)
    local_r = jnp.where(i < rows + g, i, jnp.where(i >= ext_rows - g, i - ext_rows, far))
    local_c = jnp.where(j < cols + g, j, jnp.where(j >= ext_cols - g, j - ext_cols, far))
    glob_r = c * rows + local_r
    glob_c = d * cols + local_c
    ok_r = (local_r > far) & (glob_r >= 0) & (glob_r < n_cap * rows)
    ok_c = (local_c > far) & (glob_c >= 0) & (glob_c < n_lat * cols)
    return (ok_r[:, None] & ok_c[None, :]).astype(jnp.float32)


def _pairs(n, step):
    return [(i, i + step) for i in range(n) if 0 <= i + step < n]


def _sweep_kernel(rad_ref, lam_ref, eta_ref, rowh_ref, colh_ref, mask_ref, vel_ref, dep_ref,
                  after_ref, recv_ref, send_ref, keep_ref, lam_x, eta_x):
    layers, rows, cols = lam_ref.shape
    n_r, n_c = lam_x.shape[1], lam_x.shape[2]
    for ref, src, k in ((lam_x, lam_ref, 0), (eta_x, eta_ref, 1)):
        ref[:, :rows, :cols] = src[...]
        ref[:, rows:, :cols] = rowh_ref[k]
        ref[:, :, cols:] = colh_ref[k]
    lam = lam_x[...]
    eta = eta_x[...]
    m = mask_ref[...][None]

    def up(x):
        return pltpu.roll(x, n_r - 1, 1)

    def dn(x):
        return pltpu.roll(x, 1, 1)

    def rt(x):
        return pltpu.roll(x, n_c - 1, 2)

    def lf(x):
        return pltpu.roll(x, 1, 2)

    ca_raw = 0.5 * (eta + up(eta))
    cb_raw = 0.5 * (eta + rt(eta))
    mq = relax_coef * m
    ca = ca_raw * mq
    cd = dn(ca_raw) * mq
    cb = cb_raw * mq
    cl = lf(cb_raw) * mq
    w = lam
    for _ in range(PICARD - 1):
        total = ca * (up(w) - w)
        total = total + cd * (dn(w) - w)
        total = total + cb * (rt(w) - w)
        total = total + cl * (lf(w) - w)
        w = lam + total

    def main(x):
        return x[:, :rows, :cols]

    wm = main(w)
    total = main(ca) * (main(up(w)) - wm)
    total = total + main(cd) * (main(dn(w)) - wm)
    total = total + main(cb) * (main(rt(w)) - wm)
    total = total + main(cl) * (main(lf(w)) - wm)
    w3 = main(lam) + total
    v0 = vel_ref[0].astype(jnp.float32)
    v1 = vel_ref[1].astype(jnp.float32)
    adv = v0 * main(up(lam) - dn(lam)) + v1 * main(rt(lam) - lf(lam))
    rhs = w3 + advect_coef * adv + dep_ref[...]
    half = rows // 2
    lo = rhs[:, :half, :]
    hi = rhs[:, half:, :]
    is_zero = rad_ref[0] == 0
    send_ref[...] = jnp.where(is_zero, hi, lo)
    keep_ref[...] = jnp.where(is_zero, lo, hi)


def _sweeps(rad_idx, lam, eta, rowh, colh, mask, vel, dep, after, recv, first_layer, n_layers,
            block_layers):
    _, rows, cols = lam.shape
    ext_r, ext_c = mask.shape
    half = rows // 2
    off = first_layer // block_layers
    bl = block_layers
    grid = (n_layers // bl,)
    out_shape = [jax.ShapeDtypeStruct((n_layers, half, cols), jnp.float32)] * 2
    return pl.pallas_call(
        _sweep_kernel,
        out_shape=out_shape,
        grid=grid,
        in_specs=[
            pl.BlockSpec(memory_space=pltpu.SMEM),
            pl.BlockSpec((bl, rows, cols), lambda i: (i + off, 0, 0)),
            pl.BlockSpec((bl, rows, cols), lambda i: (i + off, 0, 0)),
            pl.BlockSpec((2, bl, ext_r - rows, cols), lambda i: (0, i + off, 0, 0)),
            pl.BlockSpec((2, bl, ext_r, ext_c - cols), lambda i: (0, i + off, 0, 0)),
            pl.BlockSpec((ext_r, ext_c), lambda i: (0, 0)),
            pl.BlockSpec((2, bl, rows, cols), lambda i: (0, i + off, 0, 0)),
            pl.BlockSpec((bl, rows, cols), lambda i: (i + off, 0, 0)),
            pl.BlockSpec(memory_space=pl.ANY),
            pl.BlockSpec(memory_space=pl.ANY),
        ],
        out_specs=[
            pl.BlockSpec((bl, half, cols), lambda i: (i, 0, 0)),
            pl.BlockSpec((bl, half, cols), lambda i: (i, 0, 0)),
        ],
        scratch_shapes=[
            pltpu.VMEM((bl, ext_r, ext_c), jnp.float32),
            pltpu.VMEM((bl, ext_r, ext_c), jnp.float32),
        ],
        cost_estimate=pl.CostEstimate(
            flops=n_layers * ext_r * ext_c * 6000,
            transcendentals=0,
            bytes_accessed=n_layers * 1_600_000,
        ),
    )(rad_idx, lam, eta, rowh, colh, mask, vel, dep, after, recv)


def per_device(
    adjoint_temp,
    velocity,
    visc_flow,
    visc_yield,
    yield_mask,
    radial_inverse,
    marker_rows,
    recv_cells,
    recv_counts,
):
    layers, rows, cols = adjoint_temp.shape
    n_cap = lax.axis_size("cap")
    n_lat = lax.axis_size("lat")
    n_rad = lax.axis_size("rad")
    c = lax.axis_index("cap")
    d = lax.axis_index("lat")
    r = lax.axis_index("rad")

    flow = visc_flow.astype(jnp.float32)
    plast = visc_yield.astype(jnp.float32)
    eta = jnp.where(yield_mask == 1, flow * plast / (flow + plast), flow)

    g = GHOST
    ext_rows = ((rows + 2 * g + 7) // 8) * 8
    ext_cols = ((cols + 2 * g + 127) // 128) * 128
    top_send = jnp.concatenate([adjoint_temp[:, rows - g:], eta[:, rows - g:]], axis=1)
    bot_send = jnp.concatenate([adjoint_temp[:, :g], eta[:, :g]], axis=1)
    top = lax.ppermute(top_send, "cap", _pairs(n_cap, 1))
    bot = lax.ppermute(bot_send, "cap", _pairs(n_cap, -1))
    zr = jnp.zeros((layers, ext_rows - rows - 2 * g, cols), jnp.float32)
    rowh = jnp.stack([
        jnp.concatenate([bot[:, :g], zr, top[:, :g]], axis=1),
        jnp.concatenate([bot[:, g:], zr, top[:, g:]], axis=1),
    ])

    def col_piece(sl):
        parts = []
        for k, src in enumerate((adjoint_temp, eta)):
            parts.append(jnp.concatenate([src[:, :, sl], rowh[k][:, :, sl]], axis=1))
        return jnp.stack(parts)

    flat = jnp.stack([col_piece(slice(0, g)), col_piece(slice(cols - g, cols))]).reshape(-1)
    piece = flat.shape[0] // 2
    flat, markers = lax.optimization_barrier((flat, marker_rows))
    received = lax.all_to_all(markers, "lat", split_axis=1, concat_axis=1, tiled=True)
    from_right = lax.ppermute(flat[:piece], "lat", _pairs(n_lat, -1))
    from_left = lax.ppermute(flat[piece:], "lat", _pairs(n_lat, 1))
    got = jnp.concatenate([from_right, from_left]).reshape(2, 2, layers, ext_rows, g)
    zc = jnp.zeros((2, layers, ext_rows, ext_cols - cols - 2 * g), jnp.float32)
    colh = jnp.concatenate([got[0], zc, got[1]], axis=3)
    mask = _inside_mask(rows, cols, ext_rows, ext_cols, c, d, n_cap, n_lat)

    senders = n_lat
    slot_total = received.shape[1]
    per_sender = slot_total // senders
    live = (jnp.arange(per_sender, dtype=jnp.int32)[None, :] < recv_counts[:, None]).reshape(-1)
    cell_a = recv_cells // cols
    cell_b = recv_cells % cols
    hit_a = (cell_a[None, :] == jnp.arange(rows, dtype=jnp.int32)[:, None]) & live[None, :]
    xa = jnp.where(hit_a[None], received[:, None, :], jnp.zeros((), received.dtype))
    onehot_b = (cell_b[:, None] == jnp.arange(cols, dtype=jnp.int32)[None, :]).astype(received.dtype)
    deposit = jnp.einsum("las,sb->lab", xa, onehot_b, preferred_element_type=jnp.float32)

    rad_idx = r.astype(jnp.int32).reshape(1)
    n_chunks = 4
    chunk = layers // n_chunks
    block_layers = 8
    keeps = []
    recvs = []
    after = rad_idx
    for k in range(n_chunks):
        landed = recvs[k - 2] if k >= 2 else rad_idx
        send, keep = _sweeps(
            rad_idx, adjoint_temp, eta, rowh, colh, mask, velocity, deposit, after, landed,
            k * chunk, chunk, block_layers,
        )
        after = keep
        recvs.append(lax.ppermute(send, "rad", _pairs(n_rad, 1) + _pairs(n_rad, -1)))
        keeps.append(keep)

    my_cols = lax.dynamic_slice_in_dim(radial_inverse, r * layers, layers, axis=1)
    peer_cols = lax.dynamic_slice_in_dim(radial_inverse, (1 - r) * layers, layers, axis=1)
    r_perm = jnp.concatenate([my_cols, peer_cols], axis=1)
    pieces = keeps + recvs
    split = len(pieces) - 2
    step = pieces[0].shape[0]
    partial = _radial(r_perm[:, :split * step], pieces[:split], after=recvs[-2])
    return _radial(r_perm[:, split * step:], pieces[split:], partial=partial)


def _radial_kernel(n_pieces, has_partial, r_ref, *refs):
    pieces = refs[:n_pieces]
    rest = refs[n_pieces:]
    partial_ref = rest[0] if has_partial else None
    out_ref, xs, kr = rest[-3], rest[-2], rest[-1]
    n_k, n_l = r_ref.shape
    tile = out_ref.shape[1]
    hi = lax.Precision.HIGHEST

    @pl.when(pl.program_id(0) == 0)
    def _():
        shift = tile.bit_length() - 1
        p = lax.broadcasted_iota(jnp.int32, (n_k * tile, n_k), 0)
        q = lax.broadcasted_iota(jnp.int32, (n_k * tile, n_k), 1)
        rep_rows = jnp.where(lax.shift_right_logical(p, shift) == q, 1.0, 0.0)
        rows_r = jnp.dot(rep_rows, r_ref[...], precision=hi, preferred_element_type=jnp.float32)
        p = lax.broadcasted_iota(jnp.int32, (n_l, n_l * tile), 0)
        q = lax.broadcasted_iota(jnp.int32, (n_l, n_l * tile), 1)
        rep_cols = jnp.where(p == lax.shift_right_logical(q, shift), 1.0, 0.0)
        full = jnp.dot(rows_r, rep_cols, precision=hi, preferred_element_type=jnp.float32)
        i = lax.broadcasted_iota(jnp.int32, full.shape, 0) & (tile - 1)
        j = lax.broadcasted_iota(jnp.int32, full.shape, 1) & (tile - 1)
        kr[...] = jnp.where(i == j, full, 0.0)

    step = pieces[0].shape[0]
    for n, piece in enumerate(pieces):
        xs[n * step:(n + 1) * step] = piece[...]
    n_b = xs.shape[2]
    y = jnp.dot(kr[...], xs[...].reshape(n_l * tile, n_b), precision=hi,
                preferred_element_type=jnp.float32).reshape(out_ref.shape)
    if has_partial:
        y = partial_ref[...] + y
    out_ref[...] = y


def _radial(r_cols, pieces, partial=None, after=None):
    n_k, n_l = r_cols.shape
    step, n_a, n_b = pieces[0].shape
    tile = 8
    extra = [] if partial is None else [partial]
    fake = [] if after is None else [after]
    in_specs = [pl.BlockSpec((n_k, n_l), lambda t: (0, 0))]
    in_specs += [pl.BlockSpec((step, tile, n_b), lambda t: (0, t, 0))] * len(pieces)
    in_specs += [pl.BlockSpec((n_k, tile, n_b), lambda t: (0, t, 0))] * len(extra)
    in_specs += [pl.BlockSpec(memory_space=pl.ANY)] * len(fake)
    return pl.pallas_call(
        functools.partial(_radial_kernel, len(pieces), partial is not None),
        out_shape=jax.ShapeDtypeStruct((n_k, n_a, n_b), jnp.float32),
        grid=(n_a // tile,),
        in_specs=in_specs,
        out_specs=pl.BlockSpec((n_k, tile, n_b), lambda t: (0, t, 0)),
        scratch_shapes=[
            pltpu.VMEM((n_l, tile, n_b), jnp.float32),
            pltpu.VMEM((n_k * tile, n_l * tile), jnp.float32),
        ],
    )(r_cols, *pieces, *extra, *fake)


def solution(mesh):
    in_specs = (
        P("rad", "cap", "lat"),
        P(None, "rad", "cap", "lat"),
        P("rad", "cap", "lat"),
        P("rad", "cap", "lat"),
        P("rad", "cap", "lat"),
        P(),
        P("rad", ("cap", "lat")),
        P(("cap", "lat")),
        P(("cap", "lat")),
    )
    out_specs = P(None, ("cap", "rad"), "lat")
    return jax.shard_map(
        per_device, mesh=mesh, in_specs=in_specs, out_specs=out_specs, check_vma=False
    )
```

```python
import functools

import jax
import jax.numpy as jnp
from jax import lax
from jax.experimental import pallas as pl
from jax.experimental.pallas import tpu as pltpu
from jax.sharding import PartitionSpec as P

PICARD = 3
GHOST = 3

relax_coef = 0.25
advect_coef = 0.1


def _inside_mask(rows, cols, ext_rows, ext_cols, c, d, n_cap, n_lat):
    g = GHOST
    far = -(1 << 20)
    i = jnp.arange(ext_rows, dtype=jnp.int32)
    j = jnp.arange(ext_cols, dtype=jnp.int32)
    local_r = jnp.where(i < rows + g, i, jnp.where(i >= ext_rows - g, i - ext_rows, far))
    local_c = jnp.where(j < cols + g, j, jnp.where(j >= ext_cols - g, j - ext_cols, far))
    glob_r = c * rows + local_r
    glob_c = d * cols + local_c
    ok_r = (local_r > far) & (glob_r >= 0) & (glob_r < n_cap * rows)
    ok_c = (local_c > far) & (glob_c >= 0) & (glob_c < n_lat * cols)
    return (ok_r[:, None] & ok_c[None, :]).astype(jnp.float32)


def _pairs(n, step):
    return [(i, i + step) for i in range(n) if 0 <= i + step < n]


def _sweep_kernel(rad_ref, lam_ref, eta_ref, rowh_ref, colh_ref, mask_ref, vel_ref, dep_ref,
                  after_ref, recv_ref, send_ref, keep_ref, lam_x, eta_x):
    layers, rows, cols = lam_ref.shape
    n_r, n_c = lam_x.shape[1], lam_x.shape[2]
    for ref, src, k in ((lam_x, lam_ref, 0), (eta_x, eta_ref, 1)):
        ref[:, :rows, :cols] = src[...]
        ref[:, rows:, :cols] = rowh_ref[k]
        ref[:, :, cols:] = colh_ref[k]
    lam = lam_x[...]
    eta = eta_x[...]
    m = mask_ref[...][None]

    def up(x):
        return pltpu.roll(x, n_r - 1, 1)

    def dn(x):
        return pltpu.roll(x, 1, 1)

    def rt(x):
        return pltpu.roll(x, n_c - 1, 2)

    def lf(x):
        return pltpu.roll(x, 1, 2)

    ca_raw = 0.5 * (eta + up(eta))
    cb_raw = 0.5 * (eta + rt(eta))
    mq = relax_coef * m
    ca = ca_raw * mq
    cd = dn(ca_raw) * mq
    cb = cb_raw * mq
    cl = lf(cb_raw) * mq
    w = lam
    for _ in range(PICARD - 1):
        total = ca * (up(w) - w)
        total = total + cd * (dn(w) - w)
        total = total + cb * (rt(w) - w)
        total = total + cl * (lf(w) - w)
        w = lam + total

    def main(x):
        return x[:, :rows, :cols]

    wm = main(w)
    total = main(ca) * (main(up(w)) - wm)
    total = total + main(cd) * (main(dn(w)) - wm)
    total = total + main(cb) * (main(rt(w)) - wm)
    total = total + main(cl) * (main(lf(w)) - wm)
    w3 = main(lam) + total
    v0 = vel_ref[0].astype(jnp.float32)
    v1 = vel_ref[1].astype(jnp.float32)
    adv = v0 * main(up(lam) - dn(lam)) + v1 * main(rt(lam) - lf(lam))
    rhs = w3 + advect_coef * adv + dep_ref[...]
    half = rows // 2
    lo = rhs[:, :half, :]
    hi = rhs[:, half:, :]
    is_zero = rad_ref[0] == 0
    send_ref[...] = jnp.where(is_zero, hi, lo)
    keep_ref[...] = jnp.where(is_zero, lo, hi)


def _sweeps(rad_idx, lam, eta, rowh, colh, mask, vel, dep, after, recv, first_layer, n_layers,
            block_layers):
    _, rows, cols = lam.shape
    ext_r, ext_c = mask.shape
    half = rows // 2
    off = first_layer // block_layers
    bl = block_layers
    grid = (n_layers // bl,)
    out_shape = [jax.ShapeDtypeStruct((n_layers, half, cols), jnp.float32)] * 2
    return pl.pallas_call(
        _sweep_kernel,
        out_shape=out_shape,
        grid=grid,
        in_specs=[
            pl.BlockSpec(memory_space=pltpu.SMEM),
            pl.BlockSpec((bl, rows, cols), lambda i: (i + off, 0, 0)),
            pl.BlockSpec((bl, rows, cols), lambda i: (i + off, 0, 0)),
            pl.BlockSpec((2, bl, ext_r - rows, cols), lambda i: (0, i + off, 0, 0)),
            pl.BlockSpec((2, bl, ext_r, ext_c - cols), lambda i: (0, i + off, 0, 0)),
            pl.BlockSpec((ext_r, ext_c), lambda i: (0, 0)),
            pl.BlockSpec((2, bl, rows, cols), lambda i: (0, i + off, 0, 0)),
            pl.BlockSpec((bl, rows, cols), lambda i: (i + off, 0, 0)),
            pl.BlockSpec(memory_space=pl.ANY),
            pl.BlockSpec(memory_space=pl.ANY),
        ],
        out_specs=[
            pl.BlockSpec((bl, half, cols), lambda i: (i, 0, 0)),
            pl.BlockSpec((bl, half, cols), lambda i: (i, 0, 0)),
        ],
        scratch_shapes=[
            pltpu.VMEM((bl, ext_r, ext_c), jnp.float32),
            pltpu.VMEM((bl, ext_r, ext_c), jnp.float32),
        ],
        cost_estimate=pl.CostEstimate(
            flops=n_layers * ext_r * ext_c * 6000,
            transcendentals=0,
            bytes_accessed=n_layers * 1_600_000,
        ),
    )(rad_idx, lam, eta, rowh, colh, mask, vel, dep, after, recv)


def per_device(
    adjoint_temp,
    velocity,
    visc_flow,
    visc_yield,
    yield_mask,
    radial_inverse,
    marker_rows,
    recv_cells,
    recv_counts,
):
    layers, rows, cols = adjoint_temp.shape
    n_cap = lax.axis_size("cap")
    n_lat = lax.axis_size("lat")
    n_rad = lax.axis_size("rad")
    c = lax.axis_index("cap")
    d = lax.axis_index("lat")
    r = lax.axis_index("rad")

    flow = visc_flow.astype(jnp.float32)
    plast = visc_yield.astype(jnp.float32)
    eta = jnp.where(yield_mask == 1, flow * plast / (flow + plast), flow)

    g = GHOST
    ext_rows = ((rows + 2 * g + 7) // 8) * 8
    ext_cols = ((cols + 2 * g + 127) // 128) * 128
    top_send = jnp.concatenate([adjoint_temp[:, rows - g:], eta[:, rows - g:]], axis=1)
    bot_send = jnp.concatenate([adjoint_temp[:, :g], eta[:, :g]], axis=1)
    top = lax.ppermute(top_send, "cap", _pairs(n_cap, 1))
    bot = lax.ppermute(bot_send, "cap", _pairs(n_cap, -1))
    zr = jnp.zeros((layers, ext_rows - rows - 2 * g, cols), jnp.float32)
    rowh = jnp.stack([
        jnp.concatenate([bot[:, :g], zr, top[:, :g]], axis=1),
        jnp.concatenate([bot[:, g:], zr, top[:, g:]], axis=1),
    ])

    def col_piece(sl):
        parts = []
        for k, src in enumerate((adjoint_temp, eta)):
            parts.append(jnp.concatenate([src[:, :, sl], rowh[k][:, :, sl]], axis=1))
        return jnp.stack(parts)

    both_sides = jnp.stack([col_piece(slice(0, g)), col_piece(slice(cols - g, cols))])
    flat = both_sides.reshape(-1, 128) if both_sides.size % 256 == 0 else both_sides.reshape(-1)
    piece = flat.shape[0] // 2
    flat, markers = lax.optimization_barrier((flat, marker_rows))
    received = lax.all_to_all(markers, "lat", split_axis=1, concat_axis=1, tiled=True)
    from_right = lax.ppermute(flat[:piece], "lat", _pairs(n_lat, -1))
    from_left = lax.ppermute(flat[piece:], "lat", _pairs(n_lat, 1))
    got = jnp.concatenate([from_right, from_left]).reshape(2, 2, layers, ext_rows, g)
    zc = jnp.zeros((2, layers, ext_rows, ext_cols - cols - 2 * g), jnp.float32)
    colh = jnp.concatenate([got[0], zc, got[1]], axis=3)
    mask = _inside_mask(rows, cols, ext_rows, ext_cols, c, d, n_cap, n_lat)

    senders = n_lat
    slot_total = received.shape[1]
    per_sender = slot_total // senders
    live = (jnp.arange(per_sender, dtype=jnp.int32)[None, :] < recv_counts[:, None]).reshape(-1)
    cell_a = recv_cells // cols
    cell_b = recv_cells % cols
    hit_a = (cell_a[None, :] == jnp.arange(rows, dtype=jnp.int32)[:, None]) & live[None, :]
    xa = jnp.where(hit_a[None], received[:, None, :], jnp.zeros((), received.dtype))
    onehot_b = (cell_b[:, None] == jnp.arange(cols, dtype=jnp.int32)[None, :]).astype(received.dtype)
    deposit = jnp.einsum("las,sb->lab", xa, onehot_b, preferred_element_type=jnp.float32)

    rad_idx = r.astype(jnp.int32).reshape(1)
    n_chunks = 4
    chunk = layers // n_chunks
    block_layers = 8
    keeps = []
    recvs = []
    after = rad_idx
    for k in range(n_chunks):
        landed = recvs[k - 2] if k >= 2 else rad_idx
        send, keep = _sweeps(
            rad_idx, adjoint_temp, eta, rowh, colh, mask, velocity, deposit, after, landed,
            k * chunk, chunk, block_layers,
        )
        after = keep
        recvs.append(lax.ppermute(send, "rad", _pairs(n_rad, 1) + _pairs(n_rad, -1)))
        keeps.append(keep)

    my_cols = lax.dynamic_slice_in_dim(radial_inverse, r * layers, layers, axis=1)
    peer_cols = lax.dynamic_slice_in_dim(radial_inverse, (1 - r) * layers, layers, axis=1)
    r_perm = jnp.concatenate([my_cols, peer_cols], axis=1)
    pieces = keeps + recvs
    split = len(pieces) - 2
    step = pieces[0].shape[0]
    partial = _radial(r_perm[:, :split * step], pieces[:split], after=recvs[-2])
    return _radial(r_perm[:, split * step:], pieces[split:], partial=partial)


def _radial_kernel(n_pieces, has_partial, r_ref, *refs):
    pieces = refs[:n_pieces]
    rest = refs[n_pieces:]
    partial_ref = rest[0] if has_partial else None
    out_ref, xs = rest[-2], rest[-1]
    step = pieces[0].shape[0]
    for i, p in enumerate(pieces):
        xs[i * step:(i + 1) * step] = p[...]
    n_l, n_a, n_b = xs.shape
    y = jnp.dot(r_ref[...], xs[...].reshape(n_l, n_a * n_b), precision=lax.Precision.HIGHEST,
                preferred_element_type=jnp.float32).reshape(out_ref.shape)
    if has_partial:
        y = partial_ref[...] + y
    out_ref[...] = y


def _radial(r_cols, pieces, partial=None, after=None):
    n_k, n_l = r_cols.shape
    step, n_a, n_b = pieces[0].shape
    tile = 8
    extra = [] if partial is None else [partial]
    fake = [] if after is None else [after]
    in_specs = [pl.BlockSpec((n_k, n_l), lambda t: (0, 0))]
    in_specs += [pl.BlockSpec((step, tile, n_b), lambda t: (0, t, 0))] * len(pieces)
    in_specs += [pl.BlockSpec((n_k, tile, n_b), lambda t: (0, t, 0))] * len(extra)
    in_specs += [pl.BlockSpec(memory_space=pl.ANY)] * len(fake)
    return pl.pallas_call(
        functools.partial(_radial_kernel, len(pieces), partial is not None),
        out_shape=jax.ShapeDtypeStruct((n_k, n_a, n_b), jnp.float32),
        grid=(n_a // tile,),
        in_specs=in_specs,
        out_specs=pl.BlockSpec((n_k, tile, n_b), lambda t: (0, t, 0)),
        scratch_shapes=[pltpu.VMEM((n_l, tile, n_b), jnp.float32)],
    )(r_cols, *pieces, *extra, *fake)


def solution(mesh):
    in_specs = (
        P("rad", "cap", "lat"),
        P(None, "rad", "cap", "lat"),
        P("rad", "cap", "lat"),
        P("rad", "cap", "lat"),
        P("rad", "cap", "lat"),
        P(),
        P("rad", ("cap", "lat")),
        P(("cap", "lat")),
        P(("cap", "lat")),
    )
    out_specs = P(None, ("cap", "rad"), "lat")
    return jax.shard_map(
        per_device, mesh=mesh, in_specs=in_specs, out_specs=out_specs, check_vma=False
    )
```

```python
import functools

import jax
import jax.numpy as jnp
from jax import lax
from jax.experimental import pallas as pl
from jax.experimental.pallas import tpu as pltpu
from jax.sharding import PartitionSpec as P

PICARD = 3
GHOST = 3

relax_coef = 0.25
advect_coef = 0.1


def _inside_mask(rows, cols, ext_rows, ext_cols, c, d, n_cap, n_lat):
    g = GHOST
    far = -(1 << 20)
    i = jnp.arange(ext_rows, dtype=jnp.int32)
    j = jnp.arange(ext_cols, dtype=jnp.int32)
    local_r = jnp.where(i < rows + g, i, jnp.where(i >= ext_rows - g, i - ext_rows, far))
    local_c = jnp.where(j < cols + g, j, jnp.where(j >= ext_cols - g, j - ext_cols, far))
    glob_r = c * rows + local_r
    glob_c = d * cols + local_c
    ok_r = (local_r > far) & (glob_r >= 0) & (glob_r < n_cap * rows)
    ok_c = (local_c > far) & (glob_c >= 0) & (glob_c < n_lat * cols)
    return (ok_r[:, None] & ok_c[None, :]).astype(jnp.float32)


def _pairs(n, step):
    return [(i, i + step) for i in range(n) if 0 <= i + step < n]


def _sweep_kernel(rad_ref, lam_ref, eta_ref, rowh_ref, colh_ref, mask_ref, vel_ref, dep_ref,
                  after_ref, recv_ref, send_ref, keep_ref, lam_x, eta_x):
    layers, rows, cols = lam_ref.shape
    n_r, n_c = lam_x.shape[1], lam_x.shape[2]
    for ref, src, k in ((lam_x, lam_ref, 0), (eta_x, eta_ref, 1)):
        ref[:, :rows, :cols] = src[...]
        ref[:, rows:, :cols] = rowh_ref[k]
        ref[:, :, cols:] = colh_ref[k]
    lam = lam_x[...]
    eta = eta_x[...]
    m = mask_ref[...][None]

    def up(x):
        return pltpu.roll(x, n_r - 1, 1)

    def dn(x):
        return pltpu.roll(x, 1, 1)

    def rt(x):
        return pltpu.roll(x, n_c - 1, 2)

    def lf(x):
        return pltpu.roll(x, 1, 2)

    ca_raw = 0.5 * (eta + up(eta))
    cb_raw = 0.5 * (eta + rt(eta))
    mq = relax_coef * m
    ca = ca_raw * mq
    cd = dn(ca_raw) * mq
    cb = cb_raw * mq
    cl = lf(cb_raw) * mq
    w = lam
    for _ in range(PICARD - 1):
        total = ca * (up(w) - w)
        total = total + cd * (dn(w) - w)
        total = total + cb * (rt(w) - w)
        total = total + cl * (lf(w) - w)
        w = lam + total

    def main(x):
        return x[:, :rows, :cols]

    wm = main(w)
    total = main(ca) * (main(up(w)) - wm)
    total = total + main(cd) * (main(dn(w)) - wm)
    total = total + main(cb) * (main(rt(w)) - wm)
    total = total + main(cl) * (main(lf(w)) - wm)
    w3 = main(lam) + total
    v0 = vel_ref[0].astype(jnp.float32)
    v1 = vel_ref[1].astype(jnp.float32)
    adv = v0 * main(up(lam) - dn(lam)) + v1 * main(rt(lam) - lf(lam))
    rhs = w3 + advect_coef * adv + dep_ref[...]
    half = rows // 2
    lo = rhs[:, :half, :]
    hi = rhs[:, half:, :]
    is_zero = rad_ref[0] == 0
    send_ref[...] = jnp.where(is_zero, hi, lo)
    keep_ref[...] = jnp.where(is_zero, lo, hi)


def _sweeps(rad_idx, lam, eta, rowh, colh, mask, vel, dep, after, recv, first_layer, n_layers,
            block_layers):
    _, rows, cols = lam.shape
    ext_r, ext_c = mask.shape
    half = rows // 2
    off = first_layer // block_layers
    bl = block_layers
    grid = (n_layers // bl,)
    out_shape = [jax.ShapeDtypeStruct((n_layers, half, cols), jnp.float32)] * 2
    return pl.pallas_call(
        _sweep_kernel,
        out_shape=out_shape,
        grid=grid,
        in_specs=[
            pl.BlockSpec(memory_space=pltpu.SMEM),
            pl.BlockSpec((bl, rows, cols), lambda i: (i + off, 0, 0)),
            pl.BlockSpec((bl, rows, cols), lambda i: (i + off, 0, 0)),
            pl.BlockSpec((2, bl, ext_r - rows, cols), lambda i: (0, i + off, 0, 0)),
            pl.BlockSpec((2, bl, ext_r, ext_c - cols), lambda i: (0, i + off, 0, 0)),
            pl.BlockSpec((ext_r, ext_c), lambda i: (0, 0)),
            pl.BlockSpec((2, bl, rows, cols), lambda i: (0, i + off, 0, 0)),
            pl.BlockSpec((bl, rows, cols), lambda i: (i + off, 0, 0)),
            pl.BlockSpec(memory_space=pl.ANY),
            pl.BlockSpec(memory_space=pl.ANY),
        ],
        out_specs=[
            pl.BlockSpec((bl, half, cols), lambda i: (i, 0, 0)),
            pl.BlockSpec((bl, half, cols), lambda i: (i, 0, 0)),
        ],
        scratch_shapes=[
            pltpu.VMEM((bl, ext_r, ext_c), jnp.float32),
            pltpu.VMEM((bl, ext_r, ext_c), jnp.float32),
        ],
        cost_estimate=pl.CostEstimate(
            flops=n_layers * ext_r * ext_c * 6000,
            transcendentals=0,
            bytes_accessed=n_layers * 1_600_000,
        ),
    )(rad_idx, lam, eta, rowh, colh, mask, vel, dep, after, recv)


def per_device(
    adjoint_temp,
    velocity,
    visc_flow,
    visc_yield,
    yield_mask,
    radial_inverse,
    marker_rows,
    recv_cells,
    recv_counts,
):
    layers, rows, cols = adjoint_temp.shape
    n_cap = lax.axis_size("cap")
    n_lat = lax.axis_size("lat")
    n_rad = lax.axis_size("rad")
    c = lax.axis_index("cap")
    d = lax.axis_index("lat")
    r = lax.axis_index("rad")

    flow = visc_flow.astype(jnp.float32)
    plast = visc_yield.astype(jnp.float32)
    eta = jnp.where(yield_mask == 1, flow * plast / (flow + plast), flow)

    g = GHOST
    ext_rows = ((rows + 2 * g + 7) // 8) * 8
    ext_cols = ((cols + 2 * g + 127) // 128) * 128
    top_send = jnp.concatenate([adjoint_temp[:, rows - g:], eta[:, rows - g:]], axis=1)
    bot_send = jnp.concatenate([adjoint_temp[:, :g], eta[:, :g]], axis=1)
    top = lax.ppermute(top_send, "cap", _pairs(n_cap, 1))
    bot = lax.ppermute(bot_send, "cap", _pairs(n_cap, -1))
    zr = jnp.zeros((layers, ext_rows - rows - 2 * g, cols), jnp.float32)
    rowh = jnp.stack([
        jnp.concatenate([bot[:, :g], zr, top[:, :g]], axis=1),
        jnp.concatenate([bot[:, g:], zr, top[:, g:]], axis=1),
    ])

    def col_piece(sl):
        parts = []
        for k, src in enumerate((adjoint_temp, eta)):
            parts.append(jnp.concatenate([src[:, :, sl], rowh[k][:, :, sl]], axis=1))
        return jnp.stack(parts)

    flat = jnp.stack([col_piece(slice(0, g)), col_piece(slice(cols - g, cols))]).reshape(-1)
    piece = flat.shape[0] // 2
    from_right = lax.ppermute(flat[:piece], "lat", _pairs(n_lat, -1))
    from_left = lax.ppermute(flat[piece:], "lat", _pairs(n_lat, 1))
    got = jnp.concatenate([from_right, from_left]).reshape(2, 2, layers, ext_rows, g)
    zc = jnp.zeros((2, layers, ext_rows, ext_cols - cols - 2 * g), jnp.float32)
    colh = jnp.concatenate([got[0], zc, got[1]], axis=3)
    colh, markers = lax.optimization_barrier((colh, marker_rows))
    received = lax.all_to_all(markers, "lat", split_axis=1, concat_axis=1, tiled=True)
    mask = _inside_mask(rows, cols, ext_rows, ext_cols, c, d, n_cap, n_lat)

    senders = n_lat
    slot_total = received.shape[1]
    per_sender = slot_total // senders
    live = (jnp.arange(per_sender, dtype=jnp.int32)[None, :] < recv_counts[:, None]).reshape(-1)
    cell_a = recv_cells // cols
    cell_b = recv_cells % cols
    hit_a = (cell_a[None, :] == jnp.arange(rows, dtype=jnp.int32)[:, None]) & live[None, :]
    xa = jnp.where(hit_a[None], received[:, None, :], jnp.zeros((), received.dtype))
    onehot_b = (cell_b[:, None] == jnp.arange(cols, dtype=jnp.int32)[None, :]).astype(received.dtype)
    deposit = jnp.einsum("las,sb->lab", xa, onehot_b, preferred_element_type=jnp.float32)

    rad_idx = r.astype(jnp.int32).reshape(1)
    n_chunks = 4
    chunk = layers // n_chunks
    block_layers = 8
    keeps = []
    recvs = []
    after = rad_idx
    for k in range(n_chunks):
        landed = recvs[k - 2] if k >= 2 else rad_idx
        send, keep = _sweeps(
            rad_idx, adjoint_temp, eta, rowh, colh, mask, velocity, deposit, after, landed,
            k * chunk, chunk, block_layers,
        )
        after = keep
        recvs.append(lax.ppermute(send, "rad", _pairs(n_rad, 1) + _pairs(n_rad, -1)))
        keeps.append(keep)

    my_cols = lax.dynamic_slice_in_dim(radial_inverse, r * layers, layers, axis=1)
    peer_cols = lax.dynamic_slice_in_dim(radial_inverse, (1 - r) * layers, layers, axis=1)
    r_perm = jnp.concatenate([my_cols, peer_cols], axis=1)
    pieces = keeps + recvs
    split = len(pieces) - 2
    step = pieces[0].shape[0]
    partial = _radial(r_perm[:, :split * step], pieces[:split], after=recvs[-2])
    return _radial(r_perm[:, split * step:], pieces[split:], partial=partial)


def _radial_kernel(n_pieces, has_partial, r_ref, *refs):
    pieces = refs[:n_pieces]
    rest = refs[n_pieces:]
    partial_ref = rest[0] if has_partial else None
    out_ref, xs = rest[-2], rest[-1]
    step = pieces[0].shape[0]
    for i, p in enumerate(pieces):
        xs[i * step:(i + 1) * step] = p[...]
    n_l, n_a, n_b = xs.shape
    y = jnp.dot(r_ref[...], xs[...].reshape(n_l, n_a * n_b), precision=lax.Precision.HIGHEST,
                preferred_element_type=jnp.float32).reshape(out_ref.shape)
    if has_partial:
        y = partial_ref[...] + y
    out_ref[...] = y


def _radial(r_cols, pieces, partial=None, after=None):
    n_k, n_l = r_cols.shape
    step, n_a, n_b = pieces[0].shape
    tile = 8
    extra = [] if partial is None else [partial]
    fake = [] if after is None else [after]
    in_specs = [pl.BlockSpec((n_k, n_l), lambda t: (0, 0))]
    in_specs += [pl.BlockSpec((step, tile, n_b), lambda t: (0, t, 0))] * len(pieces)
    in_specs += [pl.BlockSpec((n_k, tile, n_b), lambda t: (0, t, 0))] * len(extra)
    in_specs += [pl.BlockSpec(memory_space=pl.ANY)] * len(fake)
    return pl.pallas_call(
        functools.partial(_radial_kernel, len(pieces), partial is not None),
        out_shape=jax.ShapeDtypeStruct((n_k, n_a, n_b), jnp.float32),
        grid=(n_a // tile,),
        in_specs=in_specs,
        out_specs=pl.BlockSpec((n_k, tile, n_b), lambda t: (0, t, 0)),
        scratch_shapes=[pltpu.VMEM((n_l, tile, n_b), jnp.float32)],
    )(r_cols, *pieces, *extra, *fake)


def solution(mesh):
    in_specs = (
        P("rad", "cap", "lat"),
        P(None, "rad", "cap", "lat"),
        P("rad", "cap", "lat"),
        P("rad", "cap", "lat"),
        P("rad", "cap", "lat"),
        P(),
        P("rad", ("cap", "lat")),
        P(("cap", "lat")),
        P(("cap", "lat")),
    )
    out_specs = P(None, ("cap", "rad"), "lat")
    return jax.shard_map(
        per_device, mesh=mesh, in_specs=in_specs, out_specs=out_specs, check_vma=False
    )
```

```python
import functools

import jax
import jax.numpy as jnp
from jax import lax
from jax.experimental import pallas as pl
from jax.experimental.pallas import tpu as pltpu
from jax.sharding import PartitionSpec as P

PICARD = 3
GHOST = 3

relax_coef = 0.25
advect_coef = 0.1


def _inside_mask(rows, cols, ext_rows, ext_cols, c, d, n_cap, n_lat):
    g = GHOST
    far = -(1 << 20)
    i = jnp.arange(ext_rows, dtype=jnp.int32)
    j = jnp.arange(ext_cols, dtype=jnp.int32)
    local_r = jnp.where(i < rows + g, i, jnp.where(i >= ext_rows - g, i - ext_rows, far))
    local_c = jnp.where(j < cols + g, j, jnp.where(j >= ext_cols - g, j - ext_cols, far))
    glob_r = c * rows + local_r
    glob_c = d * cols + local_c
    ok_r = (local_r > far) & (glob_r >= 0) & (glob_r < n_cap * rows)
    ok_c = (local_c > far) & (glob_c >= 0) & (glob_c < n_lat * cols)
    return (ok_r[:, None] & ok_c[None, :]).astype(jnp.float32)


def _pairs(n, step):
    return [(i, i + step) for i in range(n) if 0 <= i + step < n]


def _sweep_kernel(rad_ref, lam_ref, eta_ref, rowh_ref, colh_ref, mask_ref, vel_ref, dep_ref,
                  after_ref, recv_ref, send_ref, keep_ref, lam_x, eta_x):
    layers, rows, cols = lam_ref.shape
    n_r, n_c = lam_x.shape[1], lam_x.shape[2]
    g = colh_ref.shape[-1]
    for ref, src, k in ((lam_x, lam_ref, 0), (eta_x, eta_ref, 1)):
        ref[:, :rows, :cols] = src[...]
        ref[:, rows:, :cols] = rowh_ref[k]
        ref[:, :, cols:] = jnp.zeros((layers, n_r, n_c - cols), jnp.float32)
        ref[:, :, cols:cols + g] = colh_ref[1, k]
        left = ref[:, :, cols:]
        ref[:, :, cols:] = jnp.zeros((layers, n_r, n_c - cols), jnp.float32)
        ref[:, :, cols:cols + g] = colh_ref[0, k]
        ref[:, :, cols:] = ref[:, :, cols:] + pltpu.roll(left, n_c - cols - g, 2)
    lam = lam_x[...]
    eta = eta_x[...]
    m = mask_ref[...][None]

    def up(x):
        return pltpu.roll(x, n_r - 1, 1)

    def dn(x):
        return pltpu.roll(x, 1, 1)

    def rt(x):
        return pltpu.roll(x, n_c - 1, 2)

    def lf(x):
        return pltpu.roll(x, 1, 2)

    ca_raw = 0.5 * (eta + up(eta))
    cb_raw = 0.5 * (eta + rt(eta))
    mq = relax_coef * m
    ca = ca_raw * mq
    cd = dn(ca_raw) * mq
    cb = cb_raw * mq
    cl = lf(cb_raw) * mq
    w = lam
    for _ in range(PICARD - 1):
        total = ca * (up(w) - w)
        total = total + cd * (dn(w) - w)
        total = total + cb * (rt(w) - w)
        total = total + cl * (lf(w) - w)
        w = lam + total

    def main(x):
        return x[:, :rows, :cols]

    wm = main(w)
    total = main(ca) * (main(up(w)) - wm)
    total = total + main(cd) * (main(dn(w)) - wm)
    total = total + main(cb) * (main(rt(w)) - wm)
    total = total + main(cl) * (main(lf(w)) - wm)
    w3 = main(lam) + total
    v0 = vel_ref[0].astype(jnp.float32)
    v1 = vel_ref[1].astype(jnp.float32)
    adv = v0 * main(up(lam) - dn(lam)) + v1 * main(rt(lam) - lf(lam))
    rhs = w3 + advect_coef * adv + dep_ref[...]
    half = rows // 2
    lo = rhs[:, :half, :]
    hi = rhs[:, half:, :]
    is_zero = rad_ref[0] == 0
    send_ref[...] = jnp.where(is_zero, hi, lo)
    keep_ref[...] = jnp.where(is_zero, lo, hi)


def _sweeps(rad_idx, lam, eta, rowh, colh, mask, vel, dep, after, recv, first_layer, n_layers,
            block_layers):
    _, rows, cols = lam.shape
    ext_r, ext_c = mask.shape
    half = rows // 2
    off = first_layer // block_layers
    bl = block_layers
    grid = (n_layers // bl,)
    out_shape = [jax.ShapeDtypeStruct((n_layers, half, cols), jnp.float32)] * 2
    return pl.pallas_call(
        _sweep_kernel,
        out_shape=out_shape,
        grid=grid,
        in_specs=[
            pl.BlockSpec(memory_space=pltpu.SMEM),
            pl.BlockSpec((bl, rows, cols), lambda i: (i + off, 0, 0)),
            pl.BlockSpec((bl, rows, cols), lambda i: (i + off, 0, 0)),
            pl.BlockSpec((2, bl, ext_r - rows, cols), lambda i: (0, i + off, 0, 0)),
            pl.BlockSpec((2, 2, bl, ext_r, GHOST), lambda i: (0, 0, i + off, 0, 0)),
            pl.BlockSpec((ext_r, ext_c), lambda i: (0, 0)),
            pl.BlockSpec((2, bl, rows, cols), lambda i: (0, i + off, 0, 0)),
            pl.BlockSpec((bl, rows, cols), lambda i: (i + off, 0, 0)),
            pl.BlockSpec(memory_space=pl.ANY),
            pl.BlockSpec(memory_space=pl.ANY),
        ],
        out_specs=[
            pl.BlockSpec((bl, half, cols), lambda i: (i, 0, 0)),
            pl.BlockSpec((bl, half, cols), lambda i: (i, 0, 0)),
        ],
        scratch_shapes=[
            pltpu.VMEM((bl, ext_r, ext_c), jnp.float32),
            pltpu.VMEM((bl, ext_r, ext_c), jnp.float32),
        ],
        cost_estimate=pl.CostEstimate(
            flops=n_layers * ext_r * ext_c * 6000,
            transcendentals=0,
            bytes_accessed=n_layers * 1_600_000,
        ),
    )(rad_idx, lam, eta, rowh, colh, mask, vel, dep, after, recv)


def per_device(
    adjoint_temp,
    velocity,
    visc_flow,
    visc_yield,
    yield_mask,
    radial_inverse,
    marker_rows,
    recv_cells,
    recv_counts,
):
    layers, rows, cols = adjoint_temp.shape
    n_cap = lax.axis_size("cap")
    n_lat = lax.axis_size("lat")
    n_rad = lax.axis_size("rad")
    c = lax.axis_index("cap")
    d = lax.axis_index("lat")
    r = lax.axis_index("rad")

    flow = visc_flow.astype(jnp.float32)
    plast = visc_yield.astype(jnp.float32)
    eta = jnp.where(yield_mask == 1, flow * plast / (flow + plast), flow)

    g = GHOST
    ext_rows = ((rows + 2 * g + 7) // 8) * 8
    ext_cols = ((cols + 2 * g + 127) // 128) * 128
    top_send = jnp.concatenate([adjoint_temp[:, rows - g:], eta[:, rows - g:]], axis=1)
    bot_send = jnp.concatenate([adjoint_temp[:, :g], eta[:, :g]], axis=1)
    top = lax.ppermute(top_send, "cap", _pairs(n_cap, 1))
    bot = lax.ppermute(bot_send, "cap", _pairs(n_cap, -1))
    zr = jnp.zeros((layers, ext_rows - rows - 2 * g, cols), jnp.float32)
    rowh = jnp.stack([
        jnp.concatenate([bot[:, :g], zr, top[:, :g]], axis=1),
        jnp.concatenate([bot[:, g:], zr, top[:, g:]], axis=1),
    ])

    def col_piece(sl):
        parts = []
        for k, src in enumerate((adjoint_temp, eta)):
            parts.append(jnp.concatenate([src[:, :, sl], rowh[k][:, :, sl]], axis=1))
        return jnp.stack(parts)

    flat = jnp.stack([col_piece(slice(0, g)), col_piece(slice(cols - g, cols))]).reshape(-1)
    piece = flat.shape[0] // 2
    flat, markers = lax.optimization_barrier((flat, marker_rows))
    received = lax.all_to_all(markers, "lat", split_axis=1, concat_axis=1, tiled=True)
    from_right = lax.ppermute(flat[:piece], "lat", _pairs(n_lat, -1))
    from_left = lax.ppermute(flat[piece:], "lat", _pairs(n_lat, 1))
    got = jnp.concatenate([from_right, from_left]).reshape(2, 2, layers, ext_rows, g)
    colh = got
    mask = _inside_mask(rows, cols, ext_rows, ext_cols, c, d, n_cap, n_lat)

    senders = n_lat
    slot_total = received.shape[1]
    per_sender = slot_total // senders
    live = (jnp.arange(per_sender, dtype=jnp.int32)[None, :] < recv_counts[:, None]).reshape(-1)
    cell_a = recv_cells // cols
    cell_b = recv_cells % cols
    hit_a = (cell_a[None, :] == jnp.arange(rows, dtype=jnp.int32)[:, None]) & live[None, :]
    xa = jnp.where(hit_a[None], received[:, None, :], jnp.zeros((), received.dtype))
    onehot_b = (cell_b[:, None] == jnp.arange(cols, dtype=jnp.int32)[None, :]).astype(received.dtype)
    deposit = jnp.einsum("las,sb->lab", xa, onehot_b, preferred_element_type=jnp.float32)

    rad_idx = r.astype(jnp.int32).reshape(1)
    n_chunks = 4
    chunk = layers // n_chunks
    block_layers = 8
    keeps = []
    recvs = []
    after = rad_idx
    for k in range(n_chunks):
        landed = recvs[k - 2] if k >= 2 else rad_idx
        send, keep = _sweeps(
            rad_idx, adjoint_temp, eta, rowh, colh, mask, velocity, deposit, after, landed,
            k * chunk, chunk, block_layers,
        )
        after = keep
        recvs.append(lax.ppermute(send, "rad", _pairs(n_rad, 1) + _pairs(n_rad, -1)))
        keeps.append(keep)

    my_cols = lax.dynamic_slice_in_dim(radial_inverse, r * layers, layers, axis=1)
    peer_cols = lax.dynamic_slice_in_dim(radial_inverse, (1 - r) * layers, layers, axis=1)
    r_perm = jnp.concatenate([my_cols, peer_cols], axis=1)
    pieces = keeps + recvs
    split = len(pieces) - 2
    step = pieces[0].shape[0]
    partial = _radial(r_perm[:, :split * step], pieces[:split], after=recvs[-2])
    return _radial(r_perm[:, split * step:], pieces[split:], partial=partial)


def _radial_kernel(n_pieces, has_partial, r_ref, *refs):
    pieces = refs[:n_pieces]
    rest = refs[n_pieces:]
    partial_ref = rest[0] if has_partial else None
    out_ref, xs = rest[-2], rest[-1]
    step = pieces[0].shape[0]
    for i, p in enumerate(pieces):
        xs[i * step:(i + 1) * step] = p[...]
    n_l, n_a, n_b = xs.shape
    y = jnp.dot(r_ref[...], xs[...].reshape(n_l, n_a * n_b), precision=lax.Precision.HIGHEST,
                preferred_element_type=jnp.float32).reshape(out_ref.shape)
    if has_partial:
        y = partial_ref[...] + y
    out_ref[...] = y


def _radial(r_cols, pieces, partial=None, after=None):
    n_k, n_l = r_cols.shape
    step, n_a, n_b = pieces[0].shape
    tile = 8
    extra = [] if partial is None else [partial]
    fake = [] if after is None else [after]
    in_specs = [pl.BlockSpec((n_k, n_l), lambda t: (0, 0))]
    in_specs += [pl.BlockSpec((step, tile, n_b), lambda t: (0, t, 0))] * len(pieces)
    in_specs += [pl.BlockSpec((n_k, tile, n_b), lambda t: (0, t, 0))] * len(extra)
    in_specs += [pl.BlockSpec(memory_space=pl.ANY)] * len(fake)
    return pl.pallas_call(
        functools.partial(_radial_kernel, len(pieces), partial is not None),
        out_shape=jax.ShapeDtypeStruct((n_k, n_a, n_b), jnp.float32),
        grid=(n_a // tile,),
        in_specs=in_specs,
        out_specs=pl.BlockSpec((n_k, tile, n_b), lambda t: (0, t, 0)),
        scratch_shapes=[pltpu.VMEM((n_l, tile, n_b), jnp.float32)],
    )(r_cols, *pieces, *extra, *fake)


def solution(mesh):
    in_specs = (
        P("rad", "cap", "lat"),
        P(None, "rad", "cap", "lat"),
        P("rad", "cap", "lat"),
        P("rad", "cap", "lat"),
        P("rad", "cap", "lat"),
        P(),
        P("rad", ("cap", "lat")),
        P(("cap", "lat")),
        P(("cap", "lat")),
    )
    out_specs = P(None, ("cap", "rad"), "lat")
    return jax.shard_map(
        per_device, mesh=mesh, in_specs=in_specs, out_specs=out_specs, check_vma=False
    )
```
